32 devices in a mesh: groups: 2 (over y), seq: 4 (over x, core), chan: 4 (over z).
Axes of the slice: x: 2, y: 2, z: 4, core: 2. Of those that a mesh axis runs over, the one named last changes fastest.
Arguments:
- hidden: bfloat16 [4096, 2048], P(('groups', 'seq')), parts along dimension 0, may hold values from -15 to 15
- bases: int32 [4096], P(('groups', 'seq')), parts along dimension 0, may hold values from 0 to 4
- w_gate: bfloat16 [2048, 4096], P(None, 'chan'), may hold values from -0.125 to 0.125
- w_values: bfloat16 [2048, 4096], P(None, 'chan'), may hold values from -0.125 to 0.125
- w_state_io: bfloat16 [2048, 2048], P(None, 'chan'), may hold values from -0.125 to 0.125
- w_step: bfloat16 [2048, 64], P(None, 'chan'), may hold values from -0.125 to 0.125
- conv_values: float32 [4, 4096], P(None, 'chan'), may hold values from -3 to 3
- conv_values_bias: float32 [4096], P('chan'), may hold values from -3 to 3
- conv_state_io: float32 [4, 2048], P(None, 'chan'), may hold values from -3 to 3
- conv_state_bias: float32 [2048], P('chan'), may hold values from -3 to 3
- step_bias: float32 [64], P('chan'), may hold values from -2 to 0
- decay_rate: float32 [64], P('chan'), may hold values from 0.0009765625 to 0.05, as said below
- skip_gain: float32 [64], P('chan'), may hold values from 0.5 to 1.5
- norm_gain: float32 [4096], P('chan'), may hold values from 0.1 to 1.9
- w_out: bfloat16 [4096, 2048], P('chan'), may hold values from -0.125 to 0.125
Outputs:
- mixed: bfloat16 [4096, 2048], P(('groups', 'seq'), 'chan'), parts along dimension 0
The draws below stay inside these ranges and needn't reach their ends.
There are 2 independent parts, one for each index of `groups`. The reference program is written for one: setup_inputs(seed, part) draws one part's arguments, and reference() takes and returns one part's arrays. A program takes and returns all parts, laid end to end along the dimension named above; an argument that names none is the same for every part. Nothing has to cross between parts.
Inputs may be any that keep to these rules, and one draw needn't show every extreme that they name: bases 0 to 3 are A, C, G, T; 4 is N. `decay_rate`: positive rates.
All inputs are finite; a program needn't handle non-finite values.
Results may differ from the reference program's by a relative error of at most 0.014.
Values may be sent and summed in bfloat16 or wider, within the bound.
No kernel may reach another device: no remote copies, remote signals or barrier semaphores. Data moves between devices by JAX's collectives and lax.ppermute only.
A program may use at most 128 MiB of HBM per device.

```python
import math
import jax
import jax.numpy as jnp
from jax import lax

D = 2048
E = 4096
P_SIZE = 64
H = 64
G = 8
N = 128
K = 4
Q = 256
TOK_DEV = 512
L = 2048


def draw_decay_rate(key, part):
    key_pick, key_slow, key_fast = jax.random.split(key, 3)
    heads = E // P_SIZE
    slow = jnp.exp(jax.random.uniform(key_slow, (heads,), jnp.float32, math.log(2.0 / L), math.log(8.0 / L)))
    fast = jnp.exp(jax.random.uniform(key_fast, (heads,), jnp.float32, math.log(0.03), math.log(0.05)))
    share = 0.5
    pick = jax.random.uniform(key_pick, (heads,), jnp.float32) < share
    return jnp.where(pick, fast, slow).astype(jnp.float32)


def draw_hidden(key, part):
    key_scale, key_entry = jax.random.split(jax.random.fold_in(key, 11), 2)
    segments = L // TOK_DEV
    seg_scale = jnp.exp(jax.random.uniform(key_scale, (segments,), jnp.float32, math.log(0.5), math.log(2.5)))
    row_scale = jnp.repeat(seg_scale, TOK_DEV)
    entries = jnp.clip(jax.random.normal(key_entry, (L, D), jnp.float32), -6.0, 6.0)
    return (entries * row_scale[:, None]).astype(jnp.bfloat16)


def touch_ends(values, rng, smallest, largest):
    shape = values.shape
    spot = [jax.random.randint(jax.random.fold_in(rng, axis), (), 0, shape[axis]) for axis in range(len(shape))]
    values = values.at[tuple(spot)].set(smallest)
    longest = shape.index(max(shape))
    spot[longest] = (spot[longest] + 1) % shape[longest]
    return values.at[tuple(spot)].set(largest)


def with_spikes(result, stream_key, source, target, shards_of, factor):
    def block_of(position):
        return (jnp.arange(result.shape[position]) // (result.shape[position] // shards_of)).reshape((-1,) + (1,) * (result.ndim - 1 - position))

    first = jax.random.permutation(stream_key, shards_of)[block_of(target)]
    far = (block_of(target) + shards_of // 2) % shards_of
    return jnp.where((block_of(source) == first) | (block_of(source) == far), factor * result, result)


def level_of(own_key, shape, pieces, smallest, top_value):
    level, own = 1.0, jax.random.fold_in(own_key, 6)
    for position, parts in pieces:
        steps = jnp.exp(jax.random.uniform(jax.random.fold_in(own, position), (parts,), jnp.float32, smallest / len(pieces), top_value / len(pieces)))
        level = level * jnp.repeat(steps, shape[position] // parts).reshape([-1 if axis == position else 1 for axis in range(len(shape))])
    return level


def normal_values(rng, shape, spread, reach, shards=(), dtype=jnp.bfloat16):
    result = jax.random.normal(rng, shape, jnp.float32) * spread
    if len(shards) > 0:
        result = level_of(rng, shape, shards, -0.22, 0.18) * result
    return jnp.clip(result, min=-reach, max=reach).astype(dtype)


def gaussian_with(stream_key, extent, spread, most, cuts, heavy, held_as=jnp.bfloat16):
    result = spread * jax.random.normal(stream_key, extent, jnp.float32)
    if cuts:
        result = result * level_of(stream_key, extent, cuts, -0.22, 0.18)
    return jnp.clip(with_spikes(result, jax.random.fold_in(stream_key, 3), *heavy), -most, most).astype(held_as)


def setup_inputs(seed: int = 0, part: int = 0) -> dict:
    key_list = jax.random.split(jax.random.key(seed), 16)
    part_splits = jax.random.split(jax.random.fold_in(key_list[15], part), 16)
    return {
        "hidden": draw_hidden(jax.random.fold_in(jax.random.fold_in(key_list[15], part), 71), part),
        "bases": touch_ends(jax.random.randint(part_splits[1], (L,), 0, 5), jax.random.fold_in(part_splits[1], 1), 0, 4).astype(jnp.int32),
        "w_gate": normal_values(key_list[2], (D, E), D ** -0.5, 0.125, ((1, 4),)),
        "w_values": normal_values(key_list[3], (D, E), D ** -0.5, 0.125, ((1, 4),)),
        "w_state_io": normal_values(key_list[4], (D, 2 * N * G), D ** -0.5, 0.125, ((1, 4),)),
        "w_step": normal_values(key_list[5], (D, H), D ** -0.5, 0.125, ((1, 4),)),
        "conv_values": normal_values(key_list[6], (K, E), K ** -0.5, 3.0, ((1, 4),), jnp.float32),
        "conv_values_bias": normal_values(key_list[7], (E,), 0.5, 3.0, ((0, 4),), jnp.float32),
        "conv_state_io": normal_values(key_list[8], (K, 2 * N * G), K ** -0.5, 3.0, ((1, 4),), jnp.float32),
        "conv_state_bias": normal_values(key_list[9], (2 * N * G,), 0.5, 3.0, ((0, 4),), jnp.float32),
        "step_bias": jnp.clip(-2.0 + 2.0 * jax.random.uniform(key_list[10], (H,), jnp.float32) ** level_of(key_list[10], (H,), ((0, 4),), -0.2, 0.2), -2.0, 0.0),
        "decay_rate": draw_decay_rate(jax.random.fold_in(key_list[15], 71), part),
        "skip_gain": jnp.clip(0.5 + 1.0 * jax.random.uniform(key_list[12], (H,), jnp.float32) ** level_of(key_list[12], (H,), ((0, 4),), -0.2, 0.2), 0.5, 1.5),
        "norm_gain": jnp.clip(1.0 + 0.18 * jax.random.normal(key_list[13], (E,), jnp.float32), 0.1, 1.9),
        "w_out": gaussian_with(key_list[14], (E, D), E ** -0.5, 0.125, ((0, 4),), (0, 1, 4, 2.0)),
    }


EPSILON = 1e-05
HIGHEST = lax.Precision.HIGHEST

def conv_silu(source, kernel, offset):
    taps = kernel.shape[0]
    padded = jnp.pad(source.astype(jnp.float32), ((taps - 1, 0), (0, 0)))
    total = jnp.zeros(source.shape, jnp.float32) + offset.astype(jnp.float32)[None, :]
    for index in range(taps):
        total = total + kernel[index].astype(jnp.float32)[None, :] * padded[index:index + source.shape[0]]
    return jax.nn.silu(total).astype(jnp.bfloat16)

def strand_mixer(rows_in, mask, w_gate, w_values, w_state_io, w_step, conv_values, conv_values_bias, conv_state_io, conv_state_bias, step_bias, decay_rate, skip_gain, norm_gain):
    length = rows_in.shape[0]
    per_group = H // G
    gate_in = jnp.dot(rows_in, w_gate, preferred_element_type=jnp.float32).astype(jnp.bfloat16)
    values = (jnp.dot(rows_in, w_values, preferred_element_type=jnp.float32) * mask[:, None]).astype(jnp.bfloat16)
    state_io = jnp.dot(rows_in, w_state_io, preferred_element_type=jnp.float32).astype(jnp.bfloat16)
    step_raw = jnp.dot(rows_in, w_step, preferred_element_type=jnp.float32).astype(jnp.bfloat16)
    values_c = conv_silu(values, conv_values, conv_values_bias)
    state_c = conv_silu(state_io, conv_state_io, conv_state_bias)
    delta = jax.nn.softplus(step_raw.astype(jnp.float32) + step_bias[None, :])
    logdec = -decay_rate[None, :] * delta
    blocks = length // Q
    value_blocks = values_c.astype(jnp.float32).reshape(blocks, Q, H, P_SIZE)
    state_blocks = state_c.astype(jnp.float32).reshape(blocks, Q, G, 2, N)
    in_blocks = state_blocks[:, :, :, 0, :]
    out_blocks = state_blocks[:, :, :, 1, :]
    log_blocks = logdec.reshape(blocks, Q, H)
    delta_blocks = delta.reshape(blocks, Q, H)
    causal = jnp.arange(Q)[:, None] >= jnp.arange(Q)[None, :]

    def block_step(state, block):
        values_q, in_vec, out_vec, logs, deltas = block
        cumul = jnp.cumsum(logs, axis=0)
        cumul_heads = cumul.T
        differ = cumul_heads[:, :, None] - cumul_heads[:, None, :]
        weights = jnp.where(causal[None], jnp.exp(jnp.where(causal[None], differ, 0.0)), 0.0) * deltas.T[:, None, :]
        inner = jnp.einsum('tgn,sgn->gts', out_vec, in_vec, precision=HIGHEST)
        inner = jnp.repeat(inner, per_group, axis=0)
        intra = jnp.einsum('hts,shp->thp', inner * weights, values_q, precision=HIGHEST)
        out_heads = jnp.repeat(out_vec, per_group, axis=1)
        in_heads = jnp.repeat(in_vec, per_group, axis=1)
        inter = jnp.einsum('thn,hpn->thp', out_heads, state, precision=HIGHEST) * jnp.exp(cumul)[:, :, None]
        tail = jnp.exp(cumul[-1][None, :] - cumul) * deltas
        added = jnp.einsum('sh,shp,shn->hpn', tail, values_q, in_heads, precision=HIGHEST)
        new_state = jnp.exp(cumul[-1])[:, None, None] * state + added
        return (new_state, intra + inter + skip_gain[None, :, None] * values_q)
    start = jnp.zeros((H, P_SIZE, N), jnp.float32)
    final, outputs = lax.scan(block_step, start, (value_blocks, in_blocks, out_blocks, log_blocks, delta_blocks))
    mixed_y = outputs.reshape(length, E)
    gated = mixed_y * jax.nn.silu(gate_in.astype(jnp.float32))
    grouped = gated.reshape(length, G, E // G)
    scale = lax.rsqrt(lax.optimization_barrier(jnp.mean(grouped * grouped, axis=-1, keepdims=True)) + EPSILON)
    return ((grouped * scale).reshape(length, E) * norm_gain[None, :]).astype(jnp.bfloat16)

def reference(hidden, bases, w_gate, w_values, w_state_io, w_step, conv_values, conv_values_bias, conv_state_io, conv_state_bias, step_bias, decay_rate, skip_gain, norm_gain, w_out):
    known = jnp.where(bases == 4, 0.0, 1.0).astype(jnp.float32)
    params = (w_gate, w_values, w_state_io, w_step, conv_values, conv_values_bias, conv_state_io, conv_state_bias, step_bias, decay_rate, skip_gain, norm_gain)
    forward = strand_mixer(hidden, known, *params)
    backward = strand_mixer(hidden[::-1, ::-1], known[::-1], *params)
    combined = (forward.astype(jnp.float32) + backward[::-1].astype(jnp.float32)).astype(jnp.bfloat16)
    return jnp.dot(combined, w_out, preferred_element_type=jnp.float32).astype(jnp.bfloat16)
```

```python
import jax
import jax.numpy as jnp
from jax import lax
from jax.sharding import PartitionSpec as P

P_SIZE = 64
N = 128
K = 4
Q = 128
LANE = 128


EPSILON = 1e-05
HIGHEST = lax.Precision.HIGHEST
F32 = jnp.float32
BF16 = jnp.bfloat16


def shifted(value, axis, steps):
    count = lax.axis_size(axis)
    pairs = [(source, source + steps) for source in range(count) if 0 <= source + steps < count]
    if not pairs:
        return jax.tree.map(jnp.zeros_like, value)
    return lax.ppermute(value, axis, pairs)


def exclusive_carry(total_log, state, sign):
    count = lax.axis_size("seq")
    got_log, got_state = shifted((total_log, state), "seq", sign)
    x_log, x_state = got_log, got_state
    i_log = got_log + total_log
    i_state = jnp.exp(total_log)[:, None, None] * got_state + state
    covered, window = 1, 2
    while covered < count - 1:
        r_log, r_state = shifted((i_log, i_state), "seq", sign * window)
        x_state = jnp.exp(x_log)[:, None, None] * r_state + x_state
        x_log = x_log + r_log
        covered += window
        if covered < count - 1:
            i_state = jnp.exp(i_log)[:, None, None] * r_state + i_state
            i_log = i_log + r_log
            window *= 2
    return x_state


def conv_silu(padded, kernel, offset, count, forward):
    taps = kernel.shape[0]
    total = jnp.zeros((count, padded.shape[1]), F32) + offset[None, :]
    for index in range(taps):
        start = index if forward else taps - 1 - index
        total = total + kernel[index][None, :] * padded[start : start + count].astype(F32)
    return jax.nn.silu(total).astype(BF16)


def on_device(
    hidden,
    bases,
    w_gate,
    w_values,
    w_state_io,
    w_step,
    conv_values,
    conv_values_bias,
    conv_state_io,
    conv_state_bias,
    step_bias,
    decay_rate,
    skip_gain,
    norm_gain,
    w_out,
):
    rows, width = hidden.shape
    heads = w_step.shape[1]
    groups = w_state_io.shape[1] // (2 * N)
    per_group = heads // groups
    blocks = rows // Q
    known = jnp.where(bases == 4, 0.0, 1.0).astype(F32)

    lane_idx = jnp.arange(LANE)
    anti = (lane_idx[:, None] + lane_idx[None, :] == LANE - 1).astype(BF16)
    lane_flipped = jnp.einsum(
        "rki,ij->rkj", hidden.reshape(rows, width // LANE, LANE), anti, preferred_element_type=F32
    ).astype(BF16)
    hidden_rev = jnp.flip(lane_flipped, 1).reshape(rows, width)

    def project(source):
        gate_in = jnp.dot(source, w_gate, preferred_element_type=F32).astype(BF16)
        values = (jnp.dot(source, w_values, preferred_element_type=F32) * known[:, None]).astype(BF16)
        state_io = jnp.dot(source, w_state_io, preferred_element_type=F32).astype(BF16)
        step_raw = jnp.dot(source, w_step, preferred_element_type=F32).astype(BF16)
        return gate_in, values, state_io, step_raw

    t_idx = jnp.arange(Q)

    def local_scan(pieces, forward):
        gate_in, values, state_io, step_raw = pieces
        sign = 1 if forward else -1
        if forward:
            rim = shifted((values[rows - (K - 1) :], state_io[rows - (K - 1) :]), "seq", 1)
            pv = jnp.concatenate([rim[0], values], axis=0)
            ps = jnp.concatenate([rim[1], state_io], axis=0)
        else:
            rim = shifted((values[: K - 1], state_io[: K - 1]), "seq", -1)
            pv = jnp.concatenate([values, rim[0]], axis=0)
            ps = jnp.concatenate([state_io, rim[1]], axis=0)
        values_c = conv_silu(pv, conv_values, conv_values_bias, rows, forward)
        state_c = conv_silu(ps, conv_state_io, conv_state_bias, rows, forward)
        delta = jax.nn.softplus(step_raw.astype(F32) + step_bias[None, :])
        logdec = -decay_rate[None, :] * delta

        x = values_c.astype(F32).reshape(blocks, Q, groups, per_group, P_SIZE)
        sb = state_c.reshape(blocks, Q, groups, 2, N)
        b_vec = sb[:, :, :, 0, :]
        c_vec = sb[:, :, :, 1, :]
        ld = logdec.reshape(blocks, Q, heads)
        dl = delta.reshape(blocks, Q, heads)
        acc = lax.cumsum(ld, axis=1, reverse=not forward)
        if forward:
            mask = t_idx[:, None] >= t_idx[None, :]
            tail = jnp.exp(acc[:, -1:, :] - acc) * dl
        else:
            mask = t_idx[:, None] <= t_idx[None, :]
            tail = jnp.exp(acc[:, :1, :] - acc) * dl
        blk = jnp.sum(ld, axis=1)
        acc_h = jnp.swapaxes(acc, 1, 2).reshape(blocks, groups, per_group, Q)
        dl_h = jnp.swapaxes(dl, 1, 2).reshape(blocks, groups, per_group, Q)
        differ = acc_h[..., :, None] - acc_h[..., None, :]
        weights = jnp.where(mask, jnp.exp(jnp.where(mask, differ, 0.0)), 0.0) * dl_h[..., None, :]
        inner = jnp.einsum("btgn,bsgn->bgts", c_vec, b_vec, preferred_element_type=F32)
        intra = jnp.einsum(
            "bgjts,bsgjp->btgjp", inner[:, :, None] * weights, x, precision=HIGHEST
        )
        tail_x = tail.reshape(blocks, Q, groups, per_group)[..., None] * x
        states = jnp.einsum(
            "bsgjp,bsgn->bgjpn", tail_x, b_vec.astype(F32), precision=HIGHEST
        ).reshape(blocks, heads, P_SIZE, N)

        incl = lax.cumsum(blk, axis=0, reverse=not forward)
        excl = incl - blk
        b_idx = jnp.arange(blocks)
        bmask = (b_idx[:, None] > b_idx[None, :]) if forward else (b_idx[:, None] < b_idx[None, :])
        bmask = bmask[:, :, None]
        bweights = jnp.where(bmask, jnp.exp(jnp.where(bmask, excl[:, None, :] - incl[None, :, :], 0.0)), 0.0)
        local_start = jnp.einsum("bkh,khpn->bhpn", bweights, states, precision=HIGHEST)
        total = jnp.sum(blk, axis=0)
        dev_state = jnp.einsum("kh,khpn->hpn", jnp.exp(total[None, :] - incl), states, precision=HIGHEST)
        carried = exclusive_carry(total, dev_state, sign)
        start = local_start + jnp.exp(excl)[:, :, None, None] * carried[None]
        inter = jnp.einsum(
            "btgn,bgjpn->btgjp",
            c_vec.astype(F32),
            start.reshape(blocks, groups, per_group, P_SIZE, N),
            precision=HIGHEST,
        ) * jnp.exp(acc).reshape(blocks, Q, groups, per_group)[..., None]
        outputs = intra + inter + skip_gain.reshape(groups, per_group)[None, None, :, :, None] * x
        gated = outputs.reshape(rows, heads * P_SIZE) * jax.nn.silu(gate_in.astype(F32))
        grouped = gated.reshape(rows, groups, per_group * P_SIZE)
        scale = lax.rsqrt(jnp.mean(grouped * grouped, axis=-1, keepdims=True) + EPSILON)
        return ((grouped * scale).reshape(rows, heads * P_SIZE) * norm_gain[None, :]).astype(BF16)

    forward_out = local_scan(project(hidden), True)
    backward_out = local_scan(project(hidden_rev), False)
    combined = (forward_out.astype(F32) + backward_out.astype(F32)).astype(BF16)
    partial = lax.dot_general(
        w_out, combined, (((0,), (1,)), ((), ())), preferred_element_type=F32
    ).astype(BF16)
    summed = lax.psum_scatter(partial, "chan", scatter_dimension=0, tiled=True)
    return summed.T


def solution(mesh):
    return jax.shard_map(
        on_device,
        mesh=mesh,
        in_specs=(
            P(("groups", "seq"), None),
            P(("groups", "seq")),
            P(None, "chan"),
            P(None, "chan"),
            P(None, "chan"),
            P(None, "chan"),
            P(None, "chan"),
            P("chan"),
            P(None, "chan"),
            P("chan"),
            P("chan"),
            P("chan"),
            P("chan"),
            P("chan"),
            P("chan", None),
        ),
        out_specs=P(("groups", "seq"), "chan"),
        check_vma=False,
    )
```

```python
import jax
import jax.numpy as jnp
from jax import lax
from jax.sharding import PartitionSpec as P

P_SIZE = 64
N = 128
K = 4
Q = 128
LANE = 128


EPSILON = 1e-05
HIGHEST = lax.Precision.HIGHEST
F32 = jnp.float32
BF16 = jnp.bfloat16


def shifted(value, axis, steps):
    count = lax.axis_size(axis)
    pairs = [(source, source + steps) for source in range(count) if 0 <= source + steps < count]
    if not pairs:
        return jax.tree.map(jnp.zeros_like, value)
    return lax.ppermute(value, axis, pairs)


def exclusive_carry(total_log, state, sign):
    count = lax.axis_size("seq")
    got_log, got_state = shifted((total_log, state), "seq", sign)
    x_log, x_state = got_log, got_state
    i_log = got_log + total_log
    i_state = jnp.exp(total_log)[:, None, None] * got_state + state
    covered, window = 1, 2
    while covered < count - 1:
        r_log, r_state = shifted((i_log, i_state), "seq", sign * window)
        x_state = jnp.exp(x_log)[:, None, None] * r_state + x_state
        x_log = x_log + r_log
        covered += window
        if covered < count - 1:
            i_state = jnp.exp(i_log)[:, None, None] * r_state + i_state
            i_log = i_log + r_log
            window *= 2
    return x_state


def conv_silu(padded, kernel, offset, count, forward):
    taps = kernel.shape[0]
    total = jnp.zeros((count, padded.shape[1]), F32) + offset[None, :]
    for index in range(taps):
        start = index if forward else taps - 1 - index
        total = total + kernel[index][None, :] * padded[start : start + count].astype(F32)
    return jax.nn.silu(total).astype(BF16)


def on_device(
    hidden,
    bases,
    w_gate,
    w_values,
    w_state_io,
    w_step,
    conv_values,
    conv_values_bias,
    conv_state_io,
    conv_state_bias,
    step_bias,
    decay_rate,
    skip_gain,
    norm_gain,
    w_out,
):
    rows, width = hidden.shape
    heads = w_step.shape[1]
    groups = w_state_io.shape[1] // (2 * N)
    per_group = heads // groups
    blocks = rows // Q
    known = jnp.where(bases == 4, 0.0, 1.0).astype(F32)

    lane_idx = jnp.arange(LANE)
    anti = (lane_idx[:, None] + lane_idx[None, :] == LANE - 1).astype(BF16)
    lane_flipped = jnp.einsum(
        "rki,ij->rkj", hidden.reshape(rows, width // LANE, LANE), anti, preferred_element_type=F32
    ).astype(BF16)
    hidden_rev = jnp.flip(lane_flipped, 1).reshape(rows, width)

    def project(source):
        gate_in = jnp.dot(source, w_gate, preferred_element_type=F32).astype(BF16)
        values = (jnp.dot(source, w_values, preferred_element_type=F32) * known[:, None]).astype(BF16)
        state_io = jnp.dot(source, w_state_io, preferred_element_type=F32).astype(BF16)
        step_raw = jnp.dot(source, w_step, preferred_element_type=F32).astype(BF16)
        return gate_in, values, state_io, step_raw

    t_idx = jnp.arange(Q)

    def local_scan(pieces, forward):
        gate_in, values, state_io, step_raw = pieces
        sign = 1 if forward else -1
        if forward:
            rim = shifted((values[rows - (K - 1) :], state_io[rows - (K - 1) :]), "seq", 1)
            pv = jnp.concatenate([rim[0], values], axis=0)
            ps = jnp.concatenate([rim[1], state_io], axis=0)
        else:
            rim = shifted((values[: K - 1], state_io[: K - 1]), "seq", -1)
            pv = jnp.concatenate([values, rim[0]], axis=0)
            ps = jnp.concatenate([state_io, rim[1]], axis=0)
        values_c = conv_silu(pv, conv_values, conv_values_bias, rows, forward)
        state_c = conv_silu(ps, conv_state_io, conv_state_bias, rows, forward)
        delta = jax.nn.softplus(step_raw.astype(F32) + step_bias[None, :])
        logdec = -decay_rate[None, :] * delta

        x = values_c.astype(F32).reshape(blocks, Q, groups, per_group, P_SIZE)
        sb = state_c.reshape(blocks, Q, groups, 2, N)
        b_vec = sb[:, :, :, 0, :]
        c_vec = sb[:, :, :, 1, :]
        ld = logdec.reshape(blocks, Q, heads)
        dl = delta.reshape(blocks, Q, heads)
        acc = lax.cumsum(ld, axis=1, reverse=not forward)
        if forward:
            mask = t_idx[:, None] >= t_idx[None, :]
            tail = jnp.exp(acc[:, -1:, :] - acc) * dl
        else:
            mask = t_idx[:, None] <= t_idx[None, :]
            tail = jnp.exp(acc[:, :1, :] - acc) * dl
        blk = jnp.sum(ld, axis=1)
        acc_h = jnp.swapaxes(acc, 1, 2).reshape(blocks, groups, per_group, Q)
        dl_h = jnp.swapaxes(dl, 1, 2).reshape(blocks, groups, per_group, Q)
        differ = acc_h[..., :, None] - acc_h[..., None, :]
        weights = jnp.where(mask, jnp.exp(jnp.where(mask, differ, 0.0)), 0.0) * dl_h[..., None, :]
        inner = jnp.einsum("btgn,bsgn->bgts", c_vec, b_vec, preferred_element_type=F32)
        intra = jnp.einsum(
            "bgjts,bsgjp->btgjp", inner[:, :, None] * weights, x, precision=HIGHEST
        )
        tail_x = tail.reshape(blocks, Q, groups, per_group)[..., None] * x
        states = jnp.einsum(
            "bsgjp,bsgn->bgjpn", tail_x, b_vec.astype(F32), precision=HIGHEST
        ).reshape(blocks, heads, P_SIZE, N)

        incl = lax.cumsum(blk, axis=0, reverse=not forward)
        excl = incl - blk
        b_idx = jnp.arange(blocks)
        bmask = (b_idx[:, None] > b_idx[None, :]) if forward else (b_idx[:, None] < b_idx[None, :])
        bmask = bmask[:, :, None]
        bweights = jnp.where(bmask, jnp.exp(jnp.where(bmask, excl[:, None, :] - incl[None, :, :], 0.0)), 0.0)
        local_start = jnp.einsum("bkh,khpn->bhpn", bweights, states, precision=HIGHEST)
        total = jnp.sum(blk, axis=0)
        dev_state = jnp.einsum("kh,khpn->hpn", jnp.exp(total[None, :] - incl), states, precision=HIGHEST)
        carried = exclusive_carry(total, dev_state, sign)
        start = local_start + jnp.exp(excl)[:, :, None, None] * carried[None]
        exp_acc = jnp.exp(acc).reshape(blocks, Q, groups, per_group)[..., None]
        skip = skip_gain.reshape(groups, per_group)[None, :, :, None]
        start = start.reshape(blocks, groups, per_group, P_SIZE, N)
        c_f32 = c_vec.astype(F32)
        gate_rows = gate_in.reshape(blocks, Q, heads * P_SIZE)

        def finish(index):
            inter = jnp.einsum(
                "tgn,gjpn->tgjp", c_f32[index], start[index], precision=HIGHEST
            ) * exp_acc[index]
            outputs = intra[index] + inter + skip * x[index]
            gated = outputs.reshape(Q, heads * P_SIZE) * jax.nn.silu(gate_rows[index].astype(F32))
            grouped = gated.reshape(Q, groups, per_group * P_SIZE)
            scale = lax.rsqrt(jnp.mean(grouped * grouped, axis=-1, keepdims=True) + EPSILON)
            return ((grouped * scale).reshape(Q, heads * P_SIZE) * norm_gain[None, :]).astype(BF16)

        return finish

    forward_finish = local_scan(project(hidden), True)
    backward_finish = local_scan(project(hidden_rev), False)
    pieces = []
    for index in range(blocks):
        combined = (
            forward_finish(index).astype(F32) + backward_finish(index).astype(F32)
        ).astype(BF16)
        partial = lax.dot_general(
            w_out, combined, (((0,), (1,)), ((), ())), preferred_element_type=F32
        ).astype(BF16)
        pieces.append(lax.psum_scatter(partial, "chan", scatter_dimension=0, tiled=True))
    return jnp.concatenate(pieces, axis=1).T

def solution(mesh):
    return jax.shard_map(
        on_device,
        mesh=mesh,
        in_specs=(
            P(("groups", "seq"), None),
            P(("groups", "seq")),
            P(None, "chan"),
            P(None, "chan"),
            P(None, "chan"),
            P(None, "chan"),
            P(None, "chan"),
            P("chan"),
            P(None, "chan"),
            P("chan"),
            P("chan"),
            P("chan"),
            P("chan"),
            P("chan"),
            P("chan", None),
        ),
        out_specs=P(("groups", "seq"), "chan"),
        check_vma=False,
    )
```

```python
import jax
import jax.numpy as jnp
from jax import lax
from jax.sharding import PartitionSpec as P

P_SIZE = 64
N = 128
K = 4
Q = 128
LANE = 128


EPSILON = 1e-05
HIGHEST = lax.Precision.HIGHEST
F32 = jnp.float32
BF16 = jnp.bfloat16


def shifted(value, axis, steps):
    count = lax.axis_size(axis)
    pairs = [(source, source + steps) for source in range(count) if 0 <= source + steps < count]
    if not pairs:
        return jax.tree.map(jnp.zeros_like, value)
    return lax.ppermute(value, axis, pairs)


def exclusive_carry(total_log, state, sign):
    count = lax.axis_size("seq")
    got_log, got_state = shifted((total_log, state), "seq", sign)
    x_log, x_state = got_log, got_state
    i_log = got_log + total_log
    i_state = jnp.exp(total_log)[:, None, None] * got_state + state
    covered, window = 1, 2
    while covered < count - 1:
        r_log, r_state = shifted((i_log, i_state), "seq", sign * window)
        x_state = jnp.exp(x_log)[:, None, None] * r_state + x_state
        x_log = x_log + r_log
        covered += window
        if covered < count - 1:
            i_state = jnp.exp(i_log)[:, None, None] * r_state + i_state
            i_log = i_log + r_log
            window *= 2
    return x_state


def conv_silu(padded, kernel, offset, count, forward):
    taps = kernel.shape[0]
    total = jnp.zeros((count, padded.shape[1]), F32) + offset[None, :]
    for index in range(taps):
        start = index if forward else taps - 1 - index
        total = total + kernel[index][None, :] * padded[start : start + count].astype(F32)
    return jax.nn.silu(total).astype(BF16)


def on_device(
    hidden,
    bases,
    w_gate,
    w_values,
    w_state_io,
    w_step,
    conv_values,
    conv_values_bias,
    conv_state_io,
    conv_state_bias,
    step_bias,
    decay_rate,
    skip_gain,
    norm_gain,
    w_out,
):
    rows, width = hidden.shape
    heads = w_step.shape[1]
    groups = w_state_io.shape[1] // (2 * N)
    per_group = heads // groups
    blocks = rows // Q
    known = jnp.where(bases == 4, 0.0, 1.0).astype(F32)

    lane_idx = jnp.arange(LANE)
    anti = (lane_idx[:, None] + lane_idx[None, :] == LANE - 1).astype(BF16)
    lane_flipped = jnp.einsum(
        "rki,ij->rkj", hidden.reshape(rows, width // LANE, LANE), anti, preferred_element_type=F32
    ).astype(BF16)
    hidden_rev = jnp.flip(lane_flipped, 1).reshape(rows, width)

    def project(source):
        gate_in = jnp.dot(source, w_gate, preferred_element_type=F32).astype(BF16)
        values = (jnp.dot(source, w_values, preferred_element_type=F32) * known[:, None]).astype(BF16)
        state_io = jnp.dot(source, w_state_io, preferred_element_type=F32).astype(BF16)
        step_raw = jnp.dot(source, w_step, preferred_element_type=F32).astype(BF16)
        return gate_in, values, state_io, step_raw

    t_idx = jnp.arange(Q)

    def local_scan(pieces, forward):
        gate_in, values, state_io, step_raw = pieces
        sign = 1 if forward else -1
        if forward:
            rim = shifted((values[rows - (K - 1) :], state_io[rows - (K - 1) :]), "seq", 1)
            pv = jnp.concatenate([rim[0], values], axis=0)
            ps = jnp.concatenate([rim[1], state_io], axis=0)
        else:
            rim = shifted((values[: K - 1], state_io[: K - 1]), "seq", -1)
            pv = jnp.concatenate([values, rim[0]], axis=0)
            ps = jnp.concatenate([state_io, rim[1]], axis=0)
        values_c = conv_silu(pv, conv_values, conv_values_bias, rows, forward)
        state_c = conv_silu(ps, conv_state_io, conv_state_bias, rows, forward)
        delta = jax.nn.softplus(step_raw.astype(F32) + step_bias[None, :])
        logdec = -decay_rate[None, :] * delta

        x = values_c.astype(F32).reshape(blocks, Q, groups, per_group, P_SIZE)
        sb = state_c.reshape(blocks, Q, groups, 2, N)
        b_vec = sb[:, :, :, 0, :]
        c_vec = sb[:, :, :, 1, :]
        ld = logdec.reshape(blocks, Q, heads)
        dl = delta.reshape(blocks, Q, heads)
        acc = lax.cumsum(ld, axis=1, reverse=not forward)
        if forward:
            mask = t_idx[:, None] >= t_idx[None, :]
            tail = jnp.exp(acc[:, -1:, :] - acc) * dl
        else:
            mask = t_idx[:, None] <= t_idx[None, :]
            tail = jnp.exp(acc[:, :1, :] - acc) * dl
        blk = jnp.sum(ld, axis=1)
        acc_h = jnp.swapaxes(acc, 1, 2).reshape(blocks, groups, per_group, Q)
        dl_h = jnp.swapaxes(dl, 1, 2).reshape(blocks, groups, per_group, Q)
        differ = acc_h[..., :, None] - acc_h[..., None, :]
        weights = jnp.where(mask, jnp.exp(jnp.where(mask, differ, 0.0)), 0.0) * dl_h[..., None, :]
        inner = jnp.einsum("btgn,bsgn->bgts", c_vec, b_vec, preferred_element_type=F32)
        intra = jnp.einsum(
            "bgjts,bsgjp->btgjp", inner[:, :, None] * weights, x, precision=HIGHEST
        )
        tail_x = tail.reshape(blocks, Q, groups, per_group)[..., None] * x
        states = jnp.einsum(
            "bsgjp,bsgn->bgjpn", tail_x, b_vec.astype(F32), precision=HIGHEST
        ).reshape(blocks, heads, P_SIZE, N)

        incl = lax.cumsum(blk, axis=0, reverse=not forward)
        excl = incl - blk
        b_idx = jnp.arange(blocks)
        bmask = (b_idx[:, None] > b_idx[None, :]) if forward else (b_idx[:, None] < b_idx[None, :])
        bmask = bmask[:, :, None]
        bweights = jnp.where(bmask, jnp.exp(jnp.where(bmask, excl[:, None, :] - incl[None, :, :], 0.0)), 0.0)
        local_start = jnp.einsum("bkh,khpn->bhpn", bweights, states, precision=HIGHEST)
        total = jnp.sum(blk, axis=0)
        dev_state = jnp.einsum("kh,khpn->hpn", jnp.exp(total[None, :] - incl), states, precision=HIGHEST)
        carried = exclusive_carry(total, dev_state, sign)
        start = local_start + jnp.exp(excl)[:, :, None, None] * carried[None]
        exp_acc = jnp.exp(acc).reshape(blocks, Q, groups, per_group)[..., None]
        skip = skip_gain.reshape(groups, per_group)[None, :, :, None]
        start = start.reshape(blocks, groups, per_group, P_SIZE, N)
        c_f32 = c_vec.astype(F32)

        inter = jnp.einsum("btgn,bgjpn->btgjp", c_f32, start, precision=HIGHEST) * exp_acc
        outputs = intra + inter + skip[None] * x
        gated = outputs.reshape(rows, heads * P_SIZE) * jax.nn.silu(gate_in.astype(F32))
        grouped = gated.reshape(rows, groups, per_group * P_SIZE)
        scale = lax.rsqrt(jnp.mean(grouped * grouped, axis=-1, keepdims=True) + EPSILON)
        return ((grouped * scale).reshape(rows, heads * P_SIZE) * norm_gain[None, :]).astype(BF16)

    forward_out = local_scan(project(hidden), True)
    backward_out = local_scan(project(hidden_rev), False)
    combined = (forward_out.astype(F32) + backward_out.astype(F32)).astype(BF16)
    chan = lax.axis_size("chan")
    partial = jnp.dot(combined, w_out, preferred_element_type=F32).astype(BF16)
    partial = jnp.transpose(partial.reshape(rows, chan, width // chan), (1, 0, 2))
    summed = lax.psum_scatter(partial, "chan", scatter_dimension=0, tiled=True)
    return summed.reshape(rows, width // chan)


def solution(mesh):
    return jax.shard_map(
        on_device,
        mesh=mesh,
        in_specs=(
            P(("groups", "seq"), None),
            P(("groups", "seq")),
            P(None, "chan"),
            P(None, "chan"),
            P(None, "chan"),
            P(None, "chan"),
            P(None, "chan"),
            P("chan"),
            P(None, "chan"),
            P("chan"),
            P("chan"),
            P("chan"),
            P("chan"),
            P("chan"),
            P("chan", None),
        ),
        out_specs=P(("groups", "seq"), "chan"),
        check_vma=False,
    )
```

```python
import jax
import jax.numpy as jnp
from jax import lax
from jax.sharding import PartitionSpec as P

P_SIZE = 64
N = 128
K = 4
Q = 128
LANE = 128


EPSILON = 1e-05
HIGHEST = lax.Precision.HIGHEST
F32 = jnp.float32
BF16 = jnp.bfloat16


def shifted(value, axis, steps):
    count = lax.axis_size(axis)
    pairs = [(source, source + steps) for source in range(count) if 0 <= source + steps < count]
    if not pairs:
        return jax.tree.map(jnp.zeros_like, value)
    return lax.ppermute(value, axis, pairs)


def exclusive_carry(total_log, state, sign):
    count = lax.axis_size("seq")
    heads = state.shape[0]
    flat = state.reshape(heads, -1)
    size = flat.shape[1]

    def send(log, st, distance):
        packed = jnp.concatenate([st, jnp.broadcast_to(log[:, None], (heads, LANE))], axis=1)
        got = shifted(packed, "seq", sign * distance)
        return got[:, size], got[:, :size]

    got_log, got_state = send(total_log, flat, 1)
    x_log, x_state = got_log, got_state
    i_log = got_log + total_log
    i_state = jnp.exp(total_log)[:, None] * got_state + flat
    covered, window = 1, 2
    while covered < count - 1:
        r_log, r_state = send(i_log, i_state, window)
        x_state = jnp.exp(x_log)[:, None] * r_state + x_state
        x_log = x_log + r_log
        covered += window
        if covered < count - 1:
            i_state = jnp.exp(i_log)[:, None] * r_state + i_state
            i_log = i_log + r_log
            window *= 2
    return x_state.reshape(state.shape)


def conv_silu(padded, kernel, offset, count, forward):
    taps = kernel.shape[0]
    total = jnp.zeros((count, padded.shape[1]), F32) + offset[None, :]
    for index in range(taps):
        start = index if forward else taps - 1 - index
        total = total + kernel[index][None, :] * padded[start : start + count].astype(F32)
    return jax.nn.silu(total).astype(BF16)


def on_device(
    hidden,
    bases,
    w_gate,
    w_values,
    w_state_io,
    w_step,
    conv_values,
    conv_values_bias,
    conv_state_io,
    conv_state_bias,
    step_bias,
    decay_rate,
    skip_gain,
    norm_gain,
    w_out,
):
    rows, width = hidden.shape
    heads = w_step.shape[1]
    groups = w_state_io.shape[1] // (2 * N)
    per_group = heads // groups
    blocks = rows // Q
    known = jnp.where(bases == 4, 0.0, 1.0).astype(F32)

    lane_idx = jnp.arange(LANE)
    anti = (lane_idx[:, None] + lane_idx[None, :] == LANE - 1).astype(BF16)

    def lane_reverse(block):
        count = block.shape[0]
        flipped = jnp.einsum(
            "rki,ij->rkj", block.reshape(count, width // LANE, LANE), anti, preferred_element_type=F32
        ).astype(BF16)
        return jnp.flip(flipped, 1).reshape(count, width)

    hidden_rev = lane_reverse(hidden)

    taps = K - 1
    seq_count = lax.axis_size("seq")
    here = lax.axis_index("seq")
    edges = lax.all_gather(jnp.concatenate([hidden[:taps], hidden[rows - taps :]], axis=0), "seq")
    edge_known = lax.all_gather(jnp.concatenate([known[:taps], known[rows - taps :]], axis=0), "seq")
    before = jnp.where(here > 0, 1.0, 0.0)
    after = jnp.where(here < seq_count - 1, 1.0, 0.0)
    prev_index = jnp.maximum(here - 1, 0)
    next_index = jnp.minimum(here + 1, seq_count - 1)
    rim_rows = jnp.concatenate(
        [edges[prev_index][taps:], lane_reverse(edges[next_index][:taps])], axis=0
    )
    rim_known = jnp.concatenate(
        [edge_known[prev_index][taps:] * before, edge_known[next_index][:taps] * after], axis=0
    )
    rim_present = jnp.concatenate(
        [jnp.full((taps,), 1.0, F32) * before, jnp.full((taps,), 1.0, F32) * after], axis=0
    )
    rim_values = (
        jnp.dot(rim_rows, w_values, preferred_element_type=F32) * rim_known[:, None]
    ).astype(BF16)
    rim_state = (
        jnp.dot(rim_rows, w_state_io, preferred_element_type=F32) * rim_present[:, None]
    ).astype(BF16)

    def project(source):
        gate_in = jnp.dot(source, w_gate, preferred_element_type=F32).astype(BF16)
        values = (jnp.dot(source, w_values, preferred_element_type=F32) * known[:, None]).astype(BF16)
        state_io = jnp.dot(source, w_state_io, preferred_element_type=F32).astype(BF16)
        step_raw = jnp.dot(source, w_step, preferred_element_type=F32).astype(BF16)
        return gate_in, values, state_io, step_raw

    t_idx = jnp.arange(Q)

    def local_scan(pieces, forward):
        gate_in, values, state_io, step_raw = pieces
        sign = 1 if forward else -1
        if forward:
            pv = jnp.concatenate([rim_values[:taps], values], axis=0)
            ps = jnp.concatenate([rim_state[:taps], state_io], axis=0)
        else:
            pv = jnp.concatenate([values, rim_values[taps:]], axis=0)
            ps = jnp.concatenate([state_io, rim_state[taps:]], axis=0)
        values_c = conv_silu(pv, conv_values, conv_values_bias, rows, forward)
        state_c = conv_silu(ps, conv_state_io, conv_state_bias, rows, forward)
        delta = jax.nn.softplus(step_raw.astype(F32) + step_bias[None, :])
        logdec = -decay_rate[None, :] * delta

        x = values_c.astype(F32).reshape(blocks, Q, groups, per_group, P_SIZE)
        sb = state_c.reshape(blocks, Q, groups, 2, N)
        b_vec = sb[:, :, :, 0, :]
        c_vec = sb[:, :, :, 1, :]
        ld = logdec.reshape(blocks, Q, heads)
        dl = delta.reshape(blocks, Q, heads)
        acc = lax.cumsum(ld, axis=1, reverse=not forward)
        if forward:
            mask = t_idx[:, None] >= t_idx[None, :]
            tail = jnp.exp(acc[:, -1:, :] - acc) * dl
        else:
            mask = t_idx[:, None] <= t_idx[None, :]
            tail = jnp.exp(acc[:, :1, :] - acc) * dl
        blk = jnp.sum(ld, axis=1)
        acc_h = jnp.swapaxes(acc, 1, 2).reshape(blocks, groups, per_group, Q)
        dl_h = jnp.swapaxes(dl, 1, 2).reshape(blocks, groups, per_group, Q)
        differ = acc_h[..., :, None] - acc_h[..., None, :]
        weights = jnp.where(mask, jnp.exp(jnp.where(mask, differ, 0.0)), 0.0) * dl_h[..., None, :]
        inner = jnp.einsum("btgn,bsgn->bgts", c_vec, b_vec, preferred_element_type=F32)
        intra = jnp.einsum(
            "bgjts,bsgjp->btgjp", inner[:, :, None] * weights, x, precision=HIGHEST
        )
        tail_x = tail.reshape(blocks, Q, groups, per_group)[..., None] * x
        states = jnp.einsum(
            "bsgjp,bsgn->bgjpn", tail_x, b_vec.astype(F32), precision=HIGHEST
        ).reshape(blocks, heads, P_SIZE, N)

        incl = lax.cumsum(blk, axis=0, reverse=not forward)
        excl = incl - blk
        b_idx = jnp.arange(blocks)
        bmask = (b_idx[:, None] > b_idx[None, :]) if forward else (b_idx[:, None] < b_idx[None, :])
        bmask = bmask[:, :, None]
        bweights = jnp.where(bmask, jnp.exp(jnp.where(bmask, excl[:, None, :] - incl[None, :, :], 0.0)), 0.0)
        local_start = jnp.einsum("bkh,khpn->bhpn", bweights, states, precision=HIGHEST)
        total = jnp.sum(blk, axis=0)
        dev_state = jnp.einsum("kh,khpn->hpn", jnp.exp(total[None, :] - incl), states, precision=HIGHEST)
        carried = exclusive_carry(total, dev_state, sign)
        start = local_start + jnp.exp(excl)[:, :, None, None] * carried[None]
        exp_acc = jnp.exp(acc).reshape(blocks, Q, groups, per_group)[..., None]
        skip = skip_gain.reshape(groups, per_group)[None, :, :, None]
        start = start.reshape(blocks, groups, per_group, P_SIZE, N)
        c_f32 = c_vec.astype(F32)

        inter = jnp.einsum("btgn,bgjpn->btgjp", c_f32, start, precision=HIGHEST) * exp_acc
        outputs = intra + inter + skip[None] * x
        gated = outputs.reshape(rows, heads * P_SIZE) * jax.nn.silu(gate_in.astype(F32))
        grouped = gated.reshape(rows, groups, per_group * P_SIZE)
        scale = lax.rsqrt(jnp.mean(grouped * grouped, axis=-1, keepdims=True) + EPSILON)
        return ((grouped * scale).reshape(rows, heads * P_SIZE) * norm_gain[None, :]).astype(BF16)

    forward_out = local_scan(project(hidden), True)
    backward_out = local_scan(project(hidden_rev), False)
    combined = (forward_out.astype(F32) + backward_out.astype(F32)).astype(BF16)
    chan = lax.axis_size("chan")
    partial = jnp.dot(combined, w_out, preferred_element_type=F32).astype(BF16)
    partial = jnp.transpose(partial.reshape(rows, chan, width // chan), (1, 0, 2))
    summed = lax.psum_scatter(partial, "chan", scatter_dimension=0, tiled=True)
    return summed.reshape(rows, width // chan)


def solution(mesh):
    return jax.shard_map(
        on_device,
        mesh=mesh,
        in_specs=(
            P(("groups", "seq"), None),
            P(("groups", "seq")),
            P(None, "chan"),
            P(None, "chan"),
            P(None, "chan"),
            P(None, "chan"),
            P(None, "chan"),
            P("chan"),
            P(None, "chan"),
            P("chan"),
            P("chan"),
            P("chan"),
            P("chan"),
            P("chan"),
            P("chan", None),
        ),
        out_specs=P(("groups", "seq"), "chan"),
        check_vma=False,
    )
```

```python
import jax
import jax.numpy as jnp
from jax import lax
from jax.sharding import PartitionSpec as P

P_SIZE = 64
N = 128
K = 4
Q = 128
LANE = 128


EPSILON = 1e-05
HIGHEST = lax.Precision.HIGHEST
F32 = jnp.float32
BF16 = jnp.bfloat16


def shifted(value, axis, steps):
    count = lax.axis_size(axis)
    pairs = [(source, source + steps) for source in range(count) if 0 <= source + steps < count]
    if not pairs:
        return jax.tree.map(jnp.zeros_like, value)
    return lax.ppermute(value, axis, pairs)


def exclusive_carry(total_log, state, sign):
    count = lax.axis_size("seq")
    heads = state.shape[0]
    flat = state.reshape(heads, -1)
    size = flat.shape[1]

    def send(log, st, distance):
        packed = jnp.concatenate([st, jnp.broadcast_to(log[:, None], (heads, LANE))], axis=1)
        got = shifted(packed, "seq", sign * distance)
        return got[:, size], got[:, :size]

    got_log, got_state = send(total_log, flat, 1)
    x_log, x_state = got_log, got_state
    i_log = got_log + total_log
    i_state = jnp.exp(total_log)[:, None] * got_state + flat
    covered, window = 1, 2
    while covered < count - 1:
        r_log, r_state = send(i_log, i_state, window)
        x_state = jnp.exp(x_log)[:, None] * r_state + x_state
        x_log = x_log + r_log
        covered += window
        if covered < count - 1:
            i_state = jnp.exp(i_log)[:, None] * r_state + i_state
            i_log = i_log + r_log
            window *= 2
    return x_state.reshape(state.shape)


def conv_silu(padded, kernel, offset, count, forward):
    taps = kernel.shape[0]
    total = jnp.zeros((count, padded.shape[1]), F32) + offset[None, :]
    for index in range(taps):
        start = index if forward else taps - 1 - index
        total = total + kernel[index][None, :] * padded[start : start + count].astype(F32)
    return jax.nn.silu(total).astype(BF16)


def on_device(
    hidden,
    bases,
    w_gate,
    w_values,
    w_state_io,
    w_step,
    conv_values,
    conv_values_bias,
    conv_state_io,
    conv_state_bias,
    step_bias,
    decay_rate,
    skip_gain,
    norm_gain,
    w_out,
):
    rows, width = hidden.shape
    heads = w_step.shape[1]
    groups = w_state_io.shape[1] // (2 * N)
    per_group = heads // groups
    blocks = rows // Q
    known = jnp.where(bases == 4, 0.0, 1.0).astype(F32)

    lane_idx = jnp.arange(LANE)
    anti = (lane_idx[:, None] + lane_idx[None, :] == LANE - 1).astype(BF16)

    def lane_reverse(block):
        count = block.shape[0]
        flipped = jnp.einsum(
            "rki,ij->rkj", block.reshape(count, width // LANE, LANE), anti, preferred_element_type=F32
        ).astype(BF16)
        return jnp.flip(flipped, 1).reshape(count, width)

    hidden_rev = lane_reverse(hidden)

    taps = K - 1
    known_cols = jnp.broadcast_to(known.astype(BF16)[:, None], (rows, LANE))
    edge_first = jnp.concatenate([hidden[:taps], known_cols[:taps]], axis=1)
    edge_last = jnp.concatenate([hidden[rows - taps :], known_cols[rows - taps :]], axis=1)
    from_prev = shifted(edge_last, "seq", 1)
    from_next = shifted(edge_first, "seq", -1)
    rim_rows = jnp.concatenate([from_prev[:, :width], lane_reverse(from_next[:, :width])], axis=0)
    rim_known = jnp.concatenate([from_prev[:, width], from_next[:, width]], axis=0).astype(F32)
    rim_values = (
        jnp.dot(rim_rows, w_values, preferred_element_type=F32) * rim_known[:, None]
    ).astype(BF16)
    rim_state = jnp.dot(rim_rows, w_state_io, preferred_element_type=F32).astype(BF16)

    def project(source):
        gate_in = jnp.dot(source, w_gate, preferred_element_type=F32).astype(BF16)
        values = (jnp.dot(source, w_values, preferred_element_type=F32) * known[:, None]).astype(BF16)
        state_io = jnp.dot(source, w_state_io, preferred_element_type=F32).astype(BF16)
        step_raw = jnp.dot(source, w_step, preferred_element_type=F32).astype(BF16)
        return gate_in, values, state_io, step_raw

    t_idx = jnp.arange(Q)

    def local_scan(pieces, forward):
        gate_in, values, state_io, step_raw = pieces
        sign = 1 if forward else -1
        if forward:
            pv = jnp.concatenate([rim_values[:taps], values], axis=0)
            ps = jnp.concatenate([rim_state[:taps], state_io], axis=0)
        else:
            pv = jnp.concatenate([values, rim_values[taps:]], axis=0)
            ps = jnp.concatenate([state_io, rim_state[taps:]], axis=0)
        values_c = conv_silu(pv, conv_values, conv_values_bias, rows, forward)
        state_c = conv_silu(ps, conv_state_io, conv_state_bias, rows, forward)
        delta = jax.nn.softplus(step_raw.astype(F32) + step_bias[None, :])
        logdec = -decay_rate[None, :] * delta

        x = values_c.astype(F32).reshape(blocks, Q, groups, per_group, P_SIZE)
        sb = state_c.reshape(blocks, Q, groups, 2, N)
        b_vec = sb[:, :, :, 0, :]
        c_vec = sb[:, :, :, 1, :]
        ld = logdec.reshape(blocks, Q, heads)
        dl = delta.reshape(blocks, Q, heads)
        acc = lax.cumsum(ld, axis=1, reverse=not forward)
        if forward:
            mask = t_idx[:, None] >= t_idx[None, :]
            tail = jnp.exp(acc[:, -1:, :] - acc) * dl
        else:
            mask = t_idx[:, None] <= t_idx[None, :]
            tail = jnp.exp(acc[:, :1, :] - acc) * dl
        blk = jnp.sum(ld, axis=1)
        acc_h = jnp.swapaxes(acc, 1, 2).reshape(blocks, groups, per_group, Q)
        dl_h = jnp.swapaxes(dl, 1, 2).reshape(blocks, groups, per_group, Q)
        differ = acc_h[..., :, None] - acc_h[..., None, :]
        weights = jnp.where(mask, jnp.exp(jnp.where(mask, differ, 0.0)), 0.0) * dl_h[..., None, :]
        inner = jnp.einsum("btgn,bsgn->bgts", c_vec, b_vec, preferred_element_type=F32)
        intra = jnp.einsum(
            "bgjts,bsgjp->btgjp", inner[:, :, None] * weights, x, precision=HIGHEST
        )
        tail_x = tail.reshape(blocks, Q, groups, per_group)[..., None] * x
        states = jnp.einsum(
            "bsgjp,bsgn->bgjpn", tail_x, b_vec.astype(F32), precision=HIGHEST
        ).reshape(blocks, heads, P_SIZE, N)

        incl = lax.cumsum(blk, axis=0, reverse=not forward)
        excl = incl - blk
        b_idx = jnp.arange(blocks)
        bmask = (b_idx[:, None] > b_idx[None, :]) if forward else (b_idx[:, None] < b_idx[None, :])
        bmask = bmask[:, :, None]
        bweights = jnp.where(bmask, jnp.exp(jnp.where(bmask, excl[:, None, :] - incl[None, :, :], 0.0)), 0.0)
        local_start = jnp.einsum("bkh,khpn->bhpn", bweights, states, precision=HIGHEST)
        total = jnp.sum(blk, axis=0)
        dev_state = jnp.einsum("kh,khpn->hpn", jnp.exp(total[None, :] - incl), states, precision=HIGHEST)
        carried = exclusive_carry(total, dev_state, sign)
        start = local_start + jnp.exp(excl)[:, :, None, None] * carried[None]
        exp_acc = jnp.exp(acc).reshape(blocks, Q, groups, per_group)[..., None]
        skip = skip_gain.reshape(groups, per_group)[None, :, :, None]
        start = start.reshape(blocks, groups, per_group, P_SIZE, N)
        c_f32 = c_vec.astype(F32)

        inter = jnp.einsum("btgn,bgjpn->btgjp", c_f32, start, precision=HIGHEST) * exp_acc
        outputs = intra + inter + skip[None] * x
        gated = outputs.reshape(rows, heads * P_SIZE) * jax.nn.silu(gate_in.astype(F32))
        grouped = gated.reshape(rows, groups, per_group * P_SIZE)
        scale = lax.rsqrt(jnp.mean(grouped * grouped, axis=-1, keepdims=True) + EPSILON)
        return ((grouped * scale).reshape(rows, heads * P_SIZE) * norm_gain[None, :]).astype(BF16)

    forward_out = local_scan(project(hidden), True)
    backward_out = local_scan(project(hidden_rev), False)
    combined = (forward_out.astype(F32) + backward_out.astype(F32)).astype(BF16)
    chan = lax.axis_size("chan")
    partial = jnp.dot(combined, w_out, preferred_element_type=F32).astype(BF16)
    partial = jnp.transpose(partial.reshape(rows, chan, width // chan), (1, 0, 2))
    summed = lax.psum_scatter(partial, "chan", scatter_dimension=0, tiled=True)
    return summed.reshape(rows, width // chan)


def solution(mesh):
    return jax.shard_map(
        on_device,
        mesh=mesh,
        in_specs=(
            P(("groups", "seq"), None),
            P(("groups", "seq")),
            P(None, "chan"),
            P(None, "chan"),
            P(None, "chan"),
            P(None, "chan"),
            P(None, "chan"),
            P("chan"),
            P(None, "chan"),
            P("chan"),
            P("chan"),
            P("chan"),
            P("chan"),
            P("chan"),
            P("chan", None),
        ),
        out_specs=P(("groups", "seq"), "chan"),
        check_vma=False,
    )
```

```python
import jax
import jax.numpy as jnp
from jax import lax
from jax.sharding import PartitionSpec as P

P_SIZE = 64
N = 128
K = 4
Q = 128
LANE = 128


EPSILON = 1e-05
HIGHEST = lax.Precision.HIGHEST
F32 = jnp.float32
BF16 = jnp.bfloat16


def shifted(value, axis, steps):
    count = lax.axis_size(axis)
    pairs = [(source, source + steps) for source in range(count) if 0 <= source + steps < count]
    if not pairs:
        return jax.tree.map(jnp.zeros_like, value)
    return lax.ppermute(value, axis, pairs)


def exclusive_carry(total_log, state, sign):
    count = lax.axis_size("seq")
    heads = state.shape[0]
    flat = state.reshape(heads, -1)
    size = flat.shape[1]

    def send(log, st, distance):
        packed = jnp.concatenate([st, jnp.broadcast_to(log[:, None], (heads, LANE))], axis=1)
        got = shifted(packed, "seq", sign * distance)
        return got[:, size], got[:, :size]

    got_log, got_state = send(total_log, flat, 1)
    x_log, x_state = got_log, got_state
    i_log = got_log + total_log
    i_state = jnp.exp(total_log)[:, None] * got_state + flat
    covered, window = 1, 2
    while covered < count - 1:
        r_log, r_state = send(i_log, i_state, window)
        x_state = jnp.exp(x_log)[:, None] * r_state + x_state
        x_log = x_log + r_log
        covered += window
        if covered < count - 1:
            i_state = jnp.exp(i_log)[:, None] * r_state + i_state
            i_log = i_log + r_log
            window *= 2
    return x_state.reshape(state.shape)


def conv_silu(padded, kernel, offset, count, forward):
    taps = kernel.shape[0]
    total = jnp.zeros((count, padded.shape[1]), F32) + offset[None, :]
    for index in range(taps):
        start = index if forward else taps - 1 - index
        total = total + kernel[index][None, :] * padded[start : start + count].astype(F32)
    return jax.nn.silu(total).astype(BF16)


def on_device(
    hidden,
    bases,
    w_gate,
    w_values,
    w_state_io,
    w_step,
    conv_values,
    conv_values_bias,
    conv_state_io,
    conv_state_bias,
    step_bias,
    decay_rate,
    skip_gain,
    norm_gain,
    w_out,
):
    rows, width = hidden.shape
    heads = w_step.shape[1]
    groups = w_state_io.shape[1] // (2 * N)
    per_group = heads // groups
    blocks = rows // Q
    known = jnp.where(bases == 4, 0.0, 1.0).astype(F32)

    lane_idx = jnp.arange(LANE)
    anti = (lane_idx[:, None] + lane_idx[None, :] == LANE - 1).astype(BF16)

    def lane_reverse(block):
        count = block.shape[0]
        flipped = jnp.einsum(
            "rki,ij->rkj", block.reshape(count, width // LANE, LANE), anti, preferred_element_type=F32
        ).astype(BF16)
        return jnp.flip(flipped, 1).reshape(count, width)

    hidden_rev = lane_reverse(hidden)

    taps = K - 1
    known_cols = jnp.broadcast_to(known.astype(BF16)[:, None], (rows, LANE))
    edge_first = jnp.concatenate([hidden[:taps], known_cols[:taps]], axis=1)
    edge_last = jnp.concatenate([hidden[rows - taps :], known_cols[rows - taps :]], axis=1)
    from_prev = shifted(edge_last, "seq", 1)
    from_next = shifted(edge_first, "seq", -1)
    rim_rows = jnp.concatenate([from_prev[:, :width], lane_reverse(from_next[:, :width])], axis=0)
    rim_known = jnp.concatenate([from_prev[:, width], from_next[:, width]], axis=0).astype(F32)
    rim_values = (
        jnp.dot(rim_rows, w_values, preferred_element_type=F32) * rim_known[:, None]
    ).astype(BF16)
    rim_state = jnp.dot(rim_rows, w_state_io, preferred_element_type=F32).astype(BF16)

    def project(source):
        gate_in = jnp.dot(source, w_gate, preferred_element_type=F32).astype(BF16)
        values = (jnp.dot(source, w_values, preferred_element_type=F32) * known[:, None]).astype(BF16)
        state_io = jnp.dot(source, w_state_io, preferred_element_type=F32).astype(BF16)
        step_raw = jnp.dot(source, w_step, preferred_element_type=F32).astype(BF16)
        return gate_in, values, state_io, step_raw

    t_idx = jnp.arange(Q)

    def local_scan(pieces, forward):
        gate_in, values, state_io, step_raw = pieces
        sign = 1 if forward else -1
        if forward:
            pv = jnp.concatenate([rim_values[:taps], values], axis=0)
            ps = jnp.concatenate([rim_state[:taps], state_io], axis=0)
        else:
            pv = jnp.concatenate([values, rim_values[taps:]], axis=0)
            ps = jnp.concatenate([state_io, rim_state[taps:]], axis=0)
        values_c = conv_silu(pv, conv_values, conv_values_bias, rows, forward)
        state_c = conv_silu(ps, conv_state_io, conv_state_bias, rows, forward)
        delta = jax.nn.softplus(step_raw.astype(F32) + step_bias[None, :])
        logdec = -decay_rate[None, :] * delta

        x = values_c.astype(F32).reshape(blocks, Q, groups, per_group, P_SIZE)
        sb = state_c.reshape(blocks, Q, groups, 2, N)
        b_vec = sb[:, :, :, 0, :]
        c_vec = sb[:, :, :, 1, :]
        ld = logdec.reshape(blocks, Q, heads)
        dl = delta.reshape(blocks, Q, heads)
        if forward:
            mask = t_idx[:, None] >= t_idx[None, :]
        else:
            mask = t_idx[:, None] <= t_idx[None, :]
        tri = mask.astype(F32)
        acc = jnp.einsum("ts,bsh->bth", tri, ld, precision=HIGHEST)
        acc_h = jnp.einsum("ts,bsh->bht", tri, ld, precision=HIGHEST)
        blk = jnp.sum(ld, axis=1)
        if forward:
            tail = jnp.exp(acc[:, -1:, :] - acc) * dl
        else:
            tail = jnp.exp(acc[:, :1, :] - acc) * dl
        acc_h = acc_h.reshape(blocks, groups, per_group, Q)
        dl_h = jnp.swapaxes(dl, 1, 2).reshape(blocks, groups, per_group, Q)
        differ = acc_h[..., :, None] - acc_h[..., None, :]
        weights = jnp.where(mask, jnp.exp(jnp.where(mask, differ, 0.0)), 0.0) * dl_h[..., None, :]
        inner = jnp.einsum("btgn,bsgn->bgts", c_vec, b_vec, preferred_element_type=F32)
        intra = jnp.einsum(
            "bgjts,bsgjp->btgjp", inner[:, :, None] * weights, x, precision=HIGHEST
        )
        tail_x = tail.reshape(blocks, Q, groups, per_group)[..., None] * x
        states = jnp.einsum(
            "bsgjp,bsgn->bgjpn", tail_x, b_vec.astype(F32), precision=HIGHEST
        ).reshape(blocks, heads, P_SIZE, N)

        order = list(range(blocks)) if forward else list(range(blocks - 1, -1, -1))
        block_decay = jnp.exp(blk)
        running = jnp.zeros((heads, P_SIZE, N), F32)
        local_start = [None] * blocks
        entering = [None] * blocks
        log_before = jnp.zeros((heads,), F32)
        for index in order:
            local_start[index] = running
            entering[index] = jnp.exp(log_before)
            running = block_decay[index][:, None, None] * running + states[index]
            log_before = log_before + blk[index]
        total = log_before
        carried = exclusive_carry(total, running, sign)
        start = jnp.stack(
            [local_start[index] + entering[index][:, None, None] * carried for index in range(blocks)]
        )
        exp_acc = jnp.exp(acc).reshape(blocks, Q, groups, per_group)[..., None]
        skip = skip_gain.reshape(groups, per_group)[None, :, :, None]
        start = start.reshape(blocks, groups, per_group * P_SIZE, N)
        c_f32 = c_vec.astype(F32)
        inter = jnp.concatenate(
            [
                jnp.einsum("btn,bkn->btk", c_f32[:, :, group], start[:, group], precision=HIGHEST)
                for group in range(groups)
            ],
            axis=2,
        ).reshape(blocks, Q, groups, per_group, P_SIZE) * exp_acc
        outputs = intra + inter + skip[None] * x
        gated = outputs.reshape(rows, heads * P_SIZE) * jax.nn.silu(gate_in.astype(F32))
        grouped = gated.reshape(rows, groups, per_group * P_SIZE)
        scale = lax.rsqrt(jnp.mean(grouped * grouped, axis=-1, keepdims=True) + EPSILON)
        return ((grouped * scale).reshape(rows, heads * P_SIZE) * norm_gain[None, :]).astype(BF16)

    forward_out = local_scan(project(hidden), True)
    backward_out = local_scan(project(hidden_rev), False)
    combined = (forward_out.astype(F32) + backward_out.astype(F32)).astype(BF16)
    chan = lax.axis_size("chan")
    partial = jnp.dot(combined, w_out, preferred_element_type=F32).astype(BF16)
    partial = jnp.transpose(partial.reshape(rows, chan, width // chan), (1, 0, 2))
    summed = lax.psum_scatter(partial, "chan", scatter_dimension=0, tiled=True)
    return summed.reshape(rows, width // chan)


def solution(mesh):
    return jax.shard_map(
        on_device,
        mesh=mesh,
        in_specs=(
            P(("groups", "seq"), None),
            P(("groups", "seq")),
            P(None, "chan"),
            P(None, "chan"),
            P(None, "chan"),
            P(None, "chan"),
            P(None, "chan"),
            P("chan"),
            P(None, "chan"),
            P("chan"),
            P("chan"),
            P("chan"),
            P("chan"),
            P("chan"),
            P("chan", None),
        ),
        out_specs=P(("groups", "seq"), "chan"),
        check_vma=False,
    )
```

```python
import jax
import jax.numpy as jnp
from jax import lax
from jax.sharding import PartitionSpec as P
from jax.experimental import pallas as pl

P_SIZE = 64
N = 128
K = 4
Q = 128
LANE = 128


EPSILON = 1e-05
HIGHEST = lax.Precision.HIGHEST
F32 = jnp.float32
BF16 = jnp.bfloat16


def shifted(value, axis, steps):
    count = lax.axis_size(axis)
    pairs = [(source, source + steps) for source in range(count) if 0 <= source + steps < count]
    if not pairs:
        return jax.tree.map(jnp.zeros_like, value)
    return lax.ppermute(value, axis, pairs)


def exclusive_carry(total_log, state, sign):
    count = lax.axis_size("seq")
    heads = state.shape[0]
    flat = state.reshape(heads, -1)
    size = flat.shape[1]

    def send(log, st, distance):
        packed = jnp.concatenate([st, jnp.broadcast_to(log[:, None], (heads, LANE))], axis=1)
        got = shifted(packed, "seq", sign * distance)
        return got[:, size], got[:, :size]

    got_log, got_state = send(total_log, flat, 1)
    x_log, x_state = got_log, got_state
    i_log = got_log + total_log
    i_state = jnp.exp(total_log)[:, None] * got_state + flat
    covered, window = 1, 2
    while covered < count - 1:
        r_log, r_state = send(i_log, i_state, window)
        x_state = jnp.exp(x_log)[:, None] * r_state + x_state
        x_log = x_log + r_log
        covered += window
        if covered < count - 1:
            i_state = jnp.exp(i_log)[:, None] * r_state + i_state
            i_log = i_log + r_log
            window *= 2
    return x_state.reshape(state.shape)


def block_scan(state_c, values_c, acc, delta, forward, interpret=False):
    rows = values_c.shape[0]
    heads = acc.shape[1]
    groups = state_c.shape[1] // (2 * N)
    per_group = heads // groups
    blocks = rows // Q
    width_g = per_group * P_SIZE
    acc_g = jnp.transpose(acc.reshape(rows, groups, per_group), (1, 0, 2))
    delta_g = jnp.transpose(delta.reshape(rows, groups, per_group), (1, 0, 2))
    acc_t = jnp.transpose(acc_g, (0, 2, 1))
    delta_t = jnp.transpose(delta_g, (0, 2, 1))

    def kernel(c_ref, b_ref, x_ref, a_ref, at_ref, d_ref, dt_ref, y_ref, s_ref):
        c_blk = c_ref[...]
        b_blk = b_ref[...]
        inner = lax.dot_general(c_blk, b_blk, (((1,), (1,)), ((), ())), preferred_element_type=F32)
        row = lax.broadcasted_iota(jnp.int32, (Q, Q), 0)
        col = lax.broadcasted_iota(jnp.int32, (Q, Q), 1)
        mask = row >= col if forward else row <= col
        for j in range(per_group):
            a_col = a_ref[0, :, j : j + 1]
            a_row = at_ref[0, j : j + 1, :]
            d_col = d_ref[0, :, j : j + 1]
            d_row = dt_ref[0, j : j + 1, :]
            differ = jnp.where(mask, a_col - a_row, 0.0)
            m = jnp.where(mask, jnp.exp(differ), 0.0) * d_row * inner
            x_j = x_ref[:, j * P_SIZE : (j + 1) * P_SIZE]
            m_hi = m.astype(BF16)
            m_lo = (m - m_hi.astype(F32)).astype(BF16)
            y_ref[:, j * P_SIZE : (j + 1) * P_SIZE] = jnp.dot(
                m_hi, x_j, preferred_element_type=F32
            ) + jnp.dot(m_lo, x_j, preferred_element_type=F32)
            a_end = a_col[Q - 1 : Q, :] if forward else a_col[0:1, :]
            tx = (jnp.exp(a_end - a_col) * d_col) * x_j.astype(F32)
            t_hi = tx.astype(BF16)
            t_lo = (tx - t_hi.astype(F32)).astype(BF16)
            dims = (((0,), (0,)), ((), ()))
            s_ref[0, j] = lax.dot_general(
                t_hi, b_blk, dims, preferred_element_type=F32
            ) + lax.dot_general(t_lo, b_blk, dims, preferred_element_type=F32)

    return pl.pallas_call(
        kernel,
        grid=(blocks, groups),
        in_specs=[
            pl.BlockSpec((Q, N), lambda b, g: (b, 2 * g + 1)),
            pl.BlockSpec((Q, N), lambda b, g: (b, 2 * g)),
            pl.BlockSpec((Q, width_g), lambda b, g: (b, g)),
            pl.BlockSpec((1, Q, per_group), lambda b, g: (g, b, 0)),
            pl.BlockSpec((1, per_group, Q), lambda b, g: (g, 0, b)),
            pl.BlockSpec((1, Q, per_group), lambda b, g: (g, b, 0)),
            pl.BlockSpec((1, per_group, Q), lambda b, g: (g, 0, b)),
        ],
        out_specs=[
            pl.BlockSpec((Q, width_g), lambda b, g: (b, g)),
            pl.BlockSpec((1, per_group, P_SIZE, N), lambda b, g: (b, g, 0, 0)),
        ],
        out_shape=[
            jax.ShapeDtypeStruct((rows, groups * width_g), F32),
            jax.ShapeDtypeStruct((blocks, heads, P_SIZE, N), F32),
        ],
        interpret=interpret,
    )(state_c, state_c, values_c, acc_g, acc_t, delta_g, delta_t)


def conv_silu(padded, kernel, offset, count, forward):
    taps = kernel.shape[0]
    total = jnp.zeros((count, padded.shape[1]), F32) + offset[None, :]
    for index in range(taps):
        start = index if forward else taps - 1 - index
        total = total + kernel[index][None, :] * padded[start : start + count].astype(F32)
    return jax.nn.silu(total).astype(BF16)


def on_device(
    hidden,
    bases,
    w_gate,
    w_values,
    w_state_io,
    w_step,
    conv_values,
    conv_values_bias,
    conv_state_io,
    conv_state_bias,
    step_bias,
    decay_rate,
    skip_gain,
    norm_gain,
    w_out,
):
    rows, width = hidden.shape
    heads = w_step.shape[1]
    groups = w_state_io.shape[1] // (2 * N)
    per_group = heads // groups
    blocks = rows // Q
    known = jnp.where(bases == 4, 0.0, 1.0).astype(F32)

    lane_idx = jnp.arange(LANE)
    anti = (lane_idx[:, None] + lane_idx[None, :] == LANE - 1).astype(BF16)

    def lane_reverse(block):
        count = block.shape[0]
        flipped = jnp.einsum(
            "rki,ij->rkj", block.reshape(count, width // LANE, LANE), anti, preferred_element_type=F32
        ).astype(BF16)
        return jnp.flip(flipped, 1).reshape(count, width)

    hidden_rev = lane_reverse(hidden)

    taps = K - 1
    known_cols = jnp.broadcast_to(known.astype(BF16)[:, None], (rows, LANE))
    edge_first = jnp.concatenate([hidden[:taps], known_cols[:taps]], axis=1)
    edge_last = jnp.concatenate([hidden[rows - taps :], known_cols[rows - taps :]], axis=1)
    from_prev = shifted(edge_last, "seq", 1)
    from_next = shifted(edge_first, "seq", -1)
    rim_rows = jnp.concatenate([from_prev[:, :width], lane_reverse(from_next[:, :width])], axis=0)
    rim_known = jnp.concatenate([from_prev[:, width], from_next[:, width]], axis=0).astype(F32)
    rim_values = (
        jnp.dot(rim_rows, w_values, preferred_element_type=F32) * rim_known[:, None]
    ).astype(BF16)
    rim_state = jnp.dot(rim_rows, w_state_io, preferred_element_type=F32).astype(BF16)

    def project(source):
        gate_in = jnp.dot(source, w_gate, preferred_element_type=F32).astype(BF16)
        values = (jnp.dot(source, w_values, preferred_element_type=F32) * known[:, None]).astype(BF16)
        state_io = jnp.dot(source, w_state_io, preferred_element_type=F32).astype(BF16)
        step_raw = jnp.dot(source, w_step, preferred_element_type=F32).astype(BF16)
        return gate_in, values, state_io, step_raw

    t_idx = jnp.arange(Q)

    def local_scan(pieces, forward):
        gate_in, values, state_io, step_raw = pieces
        sign = 1 if forward else -1
        if forward:
            pv = jnp.concatenate([rim_values[:taps], values], axis=0)
            ps = jnp.concatenate([rim_state[:taps], state_io], axis=0)
        else:
            pv = jnp.concatenate([values, rim_values[taps:]], axis=0)
            ps = jnp.concatenate([state_io, rim_state[taps:]], axis=0)
        values_c = conv_silu(pv, conv_values, conv_values_bias, rows, forward)
        state_c = conv_silu(ps, conv_state_io, conv_state_bias, rows, forward)
        delta = jax.nn.softplus(step_raw.astype(F32) + step_bias[None, :])
        logdec = -decay_rate[None, :] * delta

        sb = state_c.reshape(blocks, Q, groups, 2, N)
        c_vec = sb[:, :, :, 1, :]
        ld = logdec.reshape(blocks, Q, heads)
        if forward:
            mask = t_idx[:, None] >= t_idx[None, :]
        else:
            mask = t_idx[:, None] <= t_idx[None, :]
        acc = jnp.einsum("ts,bsh->bth", mask.astype(F32), ld, precision=HIGHEST)
        blk = jnp.sum(ld, axis=1)
        intra, states = block_scan(state_c, values_c, acc.reshape(rows, heads), delta, forward)

        order = list(range(blocks)) if forward else list(range(blocks - 1, -1, -1))
        block_decay = jnp.exp(blk)
        running = jnp.zeros((heads, P_SIZE, N), F32)
        local_start = [None] * blocks
        entering = [None] * blocks
        log_before = jnp.zeros((heads,), F32)
        for index in order:
            local_start[index] = running
            entering[index] = jnp.exp(log_before)
            running = block_decay[index][:, None, None] * running + states[index]
            log_before = log_before + blk[index]
        total = log_before
        carried = exclusive_carry(total, running, sign)
        start = jnp.stack(
            [local_start[index] + entering[index][:, None, None] * carried for index in range(blocks)]
        )
        start = start.reshape(blocks, groups, per_group * P_SIZE, N)
        c_f32 = c_vec.astype(F32)
        inter = jnp.concatenate(
            [
                jnp.einsum("btn,bkn->btk", c_f32[:, :, group], start[:, group], precision=HIGHEST)
                for group in range(groups)
            ],
            axis=2,
        ).reshape(rows, heads, P_SIZE) * jnp.exp(acc).reshape(rows, heads)[:, :, None]
        x = values_c.astype(F32).reshape(rows, heads, P_SIZE)
        outputs = intra.reshape(rows, heads, P_SIZE) + inter + skip_gain[None, :, None] * x
        gated = outputs.reshape(rows, heads * P_SIZE) * jax.nn.silu(gate_in.astype(F32))
        grouped = gated.reshape(rows, groups, per_group * P_SIZE)
        scale = lax.rsqrt(jnp.mean(grouped * grouped, axis=-1, keepdims=True) + EPSILON)
        return ((grouped * scale).reshape(rows, heads * P_SIZE) * norm_gain[None, :]).astype(BF16)

    forward_out = local_scan(project(hidden), True)
    backward_out = local_scan(project(hidden_rev), False)
    combined = (forward_out.astype(F32) + backward_out.astype(F32)).astype(BF16)
    chan = lax.axis_size("chan")
    partial = jnp.dot(combined, w_out, preferred_element_type=F32).astype(BF16)
    partial = jnp.transpose(partial.reshape(rows, chan, width // chan), (1, 0, 2))
    summed = lax.psum_scatter(partial, "chan", scatter_dimension=0, tiled=True)
    return summed.reshape(rows, width // chan)


def solution(mesh):
    return jax.shard_map(
        on_device,
        mesh=mesh,
        in_specs=(
            P(("groups", "seq"), None),
            P(("groups", "seq")),
            P(None, "chan"),
            P(None, "chan"),
            P(None, "chan"),
            P(None, "chan"),
            P(None, "chan"),
            P("chan"),
            P(None, "chan"),
            P("chan"),
            P("chan"),
            P("chan"),
            P("chan"),
            P("chan"),
            P("chan", None),
        ),
        out_specs=P(("groups", "seq"), "chan"),
        check_vma=False,
    )
```

```python
import jax
import jax.numpy as jnp
from jax import lax
from jax.sharding import PartitionSpec as P
from jax.experimental import pallas as pl

P_SIZE = 64
N = 128
K = 4
Q = 128
LANE = 128


EPSILON = 1e-05
HIGHEST = lax.Precision.HIGHEST
F32 = jnp.float32
BF16 = jnp.bfloat16


def shifted(value, axis, steps):
    count = lax.axis_size(axis)
    pairs = [(source, source + steps) for source in range(count) if 0 <= source + steps < count]
    if not pairs:
        return jax.tree.map(jnp.zeros_like, value)
    return lax.ppermute(value, axis, pairs)


def exclusive_carry(total_log, state, sign):
    count = lax.axis_size("seq")
    heads = state.shape[0]
    flat = state.reshape(heads, -1)
    size = flat.shape[1]

    def send(log, st, distance):
        packed = jnp.concatenate([st, jnp.broadcast_to(log[:, None], (heads, LANE))], axis=1)
        got = shifted(packed, "seq", sign * distance)
        return got[:, size], got[:, :size]

    got_log, got_state = send(total_log, flat, 1)
    x_log, x_state = got_log, got_state
    i_log = got_log + total_log
    i_state = jnp.exp(total_log)[:, None] * got_state + flat
    covered, window = 1, 2
    while covered < count - 1:
        r_log, r_state = send(i_log, i_state, window)
        x_state = jnp.exp(x_log)[:, None] * r_state + x_state
        x_log = x_log + r_log
        covered += window
        if covered < count - 1:
            i_state = jnp.exp(i_log)[:, None] * r_state + i_state
            i_log = i_log + r_log
            window *= 2
    return x_state.reshape(state.shape)


def group_layout(acc, delta, groups, per_group):
    rows = acc.shape[0]
    acc_g = jnp.transpose(acc.reshape(rows, groups, per_group), (1, 0, 2))
    delta_g = jnp.transpose(delta.reshape(rows, groups, per_group), (1, 0, 2))
    return acc_g, delta_g, jnp.transpose(acc_g, (0, 2, 1)), jnp.transpose(delta_g, (0, 2, 1))


def block_states(state_c, values_c, acc_g, delta_g, forward, interpret=False):
    rows = values_c.shape[0]
    groups, _, per_group = acc_g.shape
    blocks = rows // Q
    width_g = per_group * P_SIZE

    def kernel(b_ref, x_ref, a_ref, d_ref, s_ref):
        b_blk = b_ref[...]
        for j in range(per_group):
            a_col = a_ref[0, :, j : j + 1]
            d_col = d_ref[0, :, j : j + 1]
            x_j = x_ref[:, j * P_SIZE : (j + 1) * P_SIZE]
            a_end = a_col[Q - 1 : Q, :] if forward else a_col[0:1, :]
            tx = (jnp.exp(a_end - a_col) * d_col) * x_j.astype(F32)
            t_hi = tx.astype(BF16)
            t_lo = (tx - t_hi.astype(F32)).astype(BF16)
            dims = (((0,), (0,)), ((), ()))
            s_ref[0, j] = lax.dot_general(
                t_hi, b_blk, dims, preferred_element_type=F32
            ) + lax.dot_general(t_lo, b_blk, dims, preferred_element_type=F32)

    return pl.pallas_call(
        kernel,
        grid=(blocks, groups),
        in_specs=[
            pl.BlockSpec((Q, N), lambda b, g: (b, 2 * g)),
            pl.BlockSpec((Q, width_g), lambda b, g: (b, g)),
            pl.BlockSpec((1, Q, per_group), lambda b, g: (g, b, 0)),
            pl.BlockSpec((1, Q, per_group), lambda b, g: (g, b, 0)),
        ],
        out_specs=pl.BlockSpec((1, per_group, P_SIZE, N), lambda b, g: (b, g, 0, 0)),
        out_shape=jax.ShapeDtypeStruct((blocks, groups * per_group, P_SIZE, N), F32),
        interpret=interpret,
    )(state_c, values_c, acc_g, delta_g)


def block_intra(state_c, values_c, acc_g, acc_t, delta_t, forward, interpret=False):
    rows = values_c.shape[0]
    groups, _, per_group = acc_g.shape
    blocks = rows // Q
    width_g = per_group * P_SIZE

    def kernel(c_ref, b_ref, x_ref, a_ref, at_ref, dt_ref, y_ref):
        inner = lax.dot_general(
            c_ref[...], b_ref[...], (((1,), (1,)), ((), ())), preferred_element_type=F32
        )
        row = lax.broadcasted_iota(jnp.int32, (Q, Q), 0)
        col = lax.broadcasted_iota(jnp.int32, (Q, Q), 1)
        mask = row >= col if forward else row <= col
        for j in range(per_group):
            a_col = a_ref[0, :, j : j + 1]
            a_row = at_ref[0, j : j + 1, :]
            d_row = dt_ref[0, j : j + 1, :]
            differ = jnp.where(mask, a_col - a_row, 0.0)
            m = jnp.where(mask, jnp.exp(differ), 0.0) * d_row * inner
            x_j = x_ref[:, j * P_SIZE : (j + 1) * P_SIZE]
            m_hi = m.astype(BF16)
            m_lo = (m - m_hi.astype(F32)).astype(BF16)
            y_ref[:, j * P_SIZE : (j + 1) * P_SIZE] = jnp.dot(
                m_hi, x_j, preferred_element_type=F32
            ) + jnp.dot(m_lo, x_j, preferred_element_type=F32)

    return pl.pallas_call(
        kernel,
        grid=(blocks, groups),
        in_specs=[
            pl.BlockSpec((Q, N), lambda b, g: (b, 2 * g + 1)),
            pl.BlockSpec((Q, N), lambda b, g: (b, 2 * g)),
            pl.BlockSpec((Q, width_g), lambda b, g: (b, g)),
            pl.BlockSpec((1, Q, per_group), lambda b, g: (g, b, 0)),
            pl.BlockSpec((1, per_group, Q), lambda b, g: (g, 0, b)),
            pl.BlockSpec((1, per_group, Q), lambda b, g: (g, 0, b)),
        ],
        out_specs=pl.BlockSpec((Q, width_g), lambda b, g: (b, g)),
        out_shape=jax.ShapeDtypeStruct((rows, groups * width_g), F32),
        interpret=interpret,
    )(state_c, state_c, values_c, acc_g, acc_t, delta_t)


def conv_silu(padded, kernel, offset, count, forward):
    taps = kernel.shape[0]
    total = jnp.zeros((count, padded.shape[1]), F32) + offset[None, :]
    for index in range(taps):
        start = index if forward else taps - 1 - index
        total = total + kernel[index][None, :] * padded[start : start + count].astype(F32)
    return jax.nn.silu(total).astype(BF16)


def on_device(
    hidden,
    bases,
    w_gate,
    w_values,
    w_state_io,
    w_step,
    conv_values,
    conv_values_bias,
    conv_state_io,
    conv_state_bias,
    step_bias,
    decay_rate,
    skip_gain,
    norm_gain,
    w_out,
):
    rows, width = hidden.shape
    heads = w_step.shape[1]
    groups = w_state_io.shape[1] // (2 * N)
    per_group = heads // groups
    blocks = rows // Q
    known = jnp.where(bases == 4, 0.0, 1.0).astype(F32)

    lane_idx = jnp.arange(LANE)
    anti = (lane_idx[:, None] + lane_idx[None, :] == LANE - 1).astype(BF16)

    def lane_reverse(block):
        count = block.shape[0]
        flipped = jnp.einsum(
            "rki,ij->rkj", block.reshape(count, width // LANE, LANE), anti, preferred_element_type=F32
        ).astype(BF16)
        return jnp.flip(flipped, 1).reshape(count, width)

    hidden_rev = lane_reverse(hidden)

    taps = K - 1
    known_cols = jnp.broadcast_to(known.astype(BF16)[:, None], (rows, LANE))
    edge_first = jnp.concatenate([hidden[:taps], known_cols[:taps]], axis=1)
    edge_last = jnp.concatenate([hidden[rows - taps :], known_cols[rows - taps :]], axis=1)
    from_prev = shifted(edge_last, "seq", 1)
    from_next = shifted(edge_first, "seq", -1)
    rim_rows = jnp.concatenate([from_prev[:, :width], lane_reverse(from_next[:, :width])], axis=0)
    rim_known = jnp.concatenate([from_prev[:, width], from_next[:, width]], axis=0).astype(F32)
    rim_values = (
        jnp.dot(rim_rows, w_values, preferred_element_type=F32) * rim_known[:, None]
    ).astype(BF16)
    rim_state = jnp.dot(rim_rows, w_state_io, preferred_element_type=F32).astype(BF16)

    def project(source):
        gate_in = jnp.dot(source, w_gate, preferred_element_type=F32).astype(BF16)
        values = (jnp.dot(source, w_values, preferred_element_type=F32) * known[:, None]).astype(BF16)
        state_io = jnp.dot(source, w_state_io, preferred_element_type=F32).astype(BF16)
        step_raw = jnp.dot(source, w_step, preferred_element_type=F32).astype(BF16)
        return gate_in, values, state_io, step_raw

    t_idx = jnp.arange(Q)

    def local_scan(pieces, forward):
        gate_in, values, state_io, step_raw = pieces
        sign = 1 if forward else -1
        if forward:
            pv = jnp.concatenate([rim_values[:taps], values], axis=0)
            ps = jnp.concatenate([rim_state[:taps], state_io], axis=0)
        else:
            pv = jnp.concatenate([values, rim_values[taps:]], axis=0)
            ps = jnp.concatenate([state_io, rim_state[taps:]], axis=0)
        values_c = conv_silu(pv, conv_values, conv_values_bias, rows, forward)
        state_c = conv_silu(ps, conv_state_io, conv_state_bias, rows, forward)
        delta = jax.nn.softplus(step_raw.astype(F32) + step_bias[None, :])
        logdec = -decay_rate[None, :] * delta

        sb = state_c.reshape(blocks, Q, groups, 2, N)
        c_vec = sb[:, :, :, 1, :]
        ld = logdec.reshape(blocks, Q, heads)
        if forward:
            mask = t_idx[:, None] >= t_idx[None, :]
        else:
            mask = t_idx[:, None] <= t_idx[None, :]
        acc = jnp.einsum("ts,bsh->bth", mask.astype(F32), ld, precision=HIGHEST)
        blk = jnp.sum(ld, axis=1)
        acc_g, delta_g, acc_t, delta_t = group_layout(acc.reshape(rows, heads), delta, groups, per_group)
        states = block_states(state_c, values_c, acc_g, delta_g, forward)

        order = list(range(blocks)) if forward else list(range(blocks - 1, -1, -1))
        block_decay = jnp.exp(blk)
        running = jnp.zeros((heads, P_SIZE, N), F32)
        local_start = [None] * blocks
        entering = [None] * blocks
        log_before = jnp.zeros((heads,), F32)
        for index in order:
            local_start[index] = running
            entering[index] = jnp.exp(log_before)
            running = block_decay[index][:, None, None] * running + states[index]
            log_before = log_before + blk[index]
        total = log_before
        carried = exclusive_carry(total, running, sign)
        intra = block_intra(state_c, values_c, acc_g, acc_t, delta_t, forward)
        start = jnp.stack(
            [local_start[index] + entering[index][:, None, None] * carried for index in range(blocks)]
        )
        start = start.reshape(blocks, groups, per_group * P_SIZE, N)
        c_f32 = c_vec.astype(F32)
        inter = jnp.concatenate(
            [
                jnp.einsum("btn,bkn->btk", c_f32[:, :, group], start[:, group], precision=HIGHEST)
                for group in range(groups)
            ],
            axis=2,
        ).reshape(rows, heads, P_SIZE) * jnp.exp(acc).reshape(rows, heads)[:, :, None]
        x = values_c.astype(F32).reshape(rows, heads, P_SIZE)
        outputs = intra.reshape(rows, heads, P_SIZE) + inter + skip_gain[None, :, None] * x
        gated = outputs.reshape(rows, heads * P_SIZE) * jax.nn.silu(gate_in.astype(F32))
        grouped = gated.reshape(rows, groups, per_group * P_SIZE)
        scale = lax.rsqrt(jnp.mean(grouped * grouped, axis=-1, keepdims=True) + EPSILON)
        return ((grouped * scale).reshape(rows, heads * P_SIZE) * norm_gain[None, :]).astype(BF16)

    forward_out = local_scan(project(hidden), True)
    backward_out = local_scan(project(hidden_rev), False)
    combined = (forward_out.astype(F32) + backward_out.astype(F32)).astype(BF16)
    chan = lax.axis_size("chan")
    partial = jnp.dot(combined, w_out, preferred_element_type=F32).astype(BF16)
    partial = jnp.transpose(partial.reshape(rows, chan, width // chan), (1, 0, 2))
    summed = lax.psum_scatter(partial, "chan", scatter_dimension=0, tiled=True)
    return summed.reshape(rows, width // chan)


def solution(mesh):
    return jax.shard_map(
        on_device,
        mesh=mesh,
        in_specs=(
            P(("groups", "seq"), None),
            P(("groups", "seq")),
            P(None, "chan"),
            P(None, "chan"),
            P(None, "chan"),
            P(None, "chan"),
            P(None, "chan"),
            P("chan"),
            P(None, "chan"),
            P("chan"),
            P("chan"),
            P("chan"),
            P("chan"),
            P("chan"),
            P("chan", None),
        ),
        out_specs=P(("groups", "seq"), "chan"),
        check_vma=False,
    )
```

```python
import jax
import jax.numpy as jnp
from jax import lax
from jax.sharding import PartitionSpec as P
from jax.experimental import pallas as pl

P_SIZE = 64
N = 128
K = 4
Q = 128
LANE = 128


EPSILON = 1e-05
HIGHEST = lax.Precision.HIGHEST
F32 = jnp.float32
BF16 = jnp.bfloat16


def shifted(value, axis, steps):
    count = lax.axis_size(axis)
    pairs = [(source, source + steps) for source in range(count) if 0 <= source + steps < count]
    if not pairs:
        return jax.tree.map(jnp.zeros_like, value)
    return lax.ppermute(value, axis, pairs)


def exclusive_carry(total_log, state, sign):
    count = lax.axis_size("seq")
    heads = state.shape[0]
    flat = state.reshape(heads, -1)
    size = flat.shape[1]

    def send(log, st, distance):
        packed = jnp.concatenate([st, jnp.broadcast_to(log[:, None], (heads, LANE))], axis=1)
        got = shifted(packed, "seq", sign * distance)
        return got[:, size], got[:, :size]

    got_log, got_state = send(total_log, flat, 1)
    x_log, x_state = got_log, got_state
    i_log = got_log + total_log
    i_state = jnp.exp(total_log)[:, None] * got_state + flat
    covered, window = 1, 2
    while covered < count - 1:
        r_log, r_state = send(i_log, i_state, window)
        x_state = jnp.exp(x_log)[:, None] * r_state + x_state
        x_log = x_log + r_log
        covered += window
        if covered < count - 1:
            i_state = jnp.exp(i_log)[:, None] * r_state + i_state
            i_log = i_log + r_log
            window *= 2
    return x_state.reshape(state.shape)


def group_layout(acc, delta, groups, per_group):
    rows = acc.shape[0]
    acc_g = jnp.transpose(acc.reshape(rows, groups, per_group), (1, 0, 2))
    delta_g = jnp.transpose(delta.reshape(rows, groups, per_group), (1, 0, 2))
    return acc_g, delta_g, jnp.transpose(acc_g, (0, 2, 1)), jnp.transpose(delta_g, (0, 2, 1))


def block_states(state_c, values_t, acc_t, delta_t, forward, interpret=False):
    rows = values_t.shape[1]
    groups, per_group, _ = acc_t.shape
    blocks = rows // Q
    width_g = per_group * P_SIZE

    def kernel(b_ref, xt_ref, at_ref, dt_ref, s_ref):
        b_blk = b_ref[...]
        for j in range(per_group):
            a_row = at_ref[0, j : j + 1, :]
            d_row = dt_ref[0, j : j + 1, :]
            a_end = a_row[:, Q - 1 : Q] if forward else a_row[:, 0:1]
            xt_j = xt_ref[j * P_SIZE : (j + 1) * P_SIZE, :]
            tx = (jnp.exp(a_end - a_row) * d_row) * xt_j.astype(F32)
            t_hi = tx.astype(BF16)
            t_lo = (tx - t_hi.astype(F32)).astype(BF16)
            s_ref[0, j] = jnp.dot(t_hi, b_blk, preferred_element_type=F32) + jnp.dot(
                t_lo, b_blk, preferred_element_type=F32
            )

    return pl.pallas_call(
        kernel,
        grid=(blocks, groups),
        in_specs=[
            pl.BlockSpec((Q, N), lambda b, g: (b, 2 * g)),
            pl.BlockSpec((width_g, Q), lambda b, g: (g, b)),
            pl.BlockSpec((1, per_group, Q), lambda b, g: (g, 0, b)),
            pl.BlockSpec((1, per_group, Q), lambda b, g: (g, 0, b)),
        ],
        out_specs=pl.BlockSpec((1, per_group, P_SIZE, N), lambda b, g: (b, g, 0, 0)),
        out_shape=jax.ShapeDtypeStruct((blocks, groups * per_group, P_SIZE, N), F32),
        interpret=interpret,
    )(state_c, values_t, acc_t, delta_t)


def block_intra(state_c, values_c, acc_g, acc_t, delta_t, forward, interpret=False):
    rows = values_c.shape[0]
    groups, _, per_group = acc_g.shape
    blocks = rows // Q
    width_g = per_group * P_SIZE

    def kernel(c_ref, b_ref, x_ref, a_ref, at_ref, dt_ref, y_ref):
        inner = lax.dot_general(
            c_ref[...], b_ref[...], (((1,), (1,)), ((), ())), preferred_element_type=F32
        )
        row = lax.broadcasted_iota(jnp.int32, (Q, Q), 0)
        col = lax.broadcasted_iota(jnp.int32, (Q, Q), 1)
        mask = row >= col if forward else row <= col
        for j in range(per_group):
            a_col = a_ref[0, :, j : j + 1]
            a_row = at_ref[0, j : j + 1, :]
            d_row = dt_ref[0, j : j + 1, :]
            differ = jnp.where(mask, a_col - a_row, 0.0)
            m = jnp.where(mask, jnp.exp(differ), 0.0) * d_row * inner
            x_j = x_ref[:, j * P_SIZE : (j + 1) * P_SIZE]
            m_hi = m.astype(BF16)
            m_lo = (m - m_hi.astype(F32)).astype(BF16)
            y_ref[:, j * P_SIZE : (j + 1) * P_SIZE] = jnp.dot(
                m_hi, x_j, preferred_element_type=F32
            ) + jnp.dot(m_lo, x_j, preferred_element_type=F32)

    return pl.pallas_call(
        kernel,
        grid=(blocks, groups),
        in_specs=[
            pl.BlockSpec((Q, N), lambda b, g: (b, 2 * g + 1)),
            pl.BlockSpec((Q, N), lambda b, g: (b, 2 * g)),
            pl.BlockSpec((Q, width_g), lambda b, g: (b, g)),
            pl.BlockSpec((1, Q, per_group), lambda b, g: (g, b, 0)),
            pl.BlockSpec((1, per_group, Q), lambda b, g: (g, 0, b)),
            pl.BlockSpec((1, per_group, Q), lambda b, g: (g, 0, b)),
        ],
        out_specs=pl.BlockSpec((Q, width_g), lambda b, g: (b, g)),
        out_shape=jax.ShapeDtypeStruct((rows, groups * width_g), F32),
        interpret=interpret,
    )(state_c, state_c, values_c, acc_g, acc_t, delta_t)


def conv_silu(padded, kernel, offset, count, forward):
    taps = kernel.shape[0]
    total = jnp.zeros((count, padded.shape[1]), F32) + offset[None, :]
    for index in range(taps):
        start = index if forward else taps - 1 - index
        total = total + kernel[index][None, :] * padded[start : start + count].astype(F32)
    return jax.nn.silu(total).astype(BF16)


def on_device(
    hidden,
    bases,
    w_gate,
    w_values,
    w_state_io,
    w_step,
    conv_values,
    conv_values_bias,
    conv_state_io,
    conv_state_bias,
    step_bias,
    decay_rate,
    skip_gain,
    norm_gain,
    w_out,
):
    rows, width = hidden.shape
    heads = w_step.shape[1]
    groups = w_state_io.shape[1] // (2 * N)
    per_group = heads // groups
    blocks = rows // Q
    known = jnp.where(bases == 4, 0.0, 1.0).astype(F32)

    lane_idx = jnp.arange(LANE)
    anti = (lane_idx[:, None] + lane_idx[None, :] == LANE - 1).astype(BF16)

    def lane_reverse(block):
        count = block.shape[0]
        flipped = jnp.einsum(
            "rki,ij->rkj", block.reshape(count, width // LANE, LANE), anti, preferred_element_type=F32
        ).astype(BF16)
        return jnp.flip(flipped, 1).reshape(count, width)

    hidden_rev = lane_reverse(hidden)

    taps = K - 1
    known_cols = jnp.broadcast_to(known.astype(BF16)[:, None], (rows, LANE))
    edge_first = jnp.concatenate([hidden[:taps], known_cols[:taps]], axis=1)
    edge_last = jnp.concatenate([hidden[rows - taps :], known_cols[rows - taps :]], axis=1)
    from_prev = shifted(edge_last, "seq", 1)
    from_next = shifted(edge_first, "seq", -1)
    rim_rows = jnp.concatenate([from_prev[:, :width], lane_reverse(from_next[:, :width])], axis=0)
    rim_known = jnp.concatenate([from_prev[:, width], from_next[:, width]], axis=0).astype(F32)
    rim_values = (
        jnp.dot(rim_rows, w_values, preferred_element_type=F32) * rim_known[:, None]
    ).astype(BF16)
    rim_state = jnp.dot(rim_rows, w_state_io, preferred_element_type=F32).astype(BF16)

    def project(source):
        gate_in = jnp.dot(source, w_gate, preferred_element_type=F32).astype(BF16)
        values = (jnp.dot(source, w_values, preferred_element_type=F32) * known[:, None]).astype(BF16)
        state_io = jnp.dot(source, w_state_io, preferred_element_type=F32).astype(BF16)
        step_raw = jnp.dot(source, w_step, preferred_element_type=F32).astype(BF16)
        return gate_in, values, state_io, step_raw

    t_idx = jnp.arange(Q)

    def local_scan(pieces, forward):
        gate_in, values, state_io, step_raw = pieces
        sign = 1 if forward else -1
        if forward:
            pv = jnp.concatenate([rim_values[:taps], values], axis=0)
            ps = jnp.concatenate([rim_state[:taps], state_io], axis=0)
        else:
            pv = jnp.concatenate([values, rim_values[taps:]], axis=0)
            ps = jnp.concatenate([state_io, rim_state[taps:]], axis=0)
        values_c = conv_silu(pv, conv_values, conv_values_bias, rows, forward)
        state_c = conv_silu(ps, conv_state_io, conv_state_bias, rows, forward)
        delta = jax.nn.softplus(step_raw.astype(F32) + step_bias[None, :])
        logdec = -decay_rate[None, :] * delta

        sb = state_c.reshape(blocks, Q, groups, 2, N)
        c_vec = sb[:, :, :, 1, :]
        ld = logdec.reshape(blocks, Q, heads)
        if forward:
            mask = t_idx[:, None] >= t_idx[None, :]
        else:
            mask = t_idx[:, None] <= t_idx[None, :]
        acc = jnp.einsum("ts,bsh->bth", mask.astype(F32), ld, precision=HIGHEST)
        blk = jnp.sum(ld, axis=1)
        acc_g, delta_g, acc_t, delta_t = group_layout(acc.reshape(rows, heads), delta, groups, per_group)
        states = block_states(state_c, values_c.T, acc_t, delta_t, forward)

        order = list(range(blocks)) if forward else list(range(blocks - 1, -1, -1))
        block_decay = jnp.exp(blk)
        running = jnp.zeros((heads, P_SIZE, N), F32)
        local_start = [None] * blocks
        entering = [None] * blocks
        log_before = jnp.zeros((heads,), F32)
        for index in order:
            local_start[index] = running
            entering[index] = jnp.exp(log_before)
            running = block_decay[index][:, None, None] * running + states[index]
            log_before = log_before + blk[index]
        total = log_before
        carried = exclusive_carry(total, running, sign)
        intra = block_intra(state_c, values_c, acc_g, acc_t, delta_t, forward)
        start = jnp.stack(
            [local_start[index] + entering[index][:, None, None] * carried for index in range(blocks)]
        )
        start = start.reshape(blocks, groups, per_group * P_SIZE, N)
        c_f32 = c_vec.astype(F32)
        inter = jnp.concatenate(
            [
                jnp.einsum("btn,bkn->btk", c_f32[:, :, group], start[:, group], precision=HIGHEST)
                for group in range(groups)
            ],
            axis=2,
        ).reshape(rows, heads, P_SIZE) * jnp.exp(acc).reshape(rows, heads)[:, :, None]
        x = values_c.astype(F32).reshape(rows, heads, P_SIZE)
        outputs = intra.reshape(rows, heads, P_SIZE) + inter + skip_gain[None, :, None] * x
        gated = outputs.reshape(rows, heads * P_SIZE) * jax.nn.silu(gate_in.astype(F32))
        grouped = gated.reshape(rows, groups, per_group * P_SIZE)
        scale = lax.rsqrt(jnp.mean(grouped * grouped, axis=-1, keepdims=True) + EPSILON)
        return ((grouped * scale).reshape(rows, heads * P_SIZE) * norm_gain[None, :]).astype(BF16)

    forward_out = local_scan(project(hidden), True)
    backward_out = local_scan(project(hidden_rev), False)
    combined = (forward_out.astype(F32) + backward_out.astype(F32)).astype(BF16)
    chan = lax.axis_size("chan")
    partial = jnp.dot(combined, w_out, preferred_element_type=F32).astype(BF16)
    partial = jnp.transpose(partial.reshape(rows, chan, width // chan), (1, 0, 2))
    summed = lax.psum_scatter(partial, "chan", scatter_dimension=0, tiled=True)
    return summed.reshape(rows, width // chan)


def solution(mesh):
    return jax.shard_map(
        on_device,
        mesh=mesh,
        in_specs=(
            P(("groups", "seq"), None),
            P(("groups", "seq")),
            P(None, "chan"),
            P(None, "chan"),
            P(None, "chan"),
            P(None, "chan"),
            P(None, "chan"),
            P("chan"),
            P(None, "chan"),
            P("chan"),
            P("chan"),
            P("chan"),
            P("chan"),
            P("chan"),
            P("chan", None),
        ),
        out_specs=P(("groups", "seq"), "chan"),
        check_vma=False,
    )
```

```python
import jax
import jax.numpy as jnp
from jax import lax
from jax.sharding import PartitionSpec as P
from jax.experimental import pallas as pl

P_SIZE = 64
N = 128
K = 4
Q = 128
LANE = 128


EPSILON = 1e-05
HIGHEST = lax.Precision.HIGHEST
F32 = jnp.float32
BF16 = jnp.bfloat16


def shifted(value, axis, steps):
    count = lax.axis_size(axis)
    pairs = [(source, source + steps) for source in range(count) if 0 <= source + steps < count]
    if not pairs:
        return jax.tree.map(jnp.zeros_like, value)
    return lax.ppermute(value, axis, pairs)


def exclusive_carry(total_log, state, sign):
    count = lax.axis_size("seq")
    heads = state.shape[0]
    flat = state.reshape(heads, -1)
    size = flat.shape[1]

    def send(log, st, distance):
        packed = jnp.concatenate([st, jnp.broadcast_to(log[:, None], (heads, LANE))], axis=1)
        got = shifted(packed, "seq", sign * distance)
        return got[:, size], got[:, :size]

    got_log, got_state = send(total_log, flat, 1)
    x_log, x_state = got_log, got_state
    i_log = got_log + total_log
    i_state = jnp.exp(total_log)[:, None] * got_state + flat
    covered, window = 1, 2
    while covered < count - 1:
        r_log, r_state = send(i_log, i_state, window)
        x_state = jnp.exp(x_log)[:, None] * r_state + x_state
        x_log = x_log + r_log
        covered += window
        if covered < count - 1:
            i_state = jnp.exp(i_log)[:, None] * r_state + i_state
            i_log = i_log + r_log
            window *= 2
    return x_state.reshape(state.shape)


def group_layout(acc, delta, groups, per_group):
    rows = acc.shape[0]
    acc_g = jnp.transpose(acc.reshape(rows, groups, per_group), (1, 0, 2))
    delta_g = jnp.transpose(delta.reshape(rows, groups, per_group), (1, 0, 2))
    return acc_g, delta_g, jnp.transpose(acc_g, (0, 2, 1)), jnp.transpose(delta_g, (0, 2, 1))


def block_states(state_c, values_c, acc_g, delta_g, forward, interpret=False):
    rows = values_c.shape[0]
    groups, _, per_group = acc_g.shape
    blocks = rows // Q
    width_g = per_group * P_SIZE

    def kernel(b_ref, x_ref, a_ref, d_ref, s_ref):
        b_t = b_ref[...].astype(F32).T.astype(BF16)
        for j in range(per_group):
            a_col = a_ref[0, :, j : j + 1]
            d_col = d_ref[0, :, j : j + 1]
            a_end = a_col[Q - 1 : Q, :] if forward else a_col[0:1, :]
            x_j = x_ref[:, j * P_SIZE : (j + 1) * P_SIZE]
            tx = (jnp.exp(a_end - a_col) * d_col) * x_j.astype(F32)
            t_hi = tx.astype(BF16)
            t_lo = (tx - t_hi.astype(F32)).astype(BF16)
            s_ref[0, j] = jnp.dot(b_t, t_hi, preferred_element_type=F32) + jnp.dot(
                b_t, t_lo, preferred_element_type=F32
            )

    return pl.pallas_call(
        kernel,
        grid=(blocks, groups),
        in_specs=[
            pl.BlockSpec((Q, N), lambda b, g: (b, 2 * g)),
            pl.BlockSpec((Q, width_g), lambda b, g: (b, g)),
            pl.BlockSpec((1, Q, per_group), lambda b, g: (g, b, 0)),
            pl.BlockSpec((1, Q, per_group), lambda b, g: (g, b, 0)),
        ],
        out_specs=pl.BlockSpec((1, per_group, N, P_SIZE), lambda b, g: (b, g, 0, 0)),
        out_shape=jax.ShapeDtypeStruct((blocks, groups * per_group, N, P_SIZE), F32),
        interpret=interpret,
    )(state_c, values_c, acc_g, delta_g)


def block_intra(state_c, values_c, acc_g, acc_t, delta_t, forward, interpret=False):
    rows = values_c.shape[0]
    groups, _, per_group = acc_g.shape
    blocks = rows // Q
    width_g = per_group * P_SIZE

    def kernel(c_ref, b_ref, x_ref, a_ref, at_ref, dt_ref, y_ref):
        inner = lax.dot_general(
            c_ref[...], b_ref[...], (((1,), (1,)), ((), ())), preferred_element_type=F32
        )
        row = lax.broadcasted_iota(jnp.int32, (Q, Q), 0)
        col = lax.broadcasted_iota(jnp.int32, (Q, Q), 1)
        mask = row >= col if forward else row <= col
        for j in range(per_group):
            a_col = a_ref[0, :, j : j + 1]
            a_row = at_ref[0, j : j + 1, :]
            d_row = dt_ref[0, j : j + 1, :]
            differ = jnp.where(mask, a_col - a_row, 0.0)
            m = jnp.where(mask, jnp.exp(differ), 0.0) * d_row * inner
            x_j = x_ref[:, j * P_SIZE : (j + 1) * P_SIZE]
            m_hi = m.astype(BF16)
            m_lo = (m - m_hi.astype(F32)).astype(BF16)
            y_ref[:, j * P_SIZE : (j + 1) * P_SIZE] = jnp.dot(
                m_hi, x_j, preferred_element_type=F32
            ) + jnp.dot(m_lo, x_j, preferred_element_type=F32)

    return pl.pallas_call(
        kernel,
        grid=(blocks, groups),
        in_specs=[
            pl.BlockSpec((Q, N), lambda b, g: (b, 2 * g + 1)),
            pl.BlockSpec((Q, N), lambda b, g: (b, 2 * g)),
            pl.BlockSpec((Q, width_g), lambda b, g: (b, g)),
            pl.BlockSpec((1, Q, per_group), lambda b, g: (g, b, 0)),
            pl.BlockSpec((1, per_group, Q), lambda b, g: (g, 0, b)),
            pl.BlockSpec((1, per_group, Q), lambda b, g: (g, 0, b)),
        ],
        out_specs=pl.BlockSpec((Q, width_g), lambda b, g: (b, g)),
        out_shape=jax.ShapeDtypeStruct((rows, groups * width_g), F32),
        interpret=interpret,
    )(state_c, state_c, values_c, acc_g, acc_t, delta_t)


def conv_silu(padded, kernel, offset, count, forward):
    taps = kernel.shape[0]
    total = jnp.zeros((count, padded.shape[1]), F32) + offset[None, :]
    for index in range(taps):
        start = index if forward else taps - 1 - index
        total = total + kernel[index][None, :] * padded[start : start + count].astype(F32)
    return jax.nn.silu(total).astype(BF16)


def on_device(
    hidden,
    bases,
    w_gate,
    w_values,
    w_state_io,
    w_step,
    conv_values,
    conv_values_bias,
    conv_state_io,
    conv_state_bias,
    step_bias,
    decay_rate,
    skip_gain,
    norm_gain,
    w_out,
):
    rows, width = hidden.shape
    heads = w_step.shape[1]
    groups = w_state_io.shape[1] // (2 * N)
    per_group = heads // groups
    blocks = rows // Q
    known = jnp.where(bases == 4, 0.0, 1.0).astype(F32)

    lane_idx = jnp.arange(LANE)
    anti = (lane_idx[:, None] + lane_idx[None, :] == LANE - 1).astype(BF16)

    def lane_reverse(block):
        count = block.shape[0]
        flipped = jnp.einsum(
            "rki,ij->rkj", block.reshape(count, width // LANE, LANE), anti, preferred_element_type=F32
        ).astype(BF16)
        return jnp.flip(flipped, 1).reshape(count, width)

    hidden_rev = lane_reverse(hidden)

    taps = K - 1
    known_cols = jnp.broadcast_to(known.astype(BF16)[:, None], (rows, LANE))
    edge_first = jnp.concatenate([hidden[:taps], known_cols[:taps]], axis=1)
    edge_last = jnp.concatenate([hidden[rows - taps :], known_cols[rows - taps :]], axis=1)
    from_prev = shifted(edge_last, "seq", 1)
    from_next = shifted(edge_first, "seq", -1)
    rim_rows = jnp.concatenate([from_prev[:, :width], lane_reverse(from_next[:, :width])], axis=0)
    rim_known = jnp.concatenate([from_prev[:, width], from_next[:, width]], axis=0).astype(F32)
    rim_values = (
        jnp.dot(rim_rows, w_values, preferred_element_type=F32) * rim_known[:, None]
    ).astype(BF16)
    rim_state = jnp.dot(rim_rows, w_state_io, preferred_element_type=F32).astype(BF16)

    def project(source):
        gate_in = jnp.dot(source, w_gate, preferred_element_type=F32).astype(BF16)
        values = (jnp.dot(source, w_values, preferred_element_type=F32) * known[:, None]).astype(BF16)
        state_io = jnp.dot(source, w_state_io, preferred_element_type=F32).astype(BF16)
        step_raw = jnp.dot(source, w_step, preferred_element_type=F32).astype(BF16)
        return gate_in, values, state_io, step_raw

    t_idx = jnp.arange(Q)

    def local_scan(pieces, forward):
        gate_in, values, state_io, step_raw = pieces
        sign = 1 if forward else -1
        if forward:
            pv = jnp.concatenate([rim_values[:taps], values], axis=0)
            ps = jnp.concatenate([rim_state[:taps], state_io], axis=0)
        else:
            pv = jnp.concatenate([values, rim_values[taps:]], axis=0)
            ps = jnp.concatenate([state_io, rim_state[taps:]], axis=0)
        values_c = conv_silu(pv, conv_values, conv_values_bias, rows, forward)
        state_c = conv_silu(ps, conv_state_io, conv_state_bias, rows, forward)
        delta = jax.nn.softplus(step_raw.astype(F32) + step_bias[None, :])
        logdec = -decay_rate[None, :] * delta

        sb = state_c.reshape(blocks, Q, groups, 2, N)
        c_vec = sb[:, :, :, 1, :]
        ld = logdec.reshape(blocks, Q, heads)
        if forward:
            mask = t_idx[:, None] >= t_idx[None, :]
        else:
            mask = t_idx[:, None] <= t_idx[None, :]
        acc = jnp.einsum("ts,bsh->bth", mask.astype(F32), ld, precision=HIGHEST)
        blk = jnp.sum(ld, axis=1)
        acc_g, delta_g, acc_t, delta_t = group_layout(acc.reshape(rows, heads), delta, groups, per_group)
        states = block_states(state_c, values_c, acc_g, delta_g, forward)

        order = list(range(blocks)) if forward else list(range(blocks - 1, -1, -1))
        block_decay = jnp.exp(blk)
        running = jnp.zeros((heads, N, P_SIZE), F32)
        local_start = [None] * blocks
        entering = [None] * blocks
        log_before = jnp.zeros((heads,), F32)
        for index in order:
            local_start[index] = running
            entering[index] = jnp.exp(log_before)
            running = block_decay[index][:, None, None] * running + states[index]
            log_before = log_before + blk[index]
        total = log_before
        carried = exclusive_carry(total, running, sign)
        intra = block_intra(state_c, values_c, acc_g, acc_t, delta_t, forward)
        start = jnp.stack(
            [local_start[index] + entering[index][:, None, None] * carried for index in range(blocks)]
        )
        start = start.reshape(blocks, groups, per_group, N, P_SIZE)
        c_f32 = c_vec.astype(F32)
        inter = jnp.concatenate(
            [
                jnp.einsum("btn,bjnp->btjp", c_f32[:, :, group], start[:, group], precision=HIGHEST)
                for group in range(groups)
            ],
            axis=2,
        ).reshape(rows, heads, P_SIZE) * jnp.exp(acc).reshape(rows, heads)[:, :, None]
        x = values_c.astype(F32).reshape(rows, heads, P_SIZE)
        outputs = intra.reshape(rows, heads, P_SIZE) + inter + skip_gain[None, :, None] * x
        gated = outputs.reshape(rows, heads * P_SIZE) * jax.nn.silu(gate_in.astype(F32))
        grouped = gated.reshape(rows, groups, per_group * P_SIZE)
        scale = lax.rsqrt(jnp.mean(grouped * grouped, axis=-1, keepdims=True) + EPSILON)
        return ((grouped * scale).reshape(rows, heads * P_SIZE) * norm_gain[None, :]).astype(BF16)

    forward_out = local_scan(project(hidden), True)
    backward_out = local_scan(project(hidden_rev), False)
    combined = (forward_out.astype(F32) + backward_out.astype(F32)).astype(BF16)
    chan = lax.axis_size("chan")
    partial = jnp.dot(combined, w_out, preferred_element_type=F32).astype(BF16)
    partial = jnp.transpose(partial.reshape(rows, chan, width // chan), (1, 0, 2))
    summed = lax.psum_scatter(partial, "chan", scatter_dimension=0, tiled=True)
    return summed.reshape(rows, width // chan)


def solution(mesh):
    return jax.shard_map(
        on_device,
        mesh=mesh,
        in_specs=(
            P(("groups", "seq"), None),
            P(("groups", "seq")),
            P(None, "chan"),
            P(None, "chan"),
            P(None, "chan"),
            P(None, "chan"),
            P(None, "chan"),
            P("chan"),
            P(None, "chan"),
            P("chan"),
            P("chan"),
            P("chan"),
            P("chan"),
            P("chan"),
            P("chan", None),
        ),
        out_specs=P(("groups", "seq"), "chan"),
        check_vma=False,
    )
```

```python
import jax
import jax.numpy as jnp
from jax import lax
from jax.sharding import PartitionSpec as P
from jax.experimental import pallas as pl

P_SIZE = 64
N = 128
K = 4
Q = 128
LANE = 128


EPSILON = 1e-05
HIGHEST = lax.Precision.HIGHEST
F32 = jnp.float32
BF16 = jnp.bfloat16


def shifted(value, axis, steps):
    count = lax.axis_size(axis)
    pairs = [(source, source + steps) for source in range(count) if 0 <= source + steps < count]
    if not pairs:
        return jax.tree.map(jnp.zeros_like, value)
    return lax.ppermute(value, axis, pairs)


def exclusive_carry(total_log, state, sign):
    count = lax.axis_size("seq")
    heads = state.shape[0]
    flat = state.reshape(heads, -1)
    size = flat.shape[1]

    def send(log, st, distance):
        log_hi = log.astype(BF16)
        log_lo = (log - log_hi.astype(F32)).astype(BF16)
        packed = jnp.concatenate(
            [
                st.astype(BF16),
                jnp.broadcast_to(log_hi[:, None], (heads, LANE)),
                jnp.broadcast_to(log_lo[:, None], (heads, LANE)),
            ],
            axis=1,
        )
        got = shifted(packed, "seq", sign * distance)
        got_log = got[:, size].astype(F32) + got[:, size + LANE].astype(F32)
        return got_log, got[:, :size].astype(F32)

    got_log, got_state = send(total_log, flat, 1)
    x_log, x_state = got_log, got_state
    i_log = got_log + total_log
    i_state = jnp.exp(total_log)[:, None] * got_state + flat
    covered, window = 1, 2
    while covered < count - 1:
        r_log, r_state = send(i_log, i_state, window)
        x_state = jnp.exp(x_log)[:, None] * r_state + x_state
        x_log = x_log + r_log
        covered += window
        if covered < count - 1:
            i_state = jnp.exp(i_log)[:, None] * r_state + i_state
            i_log = i_log + r_log
            window *= 2
    return x_state.reshape(state.shape)


def group_layout(acc, delta, groups, per_group):
    rows = acc.shape[0]
    acc_g = jnp.transpose(acc.reshape(rows, groups, per_group), (1, 0, 2))
    delta_g = jnp.transpose(delta.reshape(rows, groups, per_group), (1, 0, 2))
    return acc_g, delta_g, jnp.transpose(acc_g, (0, 2, 1)), jnp.transpose(delta_g, (0, 2, 1))


def block_states(state_c, values_t, acc_t, delta_t, forward, interpret=False):
    rows = values_t.shape[1]
    groups, per_group, _ = acc_t.shape
    blocks = rows // Q
    width_g = per_group * P_SIZE

    def kernel(b_ref, xt_ref, at_ref, dt_ref, s_ref):
        b_blk = b_ref[...]
        for j in range(per_group):
            a_row = at_ref[0, j : j + 1, :]
            d_row = dt_ref[0, j : j + 1, :]
            a_end = a_row[:, Q - 1 : Q] if forward else a_row[:, 0:1]
            xt_j = xt_ref[j * P_SIZE : (j + 1) * P_SIZE, :]
            tx = (jnp.exp(a_end - a_row) * d_row) * xt_j.astype(F32)
            t_hi = tx.astype(BF16)
            t_lo = (tx - t_hi.astype(F32)).astype(BF16)
            s_ref[0, j] = jnp.dot(t_hi, b_blk, preferred_element_type=F32) + jnp.dot(
                t_lo, b_blk, preferred_element_type=F32
            )

    return pl.pallas_call(
        kernel,
        grid=(blocks, groups),
        in_specs=[
            pl.BlockSpec((Q, N), lambda b, g: (b, 2 * g)),
            pl.BlockSpec((width_g, Q), lambda b, g: (g, b)),
            pl.BlockSpec((1, per_group, Q), lambda b, g: (g, 0, b)),
            pl.BlockSpec((1, per_group, Q), lambda b, g: (g, 0, b)),
        ],
        out_specs=pl.BlockSpec((1, per_group, P_SIZE, N), lambda b, g: (b, g, 0, 0)),
        out_shape=jax.ShapeDtypeStruct((blocks, groups * per_group, P_SIZE, N), F32),
        interpret=interpret,
    )(state_c, values_t, acc_t, delta_t)


def block_intra(state_c, values_c, acc_g, acc_t, delta_t, forward, interpret=False):
    rows = values_c.shape[0]
    groups, _, per_group = acc_g.shape
    blocks = rows // Q
    width_g = per_group * P_SIZE

    def kernel(c_ref, b_ref, x_ref, a_ref, at_ref, dt_ref, y_ref):
        inner = lax.dot_general(
            c_ref[...], b_ref[...], (((1,), (1,)), ((), ())), preferred_element_type=F32
        )
        row = lax.broadcasted_iota(jnp.int32, (Q, Q), 0)
        col = lax.broadcasted_iota(jnp.int32, (Q, Q), 1)
        mask = row >= col if forward else row <= col
        for j in range(per_group):
            a_col = a_ref[0, :, j : j + 1]
            a_row = at_ref[0, j : j + 1, :]
            d_row = dt_ref[0, j : j + 1, :]
            differ = jnp.where(mask, a_col - a_row, 0.0)
            m = jnp.where(mask, jnp.exp(differ), 0.0) * d_row * inner
            x_j = x_ref[:, j * P_SIZE : (j + 1) * P_SIZE]
            m_hi = m.astype(BF16)
            m_lo = (m - m_hi.astype(F32)).astype(BF16)
            y_ref[:, j * P_SIZE : (j + 1) * P_SIZE] = jnp.dot(
                m_hi, x_j, preferred_element_type=F32
            ) + jnp.dot(m_lo, x_j, preferred_element_type=F32)

    return pl.pallas_call(
        kernel,
        grid=(blocks, groups),
        in_specs=[
            pl.BlockSpec((Q, N), lambda b, g: (b, 2 * g + 1)),
            pl.BlockSpec((Q, N), lambda b, g: (b, 2 * g)),
            pl.BlockSpec((Q, width_g), lambda b, g: (b, g)),
            pl.BlockSpec((1, Q, per_group), lambda b, g: (g, b, 0)),
            pl.BlockSpec((1, per_group, Q), lambda b, g: (g, 0, b)),
            pl.BlockSpec((1, per_group, Q), lambda b, g: (g, 0, b)),
        ],
        out_specs=pl.BlockSpec((Q, width_g), lambda b, g: (b, g)),
        out_shape=jax.ShapeDtypeStruct((rows, groups * width_g), F32),
        interpret=interpret,
    )(state_c, state_c, values_c, acc_g, acc_t, delta_t)


def conv_silu(padded, kernel, offset, count, forward):
    taps = kernel.shape[0]
    total = jnp.zeros((count, padded.shape[1]), F32) + offset[None, :]
    for index in range(taps):
        start = index if forward else taps - 1 - index
        total = total + kernel[index][None, :] * padded[start : start + count].astype(F32)
    return jax.nn.silu(total).astype(BF16)


def on_device(
    hidden,
    bases,
    w_gate,
    w_values,
    w_state_io,
    w_step,
    conv_values,
    conv_values_bias,
    conv_state_io,
    conv_state_bias,
    step_bias,
    decay_rate,
    skip_gain,
    norm_gain,
    w_out,
):
    rows, width = hidden.shape
    heads = w_step.shape[1]
    groups = w_state_io.shape[1] // (2 * N)
    per_group = heads // groups
    blocks = rows // Q
    known = jnp.where(bases == 4, 0.0, 1.0).astype(F32)

    lane_idx = jnp.arange(LANE)
    anti = (lane_idx[:, None] + lane_idx[None, :] == LANE - 1).astype(BF16)

    def lane_reverse(block):
        count = block.shape[0]
        flipped = jnp.einsum(
            "rki,ij->rkj", block.reshape(count, width // LANE, LANE), anti, preferred_element_type=F32
        ).astype(BF16)
        return jnp.flip(flipped, 1).reshape(count, width)

    hidden_rev = lane_reverse(hidden)

    taps = K - 1
    known_cols = jnp.broadcast_to(known.astype(BF16)[:, None], (rows, LANE))
    edge_first = jnp.concatenate([hidden[:taps], known_cols[:taps]], axis=1)
    edge_last = jnp.concatenate([hidden[rows - taps :], known_cols[rows - taps :]], axis=1)
    from_prev = shifted(edge_last, "seq", 1)
    from_next = shifted(edge_first, "seq", -1)
    rim_rows = jnp.concatenate([from_prev[:, :width], lane_reverse(from_next[:, :width])], axis=0)
    rim_known = jnp.concatenate([from_prev[:, width], from_next[:, width]], axis=0).astype(F32)
    rim_values = (
        jnp.dot(rim_rows, w_values, preferred_element_type=F32) * rim_known[:, None]
    ).astype(BF16)
    rim_state = jnp.dot(rim_rows, w_state_io, preferred_element_type=F32).astype(BF16)

    def project(source):
        gate_in = jnp.dot(source, w_gate, preferred_element_type=F32).astype(BF16)
        values = (jnp.dot(source, w_values, preferred_element_type=F32) * known[:, None]).astype(BF16)
        state_io = jnp.dot(source, w_state_io, preferred_element_type=F32).astype(BF16)
        step_raw = jnp.dot(source, w_step, preferred_element_type=F32).astype(BF16)
        return gate_in, values, state_io, step_raw

    t_idx = jnp.arange(Q)

    def local_scan(pieces, forward):
        gate_in, values, state_io, step_raw = pieces
        sign = 1 if forward else -1
        if forward:
            pv = jnp.concatenate([rim_values[:taps], values], axis=0)
            ps = jnp.concatenate([rim_state[:taps], state_io], axis=0)
        else:
            pv = jnp.concatenate([values, rim_values[taps:]], axis=0)
            ps = jnp.concatenate([state_io, rim_state[taps:]], axis=0)
        values_c = conv_silu(pv, conv_values, conv_values_bias, rows, forward)
        state_c = conv_silu(ps, conv_state_io, conv_state_bias, rows, forward)
        delta = jax.nn.softplus(step_raw.astype(F32) + step_bias[None, :])
        logdec = -decay_rate[None, :] * delta

        sb = state_c.reshape(blocks, Q, groups, 2, N)
        c_vec = sb[:, :, :, 1, :]
        ld = logdec.reshape(blocks, Q, heads)
        if forward:
            mask = t_idx[:, None] >= t_idx[None, :]
        else:
            mask = t_idx[:, None] <= t_idx[None, :]
        acc = jnp.einsum("ts,bsh->bth", mask.astype(F32), ld, precision=HIGHEST)
        blk = jnp.sum(ld, axis=1)
        acc_g, delta_g, acc_t, delta_t = group_layout(acc.reshape(rows, heads), delta, groups, per_group)
        states = block_states(state_c, values_c.T, acc_t, delta_t, forward)

        order = list(range(blocks)) if forward else list(range(blocks - 1, -1, -1))
        block_decay = jnp.exp(blk)
        running = jnp.zeros((heads, P_SIZE, N), F32)
        local_start = [None] * blocks
        entering = [None] * blocks
        log_before = jnp.zeros((heads,), F32)
        for index in order:
            local_start[index] = running
            entering[index] = jnp.exp(log_before)
            running = block_decay[index][:, None, None] * running + states[index]
            log_before = log_before + blk[index]
        total = log_before
        carried = exclusive_carry(total, running, sign)
        intra = block_intra(state_c, values_c, acc_g, acc_t, delta_t, forward)
        start = jnp.stack(
            [local_start[index] + entering[index][:, None, None] * carried for index in range(blocks)]
        )
        start = start.reshape(blocks, groups, per_group * P_SIZE, N)
        c_f32 = c_vec.astype(F32)
        inter = jnp.concatenate(
            [
                jnp.einsum("btn,bkn->btk", c_f32[:, :, group], start[:, group], precision=HIGHEST)
                for group in range(groups)
            ],
            axis=2,
        ).reshape(rows, heads, P_SIZE) * jnp.exp(acc).reshape(rows, heads)[:, :, None]
        x = values_c.astype(F32).reshape(rows, heads, P_SIZE)
        outputs = intra.reshape(rows, heads, P_SIZE) + inter + skip_gain[None, :, None] * x
        gated = outputs.reshape(rows, heads * P_SIZE) * jax.nn.silu(gate_in.astype(F32))
        grouped = gated.reshape(rows, groups, per_group * P_SIZE)
        scale = lax.rsqrt(jnp.mean(grouped * grouped, axis=-1, keepdims=True) + EPSILON)
        return ((grouped * scale).reshape(rows, heads * P_SIZE) * norm_gain[None, :]).astype(BF16)

    forward_out = local_scan(project(hidden), True)
    backward_out = local_scan(project(hidden_rev), False)
    combined = (forward_out.astype(F32) + backward_out.astype(F32)).astype(BF16)
    chan = lax.axis_size("chan")
    partial = jnp.dot(combined, w_out, preferred_element_type=F32).astype(BF16)
    partial = jnp.transpose(partial.reshape(rows, chan, width // chan), (1, 0, 2))
    summed = lax.psum_scatter(partial, "chan", scatter_dimension=0, tiled=True)
    return summed.reshape(rows, width // chan)


def solution(mesh):
    return jax.shard_map(
        on_device,
        mesh=mesh,
        in_specs=(
            P(("groups", "seq"), None),
            P(("groups", "seq")),
            P(None, "chan"),
            P(None, "chan"),
            P(None, "chan"),
            P(None, "chan"),
            P(None, "chan"),
            P("chan"),
            P(None, "chan"),
            P("chan"),
            P("chan"),
            P("chan"),
            P("chan"),
            P("chan"),
            P("chan", None),
        ),
        out_specs=P(("groups", "seq"), "chan"),
        check_vma=False,
    )
```

```python
import jax
import jax.numpy as jnp
from jax import lax
from jax.sharding import PartitionSpec as P
from jax.experimental import pallas as pl

P_SIZE = 64
N = 128
K = 4
Q = 128
LANE = 128


EPSILON = 1e-05
HIGHEST = lax.Precision.HIGHEST
F32 = jnp.float32
BF16 = jnp.bfloat16


def shifted(value, axis, steps):
    count = lax.axis_size(axis)
    pairs = [(source, source + steps) for source in range(count) if 0 <= source + steps < count]
    if not pairs:
        return jax.tree.map(jnp.zeros_like, value)
    return lax.ppermute(value, axis, pairs)


def exclusive_carry(total_log, state, sign):
    count = lax.axis_size("seq")
    heads = state.shape[0]
    flat = state.reshape(heads, -1)
    size = flat.shape[1]

    def send(log, st, distance):
        log_hi = log.astype(BF16)
        log_lo = (log - log_hi.astype(F32)).astype(BF16)
        packed = jnp.concatenate(
            [
                st.astype(BF16),
                jnp.broadcast_to(log_hi[:, None], (heads, LANE)),
                jnp.broadcast_to(log_lo[:, None], (heads, LANE)),
            ],
            axis=1,
        )
        got = shifted(packed, "seq", sign * distance)
        got_log = got[:, size].astype(F32) + got[:, size + LANE].astype(F32)
        return got_log, got[:, :size].astype(F32)

    got_log, got_state = send(total_log, flat, 1)
    x_log, x_state = got_log, got_state
    i_log = got_log + total_log
    i_state = jnp.exp(total_log)[:, None] * got_state + flat
    covered, window = 1, 2
    while covered < count - 1:
        r_log, r_state = send(i_log, i_state, window)
        x_state = jnp.exp(x_log)[:, None] * r_state + x_state
        x_log = x_log + r_log
        covered += window
        if covered < count - 1:
            i_state = jnp.exp(i_log)[:, None] * r_state + i_state
            i_log = i_log + r_log
            window *= 2
    return x_state.reshape(state.shape)


def group_layout(acc, delta, groups, per_group):
    rows = acc.shape[0]
    acc_g = jnp.transpose(acc.reshape(rows, groups, per_group), (1, 0, 2))
    delta_g = jnp.transpose(delta.reshape(rows, groups, per_group), (1, 0, 2))
    return acc_g, delta_g, jnp.transpose(acc_g, (0, 2, 1)), jnp.transpose(delta_g, (0, 2, 1))


def block_states(state_c, values_t, acc_t, delta_t, forward, interpret=False):
    rows = values_t.shape[1]
    groups, per_group, _ = acc_t.shape
    blocks = rows // Q
    width_g = per_group * P_SIZE

    def kernel(b_ref, xt_ref, at_ref, dt_ref, s_ref):
        b_blk = b_ref[...]
        for j in range(per_group):
            a_row = at_ref[0, j : j + 1, :]
            d_row = dt_ref[0, j : j + 1, :]
            a_end = a_row[:, Q - 1 : Q] if forward else a_row[:, 0:1]
            xt_j = xt_ref[j * P_SIZE : (j + 1) * P_SIZE, :]
            tx = (jnp.exp(a_end - a_row) * d_row) * xt_j.astype(F32)
            t_hi = tx.astype(BF16)
            t_lo = (tx - t_hi.astype(F32)).astype(BF16)
            s_ref[0, j] = jnp.dot(t_hi, b_blk, preferred_element_type=F32) + jnp.dot(
                t_lo, b_blk, preferred_element_type=F32
            )

    return pl.pallas_call(
        kernel,
        grid=(blocks, groups),
        in_specs=[
            pl.BlockSpec((Q, N), lambda b, g: (b, 2 * g)),
            pl.BlockSpec((width_g, Q), lambda b, g: (g, b)),
            pl.BlockSpec((1, per_group, Q), lambda b, g: (g, 0, b)),
            pl.BlockSpec((1, per_group, Q), lambda b, g: (g, 0, b)),
        ],
        out_specs=pl.BlockSpec((1, per_group, P_SIZE, N), lambda b, g: (b, g, 0, 0)),
        out_shape=jax.ShapeDtypeStruct((blocks, groups * per_group, P_SIZE, N), F32),
        interpret=interpret,
    )(state_c, values_t, acc_t, delta_t)


def block_intra(state_c, values_c, acc_g, acc_t, delta_t, forward, interpret=False):
    rows = values_c.shape[0]
    groups, _, per_group = acc_g.shape
    blocks = rows // Q
    width_g = per_group * P_SIZE

    def kernel(c_ref, b_ref, x_ref, a_ref, at_ref, dt_ref, y_ref):
        inner = lax.dot_general(
            c_ref[...], b_ref[...], (((1,), (1,)), ((), ())), preferred_element_type=F32
        )
        row = lax.broadcasted_iota(jnp.int32, (Q, Q), 0)
        col = lax.broadcasted_iota(jnp.int32, (Q, Q), 1)
        mask = row >= col if forward else row <= col
        for j in range(per_group):
            a_col = a_ref[0, :, j : j + 1]
            a_row = at_ref[0, j : j + 1, :]
            d_row = dt_ref[0, j : j + 1, :]
            differ = jnp.where(mask, a_col - a_row, 0.0)
            m = jnp.where(mask, jnp.exp(differ), 0.0) * d_row * inner
            x_j = x_ref[:, j * P_SIZE : (j + 1) * P_SIZE]
            y_ref[:, j * P_SIZE : (j + 1) * P_SIZE] = jnp.dot(
                m.astype(BF16), x_j, preferred_element_type=F32
            )

    return pl.pallas_call(
        kernel,
        grid=(blocks, groups),
        in_specs=[
            pl.BlockSpec((Q, N), lambda b, g: (b, 2 * g + 1)),
            pl.BlockSpec((Q, N), lambda b, g: (b, 2 * g)),
            pl.BlockSpec((Q, width_g), lambda b, g: (b, g)),
            pl.BlockSpec((1, Q, per_group), lambda b, g: (g, b, 0)),
            pl.BlockSpec((1, per_group, Q), lambda b, g: (g, 0, b)),
            pl.BlockSpec((1, per_group, Q), lambda b, g: (g, 0, b)),
        ],
        out_specs=pl.BlockSpec((Q, width_g), lambda b, g: (b, g)),
        out_shape=jax.ShapeDtypeStruct((rows, groups * width_g), F32),
        interpret=interpret,
    )(state_c, state_c, values_c, acc_g, acc_t, delta_t)


def conv_silu(padded, kernel, offset, count, forward):
    taps = kernel.shape[0]
    total = jnp.zeros((count, padded.shape[1]), F32) + offset[None, :]
    for index in range(taps):
        start = index if forward else taps - 1 - index
        total = total + kernel[index][None, :] * padded[start : start + count].astype(F32)
    return jax.nn.silu(total).astype(BF16)


def on_device(
    hidden,
    bases,
    w_gate,
    w_values,
    w_state_io,
    w_step,
    conv_values,
    conv_values_bias,
    conv_state_io,
    conv_state_bias,
    step_bias,
    decay_rate,
    skip_gain,
    norm_gain,
    w_out,
):
    rows, width = hidden.shape
    heads = w_step.shape[1]
    groups = w_state_io.shape[1] // (2 * N)
    per_group = heads // groups
    blocks = rows // Q
    known = jnp.where(bases == 4, 0.0, 1.0).astype(F32)

    lane_idx = jnp.arange(LANE)
    anti = (lane_idx[:, None] + lane_idx[None, :] == LANE - 1).astype(BF16)

    def lane_reverse(block):
        count = block.shape[0]
        flipped = jnp.einsum(
            "rki,ij->rkj", block.reshape(count, width // LANE, LANE), anti, preferred_element_type=F32
        ).astype(BF16)
        return jnp.flip(flipped, 1).reshape(count, width)

    hidden_rev = lane_reverse(hidden)

    taps = K - 1
    known_cols = jnp.broadcast_to(known.astype(BF16)[:, None], (rows, LANE))
    edge_first = jnp.concatenate([hidden[:taps], known_cols[:taps]], axis=1)
    edge_last = jnp.concatenate([hidden[rows - taps :], known_cols[rows - taps :]], axis=1)
    from_prev = shifted(edge_last, "seq", 1)
    from_next = shifted(edge_first, "seq", -1)
    rim_rows = jnp.concatenate([from_prev[:, :width], lane_reverse(from_next[:, :width])], axis=0)
    rim_known = jnp.concatenate([from_prev[:, width], from_next[:, width]], axis=0).astype(F32)
    rim_values = (
        jnp.dot(rim_rows, w_values, preferred_element_type=F32) * rim_known[:, None]
    ).astype(BF16)
    rim_state = jnp.dot(rim_rows, w_state_io, preferred_element_type=F32).astype(BF16)

    def project(source):
        gate_in = jnp.dot(source, w_gate, preferred_element_type=F32).astype(BF16)
        values = (jnp.dot(source, w_values, preferred_element_type=F32) * known[:, None]).astype(BF16)
        state_io = jnp.dot(source, w_state_io, preferred_element_type=F32).astype(BF16)
        step_raw = jnp.dot(source, w_step, preferred_element_type=F32).astype(BF16)
        return gate_in, values, state_io, step_raw

    t_idx = jnp.arange(Q)

    def local_scan(pieces, forward):
        gate_in, values, state_io, step_raw = pieces
        sign = 1 if forward else -1
        if forward:
            pv = jnp.concatenate([rim_values[:taps], values], axis=0)
            ps = jnp.concatenate([rim_state[:taps], state_io], axis=0)
        else:
            pv = jnp.concatenate([values, rim_values[taps:]], axis=0)
            ps = jnp.concatenate([state_io, rim_state[taps:]], axis=0)
        values_c = conv_silu(pv, conv_values, conv_values_bias, rows, forward)
        state_c = conv_silu(ps, conv_state_io, conv_state_bias, rows, forward)
        delta = jax.nn.softplus(step_raw.astype(F32) + step_bias[None, :])
        logdec = -decay_rate[None, :] * delta

        sb = state_c.reshape(blocks, Q, groups, 2, N)
        c_vec = sb[:, :, :, 1, :]
        ld = logdec.reshape(blocks, Q, heads)
        if forward:
            mask = t_idx[:, None] >= t_idx[None, :]
        else:
            mask = t_idx[:, None] <= t_idx[None, :]
        acc = jnp.einsum("ts,bsh->bth", mask.astype(F32), ld, precision=HIGHEST)
        blk = jnp.sum(ld, axis=1)
        acc_g, delta_g, acc_t, delta_t = group_layout(acc.reshape(rows, heads), delta, groups, per_group)
        states = block_states(state_c, values_c.T, acc_t, delta_t, forward)

        order = list(range(blocks)) if forward else list(range(blocks - 1, -1, -1))
        block_decay = jnp.exp(blk)
        running = jnp.zeros((heads, P_SIZE, N), F32)
        local_start = [None] * blocks
        entering = [None] * blocks
        log_before = jnp.zeros((heads,), F32)
        for index in order:
            local_start[index] = running
            entering[index] = jnp.exp(log_before)
            running = block_decay[index][:, None, None] * running + states[index]
            log_before = log_before + blk[index]
        total = log_before
        carried = exclusive_carry(total, running, sign)
        intra = block_intra(state_c, values_c, acc_g, acc_t, delta_t, forward)
        start = jnp.stack(
            [local_start[index] + entering[index][:, None, None] * carried for index in range(blocks)]
        )
        start = start.reshape(blocks, groups, per_group * P_SIZE, N)
        c_f32 = c_vec.astype(F32)
        inter = jnp.concatenate(
            [
                jnp.einsum("btn,bkn->btk", c_f32[:, :, group], start[:, group], precision=HIGHEST)
                for group in range(groups)
            ],
            axis=2,
        ).reshape(rows, heads, P_SIZE) * jnp.exp(acc).reshape(rows, heads)[:, :, None]
        x = values_c.astype(F32).reshape(rows, heads, P_SIZE)
        outputs = intra.reshape(rows, heads, P_SIZE) + inter + skip_gain[None, :, None] * x
        gated = outputs.reshape(rows, heads * P_SIZE) * jax.nn.silu(gate_in.astype(F32))
        grouped = gated.reshape(rows, groups, per_group * P_SIZE)
        scale = lax.rsqrt(jnp.mean(grouped * grouped, axis=-1, keepdims=True) + EPSILON)
        return ((grouped * scale).reshape(rows, heads * P_SIZE) * norm_gain[None, :]).astype(BF16)

    forward_out = local_scan(project(hidden), True)
    backward_out = local_scan(project(hidden_rev), False)
    combined = (forward_out.astype(F32) + backward_out.astype(F32)).astype(BF16)
    chan = lax.axis_size("chan")
    partial = jnp.dot(combined, w_out, preferred_element_type=F32).astype(BF16)
    partial = jnp.transpose(partial.reshape(rows, chan, width // chan), (1, 0, 2))
    summed = lax.psum_scatter(partial, "chan", scatter_dimension=0, tiled=True)
    return summed.reshape(rows, width // chan)


def solution(mesh):
    return jax.shard_map(
        on_device,
        mesh=mesh,
        in_specs=(
            P(("groups", "seq"), None),
            P(("groups", "seq")),
            P(None, "chan"),
            P(None, "chan"),
            P(None, "chan"),
            P(None, "chan"),
            P(None, "chan"),
            P("chan"),
            P(None, "chan"),
            P("chan"),
            P("chan"),
            P("chan"),
            P("chan"),
            P("chan"),
            P("chan", None),
        ),
        out_specs=P(("groups", "seq"), "chan"),
        check_vma=False,
    )
```

```python
import jax
import jax.numpy as jnp
from jax import lax
from jax.sharding import PartitionSpec as P
from jax.experimental import pallas as pl

P_SIZE = 64
N = 128
K = 4
Q = 128
LANE = 128


EPSILON = 1e-05
HIGHEST = lax.Precision.HIGHEST
F32 = jnp.float32
BF16 = jnp.bfloat16


def shifted(value, axis, steps):
    count = lax.axis_size(axis)
    pairs = [(source, source + steps) for source in range(count) if 0 <= source + steps < count]
    if not pairs:
        return jax.tree.map(jnp.zeros_like, value)
    return lax.ppermute(value, axis, pairs)


def exclusive_carry(total_log, state, sign):
    count = lax.axis_size("seq")
    heads = state.shape[0]
    flat = state.reshape(heads, -1)
    size = flat.shape[1]

    def send(log, st, distance):
        log_hi = log.astype(BF16)
        log_lo = (log - log_hi.astype(F32)).astype(BF16)
        packed = jnp.concatenate(
            [
                st.astype(BF16),
                jnp.broadcast_to(log_hi[:, None], (heads, LANE)),
                jnp.broadcast_to(log_lo[:, None], (heads, LANE)),
            ],
            axis=1,
        )
        got = shifted(packed, "seq", sign * distance)
        got_log = got[:, size].astype(F32) + got[:, size + LANE].astype(F32)
        return got_log, got[:, :size].astype(F32)

    got_log, got_state = send(total_log, flat, 1)
    x_log, x_state = got_log, got_state
    i_log = got_log + total_log
    i_state = jnp.exp(total_log)[:, None] * got_state + flat
    covered, window = 1, 2
    while covered < count - 1:
        r_log, r_state = send(i_log, i_state, window)
        x_state = jnp.exp(x_log)[:, None] * r_state + x_state
        x_log = x_log + r_log
        covered += window
        if covered < count - 1:
            i_state = jnp.exp(i_log)[:, None] * r_state + i_state
            i_log = i_log + r_log
            window *= 2
    return x_state.reshape(state.shape)


def group_layout(acc, delta, groups, per_group):
    rows = acc.shape[0]
    acc_g = jnp.transpose(acc.reshape(rows, groups, per_group), (1, 0, 2))
    delta_g = jnp.transpose(delta.reshape(rows, groups, per_group), (1, 0, 2))
    return acc_g, delta_g, jnp.transpose(acc_g, (0, 2, 1)), jnp.transpose(delta_g, (0, 2, 1))


def block_states(state_c, values_t, acc_t, delta_t, forward, interpret=False):
    rows = values_t.shape[1]
    groups, per_group, _ = acc_t.shape
    blocks = rows // Q
    width_g = per_group * P_SIZE

    def kernel(b_ref, xt_ref, at_ref, dt_ref, s_ref):
        b_blk = b_ref[...]
        for j in range(per_group):
            a_row = at_ref[0, j : j + 1, :]
            d_row = dt_ref[0, j : j + 1, :]
            a_end = a_row[:, Q - 1 : Q] if forward else a_row[:, 0:1]
            xt_j = xt_ref[j * P_SIZE : (j + 1) * P_SIZE, :]
            tx = (jnp.exp(a_end - a_row) * d_row) * xt_j.astype(F32)
            t_hi = tx.astype(BF16)
            t_lo = (tx - t_hi.astype(F32)).astype(BF16)
            s_ref[0, j] = jnp.dot(t_hi, b_blk, preferred_element_type=F32) + jnp.dot(
                t_lo, b_blk, preferred_element_type=F32
            )

    return pl.pallas_call(
        kernel,
        grid=(blocks, groups),
        in_specs=[
            pl.BlockSpec((Q, N), lambda b, g: (b, 2 * g)),
            pl.BlockSpec((width_g, Q), lambda b, g: (g, b)),
            pl.BlockSpec((1, per_group, Q), lambda b, g: (g, 0, b)),
            pl.BlockSpec((1, per_group, Q), lambda b, g: (g, 0, b)),
        ],
        out_specs=pl.BlockSpec((1, per_group, P_SIZE, N), lambda b, g: (b, g, 0, 0)),
        out_shape=jax.ShapeDtypeStruct((blocks, groups * per_group, P_SIZE, N), F32),
        interpret=interpret,
    )(state_c, values_t, acc_t, delta_t)


def block_intra(state_c, values_c, acc_g, acc_t, delta_t, forward, interpret=False):
    rows = values_c.shape[0]
    groups, _, per_group = acc_g.shape
    blocks = rows // Q
    width_g = per_group * P_SIZE

    def kernel(c_ref, b_ref, x_ref, a_ref, at_ref, dt_ref, y_ref):
        inner = lax.dot_general(
            c_ref[...], b_ref[...], (((1,), (1,)), ((), ())), preferred_element_type=F32
        )
        row = lax.broadcasted_iota(jnp.int32, (Q, Q), 0)
        col = lax.broadcasted_iota(jnp.int32, (Q, Q), 1)
        mask = row >= col if forward else row <= col
        for j in range(per_group):
            a_col = a_ref[0, :, j : j + 1]
            a_row = at_ref[0, j : j + 1, :]
            d_row = dt_ref[0, j : j + 1, :]
            differ = jnp.where(mask, a_col - a_row, 0.0)
            m = jnp.where(mask, jnp.exp(differ), 0.0) * d_row * inner
            x_j = x_ref[:, j * P_SIZE : (j + 1) * P_SIZE]
            y_ref[:, j * P_SIZE : (j + 1) * P_SIZE] = jnp.dot(
                m.astype(BF16), x_j, preferred_element_type=F32
            )

    return pl.pallas_call(
        kernel,
        grid=(blocks, groups),
        in_specs=[
            pl.BlockSpec((Q, N), lambda b, g: (b, 2 * g + 1)),
            pl.BlockSpec((Q, N), lambda b, g: (b, 2 * g)),
            pl.BlockSpec((Q, width_g), lambda b, g: (b, g)),
            pl.BlockSpec((1, Q, per_group), lambda b, g: (g, b, 0)),
            pl.BlockSpec((1, per_group, Q), lambda b, g: (g, 0, b)),
            pl.BlockSpec((1, per_group, Q), lambda b, g: (g, 0, b)),
        ],
        out_specs=pl.BlockSpec((Q, width_g), lambda b, g: (b, g)),
        out_shape=jax.ShapeDtypeStruct((rows, groups * width_g), F32),
        interpret=interpret,
    )(state_c, state_c, values_c, acc_g, acc_t, delta_t)


def conv_silu(padded, kernel, offset, count, forward):
    taps = kernel.shape[0]
    total = jnp.zeros((count, padded.shape[1]), F32) + offset[None, :]
    for index in range(taps):
        start = index if forward else taps - 1 - index
        total = total + kernel[index][None, :] * padded[start : start + count].astype(F32)
    return jax.nn.silu(total).astype(BF16)


def on_device(
    hidden,
    bases,
    w_gate,
    w_values,
    w_state_io,
    w_step,
    conv_values,
    conv_values_bias,
    conv_state_io,
    conv_state_bias,
    step_bias,
    decay_rate,
    skip_gain,
    norm_gain,
    w_out,
):
    rows, width = hidden.shape
    heads = w_step.shape[1]
    groups = w_state_io.shape[1] // (2 * N)
    per_group = heads // groups
    blocks = rows // Q
    known = jnp.where(bases == 4, 0.0, 1.0).astype(F32)

    lane_idx = jnp.arange(LANE)
    anti = (lane_idx[:, None] + lane_idx[None, :] == LANE - 1).astype(BF16)

    def lane_reverse(block):
        count = block.shape[0]
        flipped = jnp.einsum(
            "rki,ij->rkj", block.reshape(count, width // LANE, LANE), anti, preferred_element_type=F32
        ).astype(BF16)
        return jnp.flip(flipped, 1).reshape(count, width)

    hidden_rev = lane_reverse(hidden)

    taps = K - 1
    known_cols = jnp.broadcast_to(known.astype(BF16)[:, None], (rows, LANE))
    edge_first = jnp.concatenate([hidden[:taps], known_cols[:taps]], axis=1)
    edge_last = jnp.concatenate([hidden[rows - taps :], known_cols[rows - taps :]], axis=1)
    from_prev = shifted(edge_last, "seq", 1)
    from_next = shifted(edge_first, "seq", -1)
    rim_rows = jnp.concatenate([from_prev[:, :width], lane_reverse(from_next[:, :width])], axis=0)
    rim_known = jnp.concatenate([from_prev[:, width], from_next[:, width]], axis=0).astype(F32)
    pad_rows = (-(rows + 2 * taps)) % 8
    rev_source = jnp.concatenate(
        [hidden_rev, rim_rows, jnp.zeros((pad_rows, width), BF16)], axis=0
    )
    rev_known = jnp.concatenate([known, rim_known, jnp.zeros((pad_rows,), F32)], axis=0)

    def project(source, mask):
        gate_in = jnp.dot(source, w_gate, preferred_element_type=F32).astype(BF16)
        values = (jnp.dot(source, w_values, preferred_element_type=F32) * mask[:, None]).astype(BF16)
        state_io = jnp.dot(source, w_state_io, preferred_element_type=F32).astype(BF16)
        step_raw = jnp.dot(source, w_step, preferred_element_type=F32).astype(BF16)
        return gate_in, values, state_io, step_raw

    t_idx = jnp.arange(Q)

    def local_scan(pieces, forward):
        gate_in, values, state_io, step_raw = pieces
        sign = 1 if forward else -1
        if forward:
            pv = jnp.concatenate([rim_values[:taps], values], axis=0)
            ps = jnp.concatenate([rim_state[:taps], state_io], axis=0)
        else:
            pv = jnp.concatenate([values, rim_values[taps:]], axis=0)
            ps = jnp.concatenate([state_io, rim_state[taps:]], axis=0)
        values_c = conv_silu(pv, conv_values, conv_values_bias, rows, forward)
        state_c = conv_silu(ps, conv_state_io, conv_state_bias, rows, forward)
        delta = jax.nn.softplus(step_raw.astype(F32) + step_bias[None, :])
        logdec = -decay_rate[None, :] * delta

        sb = state_c.reshape(blocks, Q, groups, 2, N)
        c_vec = sb[:, :, :, 1, :]
        ld = logdec.reshape(blocks, Q, heads)
        if forward:
            mask = t_idx[:, None] >= t_idx[None, :]
        else:
            mask = t_idx[:, None] <= t_idx[None, :]
        acc = jnp.einsum("ts,bsh->bth", mask.astype(F32), ld, precision=HIGHEST)
        blk = jnp.sum(ld, axis=1)
        acc_g, delta_g, acc_t, delta_t = group_layout(acc.reshape(rows, heads), delta, groups, per_group)
        states = block_states(state_c, values_c.T, acc_t, delta_t, forward)

        order = list(range(blocks)) if forward else list(range(blocks - 1, -1, -1))
        block_decay = jnp.exp(blk)
        running = jnp.zeros((heads, P_SIZE, N), F32)
        local_start = [None] * blocks
        entering = [None] * blocks
        log_before = jnp.zeros((heads,), F32)
        for index in order:
            local_start[index] = running
            entering[index] = jnp.exp(log_before)
            running = block_decay[index][:, None, None] * running + states[index]
            log_before = log_before + blk[index]
        total = log_before
        carried = exclusive_carry(total, running, sign)
        intra = block_intra(state_c, values_c, acc_g, acc_t, delta_t, forward)
        start = jnp.stack(
            [local_start[index] + entering[index][:, None, None] * carried for index in range(blocks)]
        )
        start = start.reshape(blocks, groups, per_group * P_SIZE, N)
        c_f32 = c_vec.astype(F32)
        inter = jnp.concatenate(
            [
                jnp.einsum("btn,bkn->btk", c_f32[:, :, group], start[:, group], precision=HIGHEST)
                for group in range(groups)
            ],
            axis=2,
        ).reshape(rows, heads, P_SIZE) * jnp.exp(acc).reshape(rows, heads)[:, :, None]
        x = values_c.astype(F32).reshape(rows, heads, P_SIZE)
        outputs = intra.reshape(rows, heads, P_SIZE) + inter + skip_gain[None, :, None] * x
        gated = outputs.reshape(rows, heads * P_SIZE) * jax.nn.silu(gate_in.astype(F32))
        grouped = gated.reshape(rows, groups, per_group * P_SIZE)
        scale = lax.rsqrt(jnp.mean(grouped * grouped, axis=-1, keepdims=True) + EPSILON)
        return ((grouped * scale).reshape(rows, heads * P_SIZE) * norm_gain[None, :]).astype(BF16)

    forward_pieces = project(hidden, known)
    rev_all = project(rev_source, rev_known)
    rim_values = rev_all[1][rows : rows + 2 * taps]
    rim_state = rev_all[2][rows : rows + 2 * taps]
    backward_pieces = tuple(piece[:rows] for piece in rev_all)
    forward_out = local_scan(forward_pieces, True)
    backward_out = local_scan(backward_pieces, False)
    combined = (forward_out.astype(F32) + backward_out.astype(F32)).astype(BF16)
    chan = lax.axis_size("chan")
    partial = jnp.dot(combined, w_out, preferred_element_type=F32).astype(BF16)
    partial = jnp.transpose(partial.reshape(rows, chan, width // chan), (1, 0, 2))
    summed = lax.psum_scatter(partial, "chan", scatter_dimension=0, tiled=True)
    return summed.reshape(rows, width // chan)


def solution(mesh):
    return jax.shard_map(
        on_device,
        mesh=mesh,
        in_specs=(
            P(("groups", "seq"), None),
            P(("groups", "seq")),
            P(None, "chan"),
            P(None, "chan"),
            P(None, "chan"),
            P(None, "chan"),
            P(None, "chan"),
            P("chan"),
            P(None, "chan"),
            P("chan"),
            P("chan"),
            P("chan"),
            P("chan"),
            P("chan"),
            P("chan", None),
        ),
        out_specs=P(("groups", "seq"), "chan"),
        check_vma=False,
    )
```

```python
import jax
import jax.numpy as jnp
from jax import lax
from jax.sharding import PartitionSpec as P
from jax.experimental import pallas as pl

P_SIZE = 64
N = 128
K = 4
Q = 128
LANE = 128


EPSILON = 1e-05
HIGHEST = lax.Precision.HIGHEST
F32 = jnp.float32
BF16 = jnp.bfloat16


def shifted(value, axis, steps):
    count = lax.axis_size(axis)
    pairs = [(source, source + steps) for source in range(count) if 0 <= source + steps < count]
    if not pairs:
        return jax.tree.map(jnp.zeros_like, value)
    return lax.ppermute(value, axis, pairs)


def exclusive_carry(total_log, state, sign):
    count = lax.axis_size("seq")
    heads = state.shape[0]
    flat = state.reshape(heads, -1)
    size = flat.shape[1]

    def send(log, st, distance):
        log_hi = log.astype(BF16)
        log_lo = (log - log_hi.astype(F32)).astype(BF16)
        packed = jnp.concatenate(
            [
                st.astype(BF16),
                jnp.broadcast_to(log_hi[:, None], (heads, LANE)),
                jnp.broadcast_to(log_lo[:, None], (heads, LANE)),
            ],
            axis=1,
        )
        got = shifted(packed, "seq", sign * distance)
        got_log = got[:, size].astype(F32) + got[:, size + LANE].astype(F32)
        return got_log, got[:, :size].astype(F32)

    got_log, got_state = send(total_log, flat, 1)
    x_log, x_state = got_log, got_state
    i_log = got_log + total_log
    i_state = jnp.exp(total_log)[:, None] * got_state + flat
    covered, window = 1, 2
    while covered < count - 1:
        r_log, r_state = send(i_log, i_state, window)
        x_state = jnp.exp(x_log)[:, None] * r_state + x_state
        x_log = x_log + r_log
        covered += window
        if covered < count - 1:
            i_state = jnp.exp(i_log)[:, None] * r_state + i_state
            i_log = i_log + r_log
            window *= 2
    return x_state.reshape(state.shape)


def group_layout(acc, delta, groups, per_group):
    rows = acc.shape[0]
    acc_g = jnp.transpose(acc.reshape(rows, groups, per_group), (1, 0, 2))
    delta_g = jnp.transpose(delta.reshape(rows, groups, per_group), (1, 0, 2))
    return acc_g, delta_g, jnp.transpose(acc_g, (0, 2, 1)), jnp.transpose(delta_g, (0, 2, 1))


def block_states(state_c, values_t, acc_t, delta_t, forward, interpret=False):
    rows = values_t.shape[1]
    groups, per_group, _ = acc_t.shape
    blocks = rows // Q
    width_g = per_group * P_SIZE

    def kernel(b_ref, xt_ref, at_ref, dt_ref, s_ref):
        b_blk = b_ref[...]
        for j in range(per_group):
            a_row = at_ref[0, j : j + 1, :]
            d_row = dt_ref[0, j : j + 1, :]
            a_end = a_row[:, Q - 1 : Q] if forward else a_row[:, 0:1]
            xt_j = xt_ref[j * P_SIZE : (j + 1) * P_SIZE, :]
            tx = (jnp.exp(a_end - a_row) * d_row) * xt_j.astype(F32)
            t_hi = tx.astype(BF16)
            t_lo = (tx - t_hi.astype(F32)).astype(BF16)
            s_ref[0, j] = jnp.dot(t_hi, b_blk, preferred_element_type=F32) + jnp.dot(
                t_lo, b_blk, preferred_element_type=F32
            )

    return pl.pallas_call(
        kernel,
        grid=(blocks, groups),
        in_specs=[
            pl.BlockSpec((Q, N), lambda b, g: (b, 2 * g)),
            pl.BlockSpec((width_g, Q), lambda b, g: (g, b)),
            pl.BlockSpec((1, per_group, Q), lambda b, g: (g, 0, b)),
            pl.BlockSpec((1, per_group, Q), lambda b, g: (g, 0, b)),
        ],
        out_specs=pl.BlockSpec((1, per_group, P_SIZE, N), lambda b, g: (b, g, 0, 0)),
        out_shape=jax.ShapeDtypeStruct((blocks, groups * per_group, P_SIZE, N), F32),
        interpret=interpret,
    )(state_c, values_t, acc_t, delta_t)


def block_intra(state_c, values_t, acc_g, acc_t, delta_t, forward, interpret=False):
    rows = values_t.shape[1]
    groups, _, per_group = acc_g.shape
    blocks = rows // Q
    width_g = per_group * P_SIZE

    def kernel(c_ref, b_ref, xt_ref, a_ref, at_ref, dt_ref, y_ref):
        inner = lax.dot_general(
            c_ref[...], b_ref[...], (((1,), (1,)), ((), ())), preferred_element_type=F32
        )
        row = lax.broadcasted_iota(jnp.int32, (Q, Q), 0)
        col = lax.broadcasted_iota(jnp.int32, (Q, Q), 1)
        mask = row >= col if forward else row <= col
        for j in range(per_group):
            a_col = a_ref[0, :, j : j + 1]
            a_row = at_ref[0, j : j + 1, :]
            d_row = dt_ref[0, j : j + 1, :]
            differ = jnp.where(mask, a_col - a_row, 0.0)
            m = jnp.where(mask, jnp.exp(differ), 0.0) * d_row * inner
            xt_j = xt_ref[j * P_SIZE : (j + 1) * P_SIZE, :]
            y_ref[j * P_SIZE : (j + 1) * P_SIZE, :] = lax.dot_general(
                xt_j, m.astype(BF16), (((1,), (1,)), ((), ())), preferred_element_type=F32
            )

    return pl.pallas_call(
        kernel,
        grid=(blocks, groups),
        in_specs=[
            pl.BlockSpec((Q, N), lambda b, g: (b, 2 * g + 1)),
            pl.BlockSpec((Q, N), lambda b, g: (b, 2 * g)),
            pl.BlockSpec((width_g, Q), lambda b, g: (g, b)),
            pl.BlockSpec((1, Q, per_group), lambda b, g: (g, b, 0)),
            pl.BlockSpec((1, per_group, Q), lambda b, g: (g, 0, b)),
            pl.BlockSpec((1, per_group, Q), lambda b, g: (g, 0, b)),
        ],
        out_specs=pl.BlockSpec((width_g, Q), lambda b, g: (g, b)),
        out_shape=jax.ShapeDtypeStruct((groups * width_g, rows), F32),
        interpret=interpret,
    )(state_c, state_c, values_t, acc_g, acc_t, delta_t)


def conv_silu(padded, kernel, offset, count, forward):
    taps = kernel.shape[0]
    total = jnp.zeros((count, padded.shape[1]), F32) + offset[None, :]
    for index in range(taps):
        start = index if forward else taps - 1 - index
        total = total + kernel[index][None, :] * padded[start : start + count].astype(F32)
    return jax.nn.silu(total).astype(BF16)


def on_device(
    hidden,
    bases,
    w_gate,
    w_values,
    w_state_io,
    w_step,
    conv_values,
    conv_values_bias,
    conv_state_io,
    conv_state_bias,
    step_bias,
    decay_rate,
    skip_gain,
    norm_gain,
    w_out,
):
    rows, width = hidden.shape
    heads = w_step.shape[1]
    groups = w_state_io.shape[1] // (2 * N)
    per_group = heads // groups
    blocks = rows // Q
    known = jnp.where(bases == 4, 0.0, 1.0).astype(F32)

    lane_idx = jnp.arange(LANE)
    anti = (lane_idx[:, None] + lane_idx[None, :] == LANE - 1).astype(BF16)

    def lane_reverse(block):
        count = block.shape[0]
        flipped = jnp.einsum(
            "rki,ij->rkj", block.reshape(count, width // LANE, LANE), anti, preferred_element_type=F32
        ).astype(BF16)
        return jnp.flip(flipped, 1).reshape(count, width)

    hidden_rev = lane_reverse(hidden)

    taps = K - 1
    known_cols = jnp.broadcast_to(known.astype(BF16)[:, None], (rows, LANE))
    edge_first = jnp.concatenate([hidden[:taps], known_cols[:taps]], axis=1)
    edge_last = jnp.concatenate([hidden[rows - taps :], known_cols[rows - taps :]], axis=1)
    from_prev = shifted(edge_last, "seq", 1)
    from_next = shifted(edge_first, "seq", -1)
    rim_rows = jnp.concatenate([from_prev[:, :width], lane_reverse(from_next[:, :width])], axis=0)
    rim_known = jnp.concatenate([from_prev[:, width], from_next[:, width]], axis=0).astype(F32)
    rim_values = (
        jnp.dot(rim_rows, w_values, preferred_element_type=F32) * rim_known[:, None]
    ).astype(BF16)
    rim_state = jnp.dot(rim_rows, w_state_io, preferred_element_type=F32).astype(BF16)

    def project(source):
        gate_in = jnp.dot(source, w_gate, preferred_element_type=F32).astype(BF16)
        values = (jnp.dot(source, w_values, preferred_element_type=F32) * known[:, None]).astype(BF16)
        state_io = jnp.dot(source, w_state_io, preferred_element_type=F32).astype(BF16)
        step_raw = jnp.dot(source, w_step, preferred_element_type=F32).astype(BF16)
        return gate_in, values, state_io, step_raw

    t_idx = jnp.arange(Q)

    def local_scan(pieces, forward):
        gate_in, values, state_io, step_raw = pieces
        sign = 1 if forward else -1
        if forward:
            pv = jnp.concatenate([rim_values[:taps], values], axis=0)
            ps = jnp.concatenate([rim_state[:taps], state_io], axis=0)
        else:
            pv = jnp.concatenate([values, rim_values[taps:]], axis=0)
            ps = jnp.concatenate([state_io, rim_state[taps:]], axis=0)
        values_c = conv_silu(pv, conv_values, conv_values_bias, rows, forward)
        state_c = conv_silu(ps, conv_state_io, conv_state_bias, rows, forward)
        delta = jax.nn.softplus(step_raw.astype(F32) + step_bias[None, :])
        logdec = -decay_rate[None, :] * delta

        sb = state_c.reshape(blocks, Q, groups, 2, N)
        c_vec = sb[:, :, :, 1, :]
        ld = logdec.reshape(blocks, Q, heads)
        if forward:
            mask = t_idx[:, None] >= t_idx[None, :]
        else:
            mask = t_idx[:, None] <= t_idx[None, :]
        acc = jnp.einsum("ts,bsh->bth", mask.astype(F32), ld, precision=HIGHEST)
        blk = jnp.sum(ld, axis=1)
        acc_g, delta_g, acc_t, delta_t = group_layout(acc.reshape(rows, heads), delta, groups, per_group)
        values_t = values_c.T
        states = block_states(state_c, values_t, acc_t, delta_t, forward)

        order = list(range(blocks)) if forward else list(range(blocks - 1, -1, -1))
        block_decay = jnp.exp(blk)
        running = jnp.zeros((heads, P_SIZE, N), F32)
        local_start = [None] * blocks
        entering = [None] * blocks
        log_before = jnp.zeros((heads,), F32)
        for index in order:
            local_start[index] = running
            entering[index] = jnp.exp(log_before)
            running = block_decay[index][:, None, None] * running + states[index]
            log_before = log_before + blk[index]
        total = log_before
        carried = exclusive_carry(total, running, sign)
        intra = block_intra(state_c, values_t, acc_g, acc_t, delta_t, forward).T
        start = jnp.stack(
            [local_start[index] + entering[index][:, None, None] * carried for index in range(blocks)]
        )
        start = start.reshape(blocks, groups, per_group * P_SIZE, N)
        c_f32 = c_vec.astype(F32)
        inter = jnp.concatenate(
            [
                jnp.einsum("btn,bkn->btk", c_f32[:, :, group], start[:, group], precision=HIGHEST)
                for group in range(groups)
            ],
            axis=2,
        ).reshape(rows, heads, P_SIZE) * jnp.exp(acc).reshape(rows, heads)[:, :, None]
        x = values_c.astype(F32).reshape(rows, heads, P_SIZE)
        outputs = intra.reshape(rows, heads, P_SIZE) + inter + skip_gain[None, :, None] * x
        gated = outputs.reshape(rows, heads * P_SIZE) * jax.nn.silu(gate_in.astype(F32))
        grouped = gated.reshape(rows, groups, per_group * P_SIZE)
        scale = lax.rsqrt(jnp.mean(grouped * grouped, axis=-1, keepdims=True) + EPSILON)
        return ((grouped * scale).reshape(rows, heads * P_SIZE) * norm_gain[None, :]).astype(BF16)

    forward_out = local_scan(project(hidden), True)
    backward_out = local_scan(project(hidden_rev), False)
    combined = (forward_out.astype(F32) + backward_out.astype(F32)).astype(BF16)
    chan = lax.axis_size("chan")
    partial = jnp.dot(combined, w_out, preferred_element_type=F32).astype(BF16)
    partial = jnp.transpose(partial.reshape(rows, chan, width // chan), (1, 0, 2))
    summed = lax.psum_scatter(partial, "chan", scatter_dimension=0, tiled=True)
    return summed.reshape(rows, width // chan)


def solution(mesh):
    return jax.shard_map(
        on_device,
        mesh=mesh,
        in_specs=(
            P(("groups", "seq"), None),
            P(("groups", "seq")),
            P(None, "chan"),
            P(None, "chan"),
            P(None, "chan"),
            P(None, "chan"),
            P(None, "chan"),
            P("chan"),
            P(None, "chan"),
            P("chan"),
            P("chan"),
            P("chan"),
            P("chan"),
            P("chan"),
            P("chan", None),
        ),
        out_specs=P(("groups", "seq"), "chan"),
        check_vma=False,
    )
```

```python
import jax
import jax.numpy as jnp
from jax import lax
from jax.sharding import PartitionSpec as P
from jax.experimental import pallas as pl

P_SIZE = 64
N = 128
K = 4
Q = 128
LANE = 128


EPSILON = 1e-05
HIGHEST = lax.Precision.HIGHEST
F32 = jnp.float32
BF16 = jnp.bfloat16


def shifted(value, axis, steps):
    count = lax.axis_size(axis)
    pairs = [(source, source + steps) for source in range(count) if 0 <= source + steps < count]
    if not pairs:
        return jax.tree.map(jnp.zeros_like, value)
    return lax.ppermute(value, axis, pairs)


def exclusive_carry(total_log, state, sign):
    count = lax.axis_size("seq")
    heads = state.shape[0]
    flat = state.reshape(heads, -1)
    size = flat.shape[1]

    def send(log, st, distance):
        log_hi = log.astype(BF16)
        log_lo = (log - log_hi.astype(F32)).astype(BF16)
        packed = jnp.concatenate(
            [
                st.astype(BF16),
                jnp.broadcast_to(log_hi[:, None], (heads, LANE)),
                jnp.broadcast_to(log_lo[:, None], (heads, LANE)),
            ],
            axis=1,
        )
        got = shifted(packed, "seq", sign * distance)
        got_log = got[:, size].astype(F32) + got[:, size + LANE].astype(F32)
        return got_log, got[:, :size].astype(F32)

    got_log, got_state = send(total_log, flat, 1)
    x_log, x_state = got_log, got_state
    i_log = got_log + total_log
    i_state = jnp.exp(total_log)[:, None] * got_state + flat
    covered, window = 1, 2
    while covered < count - 1:
        r_log, r_state = send(i_log, i_state, window)
        x_state = jnp.exp(x_log)[:, None] * r_state + x_state
        x_log = x_log + r_log
        covered += window
        if covered < count - 1:
            i_state = jnp.exp(i_log)[:, None] * r_state + i_state
            i_log = i_log + r_log
            window *= 2
    return x_state.reshape(state.shape)


def group_layout(acc, delta, groups, per_group):
    rows = acc.shape[0]
    acc_g = jnp.transpose(acc.reshape(rows, groups, per_group), (1, 0, 2))
    delta_g = jnp.transpose(delta.reshape(rows, groups, per_group), (1, 0, 2))
    return acc_g, delta_g, jnp.transpose(acc_g, (0, 2, 1)), jnp.transpose(delta_g, (0, 2, 1))


def block_states(state_c, values_t, acc_t, delta_t, forward, interpret=False):
    rows = values_t.shape[1]
    groups, per_group, _ = acc_t.shape
    blocks = rows // Q
    width_g = per_group * P_SIZE

    def kernel(b_ref, xt_ref, at_ref, dt_ref, s_ref):
        b_blk = b_ref[...]
        for j in range(per_group):
            a_row = at_ref[0, j : j + 1, :]
            d_row = dt_ref[0, j : j + 1, :]
            a_end = a_row[:, Q - 1 : Q] if forward else a_row[:, 0:1]
            xt_j = xt_ref[j * P_SIZE : (j + 1) * P_SIZE, :]
            tx = (jnp.exp(a_end - a_row) * d_row) * xt_j.astype(F32)
            t_hi = tx.astype(BF16)
            t_lo = (tx - t_hi.astype(F32)).astype(BF16)
            s_ref[0, j] = jnp.dot(t_hi, b_blk, preferred_element_type=F32) + jnp.dot(
                t_lo, b_blk, preferred_element_type=F32
            )

    return pl.pallas_call(
        kernel,
        grid=(blocks, groups),
        in_specs=[
            pl.BlockSpec((Q, N), lambda b, g: (b, 2 * g)),
            pl.BlockSpec((width_g, Q), lambda b, g: (g, b)),
            pl.BlockSpec((1, per_group, Q), lambda b, g: (g, 0, b)),
            pl.BlockSpec((1, per_group, Q), lambda b, g: (g, 0, b)),
        ],
        out_specs=pl.BlockSpec((1, per_group, P_SIZE, N), lambda b, g: (b, g, 0, 0)),
        out_shape=jax.ShapeDtypeStruct((blocks, groups * per_group, P_SIZE, N), F32),
        interpret=interpret,
    )(state_c, values_t, acc_t, delta_t)


def block_intra(state_c, values_t, acc_g, acc_t, delta_t, forward, interpret=False):
    rows = values_t.shape[1]
    groups, _, per_group = acc_g.shape
    blocks = rows // Q
    width_g = per_group * P_SIZE

    def kernel(c_ref, b_ref, xt_ref, a_ref, at_ref, dt_ref, y_ref):
        inner = lax.dot_general(
            c_ref[...], b_ref[...], (((1,), (1,)), ((), ())), preferred_element_type=F32
        )
        row = lax.broadcasted_iota(jnp.int32, (Q, Q), 0)
        col = lax.broadcasted_iota(jnp.int32, (Q, Q), 1)
        mask = row >= col if forward else row <= col
        for j in range(per_group):
            a_col = a_ref[0, :, j : j + 1]
            a_row = at_ref[0, j : j + 1, :]
            d_row = dt_ref[0, j : j + 1, :]
            differ = jnp.where(mask, a_col - a_row, 0.0)
            m = jnp.where(mask, jnp.exp(differ), 0.0) * d_row * inner
            xt_j = xt_ref[j * P_SIZE : (j + 1) * P_SIZE, :]
            y_ref[j * P_SIZE : (j + 1) * P_SIZE, :] = lax.dot_general(
                xt_j, m.astype(BF16), (((1,), (1,)), ((), ())), preferred_element_type=F32
            )

    return pl.pallas_call(
        kernel,
        grid=(blocks, groups),
        in_specs=[
            pl.BlockSpec((Q, N), lambda b, g: (b, 2 * g + 1)),
            pl.BlockSpec((Q, N), lambda b, g: (b, 2 * g)),
            pl.BlockSpec((width_g, Q), lambda b, g: (g, b)),
            pl.BlockSpec((1, Q, per_group), lambda b, g: (g, b, 0)),
            pl.BlockSpec((1, per_group, Q), lambda b, g: (g, 0, b)),
            pl.BlockSpec((1, per_group, Q), lambda b, g: (g, 0, b)),
        ],
        out_specs=pl.BlockSpec((width_g, Q), lambda b, g: (g, b)),
        out_shape=jax.ShapeDtypeStruct((groups * width_g, rows), F32),
        interpret=interpret,
    )(state_c, state_c, values_t, acc_g, acc_t, delta_t)


def block_finish(intra_t, state_c, values_t, acc_t, start, skip_col, interpret=False):
    rows = values_t.shape[1]
    groups, per_group, _ = acc_t.shape
    blocks = rows // Q
    width_g = per_group * P_SIZE

    def kernel(y_ref, c_ref, xt_ref, at_ref, s_ref, k_ref, o_ref):
        c_blk = c_ref[...]
        dims = (((1,), (1,)), ((), ()))
        for j in range(per_group):
            lo_row, hi_row = j * P_SIZE, (j + 1) * P_SIZE
            s_j = s_ref[0, j]
            s_hi = s_j.astype(BF16)
            s_lo = (s_j - s_hi.astype(F32)).astype(BF16)
            inter = lax.dot_general(s_hi, c_blk, dims, preferred_element_type=F32) + lax.dot_general(
                s_lo, c_blk, dims, preferred_element_type=F32
            )
            inter = inter * jnp.exp(at_ref[0, j : j + 1, :])
            o_ref[lo_row:hi_row, :] = (
                y_ref[lo_row:hi_row, :]
                + inter
                + k_ref[lo_row:hi_row, :] * xt_ref[lo_row:hi_row, :].astype(F32)
            )

    return pl.pallas_call(
        kernel,
        grid=(blocks, groups),
        in_specs=[
            pl.BlockSpec((width_g, Q), lambda b, g: (g, b)),
            pl.BlockSpec((Q, N), lambda b, g: (b, 2 * g + 1)),
            pl.BlockSpec((width_g, Q), lambda b, g: (g, b)),
            pl.BlockSpec((1, per_group, Q), lambda b, g: (g, 0, b)),
            pl.BlockSpec((1, per_group, P_SIZE, N), lambda b, g: (b, g, 0, 0)),
            pl.BlockSpec((width_g, 1), lambda b, g: (g, 0)),
        ],
        out_specs=pl.BlockSpec((width_g, Q), lambda b, g: (g, b)),
        out_shape=jax.ShapeDtypeStruct((groups * width_g, rows), F32),
        interpret=interpret,
    )(intra_t, state_c, values_t, acc_t, start, skip_col)


def conv_silu(padded, kernel, offset, count, forward):
    taps = kernel.shape[0]
    total = jnp.zeros((count, padded.shape[1]), F32) + offset[None, :]
    for index in range(taps):
        start = index if forward else taps - 1 - index
        total = total + kernel[index][None, :] * padded[start : start + count].astype(F32)
    return jax.nn.silu(total).astype(BF16)


def on_device(
    hidden,
    bases,
    w_gate,
    w_values,
    w_state_io,
    w_step,
    conv_values,
    conv_values_bias,
    conv_state_io,
    conv_state_bias,
    step_bias,
    decay_rate,
    skip_gain,
    norm_gain,
    w_out,
):
    rows, width = hidden.shape
    heads = w_step.shape[1]
    groups = w_state_io.shape[1] // (2 * N)
    per_group = heads // groups
    blocks = rows // Q
    known = jnp.where(bases == 4, 0.0, 1.0).astype(F32)

    lane_idx = jnp.arange(LANE)
    anti = (lane_idx[:, None] + lane_idx[None, :] == LANE - 1).astype(BF16)

    def lane_reverse(block):
        count = block.shape[0]
        flipped = jnp.einsum(
            "rki,ij->rkj", block.reshape(count, width // LANE, LANE), anti, preferred_element_type=F32
        ).astype(BF16)
        return jnp.flip(flipped, 1).reshape(count, width)

    hidden_rev = lane_reverse(hidden)

    taps = K - 1
    known_cols = jnp.broadcast_to(known.astype(BF16)[:, None], (rows, LANE))
    edge_first = jnp.concatenate([hidden[:taps], known_cols[:taps]], axis=1)
    edge_last = jnp.concatenate([hidden[rows - taps :], known_cols[rows - taps :]], axis=1)
    from_prev = shifted(edge_last, "seq", 1)
    from_next = shifted(edge_first, "seq", -1)
    rim_rows = jnp.concatenate([from_prev[:, :width], lane_reverse(from_next[:, :width])], axis=0)
    rim_known = jnp.concatenate([from_prev[:, width], from_next[:, width]], axis=0).astype(F32)
    rim_values = (
        jnp.dot(rim_rows, w_values, preferred_element_type=F32) * rim_known[:, None]
    ).astype(BF16)
    rim_state = jnp.dot(rim_rows, w_state_io, preferred_element_type=F32).astype(BF16)

    def project(source):
        gate_in = jnp.dot(source, w_gate, preferred_element_type=F32).astype(BF16)
        values = (jnp.dot(source, w_values, preferred_element_type=F32) * known[:, None]).astype(BF16)
        state_io = jnp.dot(source, w_state_io, preferred_element_type=F32).astype(BF16)
        step_raw = jnp.dot(source, w_step, preferred_element_type=F32).astype(BF16)
        return gate_in, values, state_io, step_raw

    t_idx = jnp.arange(Q)

    def local_scan(pieces, forward):
        gate_in, values, state_io, step_raw = pieces
        sign = 1 if forward else -1
        if forward:
            pv = jnp.concatenate([rim_values[:taps], values], axis=0)
            ps = jnp.concatenate([rim_state[:taps], state_io], axis=0)
        else:
            pv = jnp.concatenate([values, rim_values[taps:]], axis=0)
            ps = jnp.concatenate([state_io, rim_state[taps:]], axis=0)
        values_c = conv_silu(pv, conv_values, conv_values_bias, rows, forward)
        state_c = conv_silu(ps, conv_state_io, conv_state_bias, rows, forward)
        delta = jax.nn.softplus(step_raw.astype(F32) + step_bias[None, :])
        logdec = -decay_rate[None, :] * delta

        sb = state_c.reshape(blocks, Q, groups, 2, N)
        c_vec = sb[:, :, :, 1, :]
        ld = logdec.reshape(blocks, Q, heads)
        if forward:
            mask = t_idx[:, None] >= t_idx[None, :]
        else:
            mask = t_idx[:, None] <= t_idx[None, :]
        acc = jnp.einsum("ts,bsh->bth", mask.astype(F32), ld, precision=HIGHEST)
        blk = jnp.sum(ld, axis=1)
        acc_g, delta_g, acc_t, delta_t = group_layout(acc.reshape(rows, heads), delta, groups, per_group)
        values_t = values_c.T
        states = block_states(state_c, values_t, acc_t, delta_t, forward)

        order = list(range(blocks)) if forward else list(range(blocks - 1, -1, -1))
        block_decay = jnp.exp(blk)
        running = jnp.zeros((heads, P_SIZE, N), F32)
        local_start = [None] * blocks
        entering = [None] * blocks
        log_before = jnp.zeros((heads,), F32)
        for index in order:
            local_start[index] = running
            entering[index] = jnp.exp(log_before)
            running = block_decay[index][:, None, None] * running + states[index]
            log_before = log_before + blk[index]
        total = log_before
        carried = exclusive_carry(total, running, sign)
        intra_t = block_intra(state_c, values_t, acc_g, acc_t, delta_t, forward)
        start = jnp.stack(
            [local_start[index] + entering[index][:, None, None] * carried for index in range(blocks)]
        )
        skip_col = jnp.repeat(skip_gain, P_SIZE)[:, None]
        outputs = block_finish(intra_t, state_c, values_t, acc_t, start, skip_col).T
        gated = outputs.reshape(rows, heads * P_SIZE) * jax.nn.silu(gate_in.astype(F32))
        grouped = gated.reshape(rows, groups, per_group * P_SIZE)
        scale = lax.rsqrt(jnp.mean(grouped * grouped, axis=-1, keepdims=True) + EPSILON)
        return ((grouped * scale).reshape(rows, heads * P_SIZE) * norm_gain[None, :]).astype(BF16)

    forward_out = local_scan(project(hidden), True)
    backward_out = local_scan(project(hidden_rev), False)
    combined = (forward_out.astype(F32) + backward_out.astype(F32)).astype(BF16)
    chan = lax.axis_size("chan")
    partial = jnp.dot(combined, w_out, preferred_element_type=F32).astype(BF16)
    partial = jnp.transpose(partial.reshape(rows, chan, width // chan), (1, 0, 2))
    summed = lax.psum_scatter(partial, "chan", scatter_dimension=0, tiled=True)
    return summed.reshape(rows, width // chan)


def solution(mesh):
    return jax.shard_map(
        on_device,
        mesh=mesh,
        in_specs=(
            P(("groups", "seq"), None),
            P(("groups", "seq")),
            P(None, "chan"),
            P(None, "chan"),
            P(None, "chan"),
            P(None, "chan"),
            P(None, "chan"),
            P("chan"),
            P(None, "chan"),
            P("chan"),
            P("chan"),
            P("chan"),
            P("chan"),
            P("chan"),
            P("chan", None),
        ),
        out_specs=P(("groups", "seq"), "chan"),
        check_vma=False,
    )
```

```python
import jax
import jax.numpy as jnp
from jax import lax
from jax.sharding import PartitionSpec as P
from jax.experimental import pallas as pl

P_SIZE = 64
N = 128
K = 4
Q = 128
LANE = 128


EPSILON = 1e-05
HIGHEST = lax.Precision.HIGHEST
F32 = jnp.float32
BF16 = jnp.bfloat16


def shifted(value, axis, steps):
    count = lax.axis_size(axis)
    pairs = [(source, source + steps) for source in range(count) if 0 <= source + steps < count]
    if not pairs:
        return jax.tree.map(jnp.zeros_like, value)
    return lax.ppermute(value, axis, pairs)


def exclusive_carry(total_log, state, sign):
    count = lax.axis_size("seq")
    heads = state.shape[0]
    flat = state.reshape(heads, -1)
    size = flat.shape[1]

    def send(log, st, distance):
        log_hi = log.astype(BF16)
        log_lo = (log - log_hi.astype(F32)).astype(BF16)
        packed = jnp.concatenate(
            [
                st.astype(BF16),
                jnp.broadcast_to(log_hi[:, None], (heads, LANE)),
                jnp.broadcast_to(log_lo[:, None], (heads, LANE)),
            ],
            axis=1,
        )
        got = shifted(packed, "seq", sign * distance)
        got_log = got[:, size].astype(F32) + got[:, size + LANE].astype(F32)
        return got_log, got[:, :size].astype(F32)

    got_log, got_state = send(total_log, flat, 1)
    x_log, x_state = got_log, got_state
    i_log = got_log + total_log
    i_state = jnp.exp(total_log)[:, None] * got_state + flat
    covered, window = 1, 2
    while covered < count - 1:
        r_log, r_state = send(i_log, i_state, window)
        x_state = jnp.exp(x_log)[:, None] * r_state + x_state
        x_log = x_log + r_log
        covered += window
        if covered < count - 1:
            i_state = jnp.exp(i_log)[:, None] * r_state + i_state
            i_log = i_log + r_log
            window *= 2
    return x_state.reshape(state.shape)


def group_layout(acc, delta, groups, per_group):
    rows = acc.shape[0]
    acc_g = jnp.transpose(acc.reshape(rows, groups, per_group), (1, 0, 2))
    delta_g = jnp.transpose(delta.reshape(rows, groups, per_group), (1, 0, 2))
    return acc_g, delta_g, jnp.transpose(acc_g, (0, 2, 1)), jnp.transpose(delta_g, (0, 2, 1))


def block_states(state_c, values_t, acc_t, delta_t, forward, interpret=False):
    rows = values_t.shape[1]
    groups, per_group, _ = acc_t.shape
    blocks = rows // Q
    width_g = per_group * P_SIZE

    def kernel(b_ref, xt_ref, at_ref, dt_ref, s_ref):
        b_blk = b_ref[...]
        for j in range(per_group):
            a_row = at_ref[0, j : j + 1, :]
            d_row = dt_ref[0, j : j + 1, :]
            a_end = a_row[:, Q - 1 : Q] if forward else a_row[:, 0:1]
            xt_j = xt_ref[j * P_SIZE : (j + 1) * P_SIZE, :]
            tx = (jnp.exp(a_end - a_row) * d_row) * xt_j.astype(F32)
            t_hi = tx.astype(BF16)
            t_lo = (tx - t_hi.astype(F32)).astype(BF16)
            s_ref[0, j] = jnp.dot(t_hi, b_blk, preferred_element_type=F32) + jnp.dot(
                t_lo, b_blk, preferred_element_type=F32
            )

    return pl.pallas_call(
        kernel,
        grid=(blocks, groups),
        in_specs=[
            pl.BlockSpec((Q, N), lambda b, g: (b, 2 * g)),
            pl.BlockSpec((width_g, Q), lambda b, g: (g, b)),
            pl.BlockSpec((1, per_group, Q), lambda b, g: (g, 0, b)),
            pl.BlockSpec((1, per_group, Q), lambda b, g: (g, 0, b)),
        ],
        out_specs=pl.BlockSpec((1, per_group, P_SIZE, N), lambda b, g: (b, g, 0, 0)),
        out_shape=jax.ShapeDtypeStruct((blocks, groups * per_group, P_SIZE, N), F32),
        interpret=interpret,
    )(state_c, values_t, acc_t, delta_t)


def block_intra(state_c, values_t, acc_g, acc_t, delta_t, forward, interpret=False):
    rows = values_t.shape[1]
    groups, _, per_group = acc_g.shape
    blocks = rows // Q
    width_g = per_group * P_SIZE

    def kernel(c_ref, b_ref, xt_ref, a_ref, at_ref, dt_ref, y_ref):
        inner = lax.dot_general(
            c_ref[...], b_ref[...], (((1,), (1,)), ((), ())), preferred_element_type=F32
        )
        row = lax.broadcasted_iota(jnp.int32, (Q, Q), 0)
        col = lax.broadcasted_iota(jnp.int32, (Q, Q), 1)
        mask = row >= col if forward else row <= col
        for j in range(per_group):
            a_col = a_ref[0, :, j : j + 1]
            a_row = at_ref[0, j : j + 1, :]
            d_row = dt_ref[0, j : j + 1, :]
            differ = jnp.where(mask, a_col - a_row, 0.0)
            m = jnp.where(mask, jnp.exp(differ), 0.0) * d_row * inner
            xt_j = xt_ref[j * P_SIZE : (j + 1) * P_SIZE, :]
            y_ref[j * P_SIZE : (j + 1) * P_SIZE, :] = lax.dot_general(
                xt_j, m.astype(BF16), (((1,), (1,)), ((), ())), preferred_element_type=F32
            )

    return pl.pallas_call(
        kernel,
        grid=(blocks, groups),
        in_specs=[
            pl.BlockSpec((Q, N), lambda b, g: (b, 2 * g + 1)),
            pl.BlockSpec((Q, N), lambda b, g: (b, 2 * g)),
            pl.BlockSpec((width_g, Q), lambda b, g: (g, b)),
            pl.BlockSpec((1, Q, per_group), lambda b, g: (g, b, 0)),
            pl.BlockSpec((1, per_group, Q), lambda b, g: (g, 0, b)),
            pl.BlockSpec((1, per_group, Q), lambda b, g: (g, 0, b)),
        ],
        out_specs=pl.BlockSpec((width_g, Q), lambda b, g: (g, b)),
        out_shape=jax.ShapeDtypeStruct((groups * width_g, rows), F32),
        interpret=interpret,
    )(state_c, state_c, values_t, acc_g, acc_t, delta_t)


def block_finish(intra_t, state_c, values_t, acc_t, start, skip_col, gate_t, gain_col, interpret=False):
    rows = values_t.shape[1]
    groups, per_group, _ = acc_t.shape
    blocks = rows // Q
    width_g = per_group * P_SIZE

    def kernel(y_ref, c_ref, xt_ref, at_ref, s_ref, k_ref, g_ref, n_ref, o_ref):
        c_blk = c_ref[...]
        dims = (((1,), (1,)), ((), ()))
        total = jnp.zeros((1, Q), F32)
        for j in range(per_group):
            lo_row, hi_row = j * P_SIZE, (j + 1) * P_SIZE
            s_j = s_ref[0, j]
            s_hi = s_j.astype(BF16)
            s_lo = (s_j - s_hi.astype(F32)).astype(BF16)
            inter = lax.dot_general(s_hi, c_blk, dims, preferred_element_type=F32) + lax.dot_general(
                s_lo, c_blk, dims, preferred_element_type=F32
            )
            inter = inter * jnp.exp(at_ref[0, j : j + 1, :])
            out = (
                y_ref[lo_row:hi_row, :]
                + inter
                + k_ref[lo_row:hi_row, :] * xt_ref[lo_row:hi_row, :].astype(F32)
            )
            gate = g_ref[lo_row:hi_row, :].astype(F32)
            gated = out * (gate / (1.0 + jnp.exp(-gate)))
            total = total + jnp.sum(gated * gated, axis=0, keepdims=True)
            o_ref[lo_row:hi_row, :] = gated
        scale = lax.rsqrt(total / width_g + EPSILON)
        for j in range(per_group):
            lo_row, hi_row = j * P_SIZE, (j + 1) * P_SIZE
            o_ref[lo_row:hi_row, :] = o_ref[lo_row:hi_row, :] * scale * n_ref[lo_row:hi_row, :]

    return pl.pallas_call(
        kernel,
        grid=(blocks, groups),
        in_specs=[
            pl.BlockSpec((width_g, Q), lambda b, g: (g, b)),
            pl.BlockSpec((Q, N), lambda b, g: (b, 2 * g + 1)),
            pl.BlockSpec((width_g, Q), lambda b, g: (g, b)),
            pl.BlockSpec((1, per_group, Q), lambda b, g: (g, 0, b)),
            pl.BlockSpec((1, per_group, P_SIZE, N), lambda b, g: (b, g, 0, 0)),
            pl.BlockSpec((width_g, 1), lambda b, g: (g, 0)),
            pl.BlockSpec((width_g, Q), lambda b, g: (g, b)),
            pl.BlockSpec((width_g, 1), lambda b, g: (g, 0)),
        ],
        out_specs=pl.BlockSpec((width_g, Q), lambda b, g: (g, b)),
        out_shape=jax.ShapeDtypeStruct((groups * width_g, rows), F32),
        interpret=interpret,
    )(intra_t, state_c, values_t, acc_t, start, skip_col, gate_t, gain_col)


def conv_silu(padded, kernel, offset, count, forward):
    taps = kernel.shape[0]
    total = jnp.zeros((count, padded.shape[1]), F32) + offset[None, :]
    for index in range(taps):
        start = index if forward else taps - 1 - index
        total = total + kernel[index][None, :] * padded[start : start + count].astype(F32)
    return jax.nn.silu(total).astype(BF16)


def on_device(
    hidden,
    bases,
    w_gate,
    w_values,
    w_state_io,
    w_step,
    conv_values,
    conv_values_bias,
    conv_state_io,
    conv_state_bias,
    step_bias,
    decay_rate,
    skip_gain,
    norm_gain,
    w_out,
):
    rows, width = hidden.shape
    heads = w_step.shape[1]
    groups = w_state_io.shape[1] // (2 * N)
    per_group = heads // groups
    blocks = rows // Q
    known = jnp.where(bases == 4, 0.0, 1.0).astype(F32)

    lane_idx = jnp.arange(LANE)
    anti = (lane_idx[:, None] + lane_idx[None, :] == LANE - 1).astype(BF16)

    def lane_reverse(block):
        count = block.shape[0]
        flipped = jnp.einsum(
            "rki,ij->rkj", block.reshape(count, width // LANE, LANE), anti, preferred_element_type=F32
        ).astype(BF16)
        return jnp.flip(flipped, 1).reshape(count, width)

    hidden_rev = lane_reverse(hidden)

    taps = K - 1
    known_cols = jnp.broadcast_to(known.astype(BF16)[:, None], (rows, LANE))
    edge_first = jnp.concatenate([hidden[:taps], known_cols[:taps]], axis=1)
    edge_last = jnp.concatenate([hidden[rows - taps :], known_cols[rows - taps :]], axis=1)
    from_prev = shifted(edge_last, "seq", 1)
    from_next = shifted(edge_first, "seq", -1)
    rim_rows = jnp.concatenate([from_prev[:, :width], lane_reverse(from_next[:, :width])], axis=0)
    rim_known = jnp.concatenate([from_prev[:, width], from_next[:, width]], axis=0).astype(F32)
    rim_values = (
        jnp.dot(rim_rows, w_values, preferred_element_type=F32) * rim_known[:, None]
    ).astype(BF16)
    rim_state = jnp.dot(rim_rows, w_state_io, preferred_element_type=F32).astype(BF16)

    def project(source):
        gate_in = jnp.dot(source, w_gate, preferred_element_type=F32).astype(BF16)
        values = (jnp.dot(source, w_values, preferred_element_type=F32) * known[:, None]).astype(BF16)
        state_io = jnp.dot(source, w_state_io, preferred_element_type=F32).astype(BF16)
        step_raw = jnp.dot(source, w_step, preferred_element_type=F32).astype(BF16)
        return gate_in, values, state_io, step_raw

    t_idx = jnp.arange(Q)

    def local_scan(pieces, forward):
        gate_in, values, state_io, step_raw = pieces
        sign = 1 if forward else -1
        if forward:
            pv = jnp.concatenate([rim_values[:taps], values], axis=0)
            ps = jnp.concatenate([rim_state[:taps], state_io], axis=0)
        else:
            pv = jnp.concatenate([values, rim_values[taps:]], axis=0)
            ps = jnp.concatenate([state_io, rim_state[taps:]], axis=0)
        values_c = conv_silu(pv, conv_values, conv_values_bias, rows, forward)
        state_c = conv_silu(ps, conv_state_io, conv_state_bias, rows, forward)
        delta = jax.nn.softplus(step_raw.astype(F32) + step_bias[None, :])
        logdec = -decay_rate[None, :] * delta

        sb = state_c.reshape(blocks, Q, groups, 2, N)
        c_vec = sb[:, :, :, 1, :]
        ld = logdec.reshape(blocks, Q, heads)
        if forward:
            mask = t_idx[:, None] >= t_idx[None, :]
        else:
            mask = t_idx[:, None] <= t_idx[None, :]
        acc = jnp.einsum("ts,bsh->bth", mask.astype(F32), ld, precision=HIGHEST)
        blk = jnp.sum(ld, axis=1)
        acc_g, delta_g, acc_t, delta_t = group_layout(acc.reshape(rows, heads), delta, groups, per_group)
        values_t = values_c.T
        states = block_states(state_c, values_t, acc_t, delta_t, forward)

        order = list(range(blocks)) if forward else list(range(blocks - 1, -1, -1))
        block_decay = jnp.exp(blk)
        running = jnp.zeros((heads, P_SIZE, N), F32)
        local_start = [None] * blocks
        entering = [None] * blocks
        log_before = jnp.zeros((heads,), F32)
        for index in order:
            local_start[index] = running
            entering[index] = jnp.exp(log_before)
            running = block_decay[index][:, None, None] * running + states[index]
            log_before = log_before + blk[index]
        total = log_before
        carried = exclusive_carry(total, running, sign)
        intra_t = block_intra(state_c, values_t, acc_g, acc_t, delta_t, forward)
        start = jnp.stack(
            [local_start[index] + entering[index][:, None, None] * carried for index in range(blocks)]
        )
        skip_col = jnp.repeat(skip_gain, P_SIZE)[:, None]
        normed = block_finish(
            intra_t, state_c, values_t, acc_t, start, skip_col, gate_in.T, norm_gain[:, None]
        )
        return normed.T.astype(BF16)

    forward_out = local_scan(project(hidden), True)
    backward_out = local_scan(project(hidden_rev), False)
    combined = (forward_out.astype(F32) + backward_out.astype(F32)).astype(BF16)
    chan = lax.axis_size("chan")
    partial = jnp.dot(combined, w_out, preferred_element_type=F32).astype(BF16)
    partial = jnp.transpose(partial.reshape(rows, chan, width // chan), (1, 0, 2))
    summed = lax.psum_scatter(partial, "chan", scatter_dimension=0, tiled=True)
    return summed.reshape(rows, width // chan)


def solution(mesh):
    return jax.shard_map(
        on_device,
        mesh=mesh,
        in_specs=(
            P(("groups", "seq"), None),
            P(("groups", "seq")),
            P(None, "chan"),
            P(None, "chan"),
            P(None, "chan"),
            P(None, "chan"),
            P(None, "chan"),
            P("chan"),
            P(None, "chan"),
            P("chan"),
            P("chan"),
            P("chan"),
            P("chan"),
            P("chan"),
            P("chan", None),
        ),
        out_specs=P(("groups", "seq"), "chan"),
        check_vma=False,
    )
```

```python
import jax
import jax.numpy as jnp
from jax import lax
from jax.sharding import PartitionSpec as P
from jax.experimental import pallas as pl

P_SIZE = 64
N = 128
K = 4
Q = 128
LANE = 128


EPSILON = 1e-05
HIGHEST = lax.Precision.HIGHEST
F32 = jnp.float32
BF16 = jnp.bfloat16


def shifted(value, axis, steps):
    count = lax.axis_size(axis)
    pairs = [(source, source + steps) for source in range(count) if 0 <= source + steps < count]
    if not pairs:
        return jax.tree.map(jnp.zeros_like, value)
    return lax.ppermute(value, axis, pairs)


def exclusive_carry(total_log, state, sign):
    count = lax.axis_size("seq")
    heads = state.shape[0]
    flat = state.reshape(heads, -1)
    size = flat.shape[1]

    def send(log, st, distance):
        log_hi = log.astype(BF16)
        log_lo = (log - log_hi.astype(F32)).astype(BF16)
        packed = jnp.concatenate(
            [
                st.astype(BF16),
                jnp.broadcast_to(log_hi[:, None], (heads, LANE)),
                jnp.broadcast_to(log_lo[:, None], (heads, LANE)),
            ],
            axis=1,
        )
        got = shifted(packed, "seq", sign * distance)
        got_log = got[:, size].astype(F32) + got[:, size + LANE].astype(F32)
        return got_log, got[:, :size].astype(F32)

    got_log, got_state = send(total_log, flat, 1)
    x_log, x_state = got_log, got_state
    i_log = got_log + total_log
    i_state = jnp.exp(total_log)[:, None] * got_state + flat
    covered, window = 1, 2
    while covered < count - 1:
        r_log, r_state = send(i_log, i_state, window)
        x_state = jnp.exp(x_log)[:, None] * r_state + x_state
        x_log = x_log + r_log
        covered += window
        if covered < count - 1:
            i_state = jnp.exp(i_log)[:, None] * r_state + i_state
            i_log = i_log + r_log
            window *= 2
    return x_state.reshape(state.shape)


def group_layout(acc, delta, groups, per_group):
    rows = acc.shape[0]
    acc_g = jnp.transpose(acc.reshape(rows, groups, per_group), (1, 0, 2))
    delta_g = jnp.transpose(delta.reshape(rows, groups, per_group), (1, 0, 2))
    return acc_g, delta_g, jnp.transpose(acc_g, (0, 2, 1)), jnp.transpose(delta_g, (0, 2, 1))


def block_states(state_c, values_t, acc_t, delta_t, forward, interpret=False):
    rows = values_t.shape[1]
    groups, per_group, _ = acc_t.shape
    blocks = rows // Q
    width_g = per_group * P_SIZE

    def kernel(b_ref, xt_ref, at_ref, dt_ref, s_ref):
        b_blk = b_ref[...]
        for j in range(per_group):
            a_row = at_ref[0, j : j + 1, :]
            d_row = dt_ref[0, j : j + 1, :]
            a_end = a_row[:, Q - 1 : Q] if forward else a_row[:, 0:1]
            xt_j = xt_ref[j * P_SIZE : (j + 1) * P_SIZE, :]
            tx = (jnp.exp(a_end - a_row) * d_row) * xt_j.astype(F32)
            t_hi = tx.astype(BF16)
            t_lo = (tx - t_hi.astype(F32)).astype(BF16)
            s_ref[0, j] = jnp.dot(t_hi, b_blk, preferred_element_type=F32) + jnp.dot(
                t_lo, b_blk, preferred_element_type=F32
            )

    return pl.pallas_call(
        kernel,
        grid=(blocks, groups),
        in_specs=[
            pl.BlockSpec((Q, N), lambda b, g: (b, 2 * g)),
            pl.BlockSpec((width_g, Q), lambda b, g: (g, b)),
            pl.BlockSpec((1, per_group, Q), lambda b, g: (g, 0, b)),
            pl.BlockSpec((1, per_group, Q), lambda b, g: (g, 0, b)),
        ],
        out_specs=pl.BlockSpec((1, per_group, P_SIZE, N), lambda b, g: (b, g, 0, 0)),
        out_shape=jax.ShapeDtypeStruct((blocks, groups * per_group, P_SIZE, N), F32),
        interpret=interpret,
    )(state_c, values_t, acc_t, delta_t)


def block_intra(state_c, values_t, acc_g, acc_t, delta_t, forward, interpret=False):
    rows = values_t.shape[1]
    groups, _, per_group = acc_g.shape
    blocks = rows // Q
    width_g = per_group * P_SIZE

    def kernel(c_ref, b_ref, xt_ref, a_ref, at_ref, dt_ref, y_ref):
        inner = lax.dot_general(
            c_ref[...], b_ref[...], (((1,), (1,)), ((), ())), preferred_element_type=F32
        )
        row = lax.broadcasted_iota(jnp.int32, (Q, Q), 0)
        col = lax.broadcasted_iota(jnp.int32, (Q, Q), 1)
        mask = row >= col if forward else row <= col
        for j in range(per_group):
            a_col = a_ref[0, :, j : j + 1]
            a_row = at_ref[0, j : j + 1, :]
            d_row = dt_ref[0, j : j + 1, :]
            differ = jnp.where(mask, a_col - a_row, 0.0)
            m = jnp.where(mask, jnp.exp(differ), 0.0) * d_row * inner
            xt_j = xt_ref[j * P_SIZE : (j + 1) * P_SIZE, :]
            y_ref[j * P_SIZE : (j + 1) * P_SIZE, :] = lax.dot_general(
                xt_j, m.astype(BF16), (((1,), (1,)), ((), ())), preferred_element_type=F32
            )

    return pl.pallas_call(
        kernel,
        grid=(blocks, groups),
        in_specs=[
            pl.BlockSpec((Q, N), lambda b, g: (b, 2 * g + 1)),
            pl.BlockSpec((Q, N), lambda b, g: (b, 2 * g)),
            pl.BlockSpec((width_g, Q), lambda b, g: (g, b)),
            pl.BlockSpec((1, Q, per_group), lambda b, g: (g, b, 0)),
            pl.BlockSpec((1, per_group, Q), lambda b, g: (g, 0, b)),
            pl.BlockSpec((1, per_group, Q), lambda b, g: (g, 0, b)),
        ],
        out_specs=pl.BlockSpec((width_g, Q), lambda b, g: (g, b)),
        out_shape=jax.ShapeDtypeStruct((groups * width_g, rows), F32),
        interpret=interpret,
    )(state_c, state_c, values_t, acc_g, acc_t, delta_t)


def block_finish(intra_t, state_c, values_t, acc_t, start, skip_col, interpret=False):
    rows = values_t.shape[1]
    groups, per_group, _ = acc_t.shape
    blocks = rows // Q
    width_g = per_group * P_SIZE

    def kernel(y_ref, c_ref, xt_ref, at_ref, s_ref, k_ref, o_ref):
        dims = (((1,), (1,)), ((), ()))
        for b in range(blocks):
            cols = slice(b * Q, (b + 1) * Q)
            c_blk = c_ref[cols, :]
            for j in range(per_group):
                lo_row, hi_row = j * P_SIZE, (j + 1) * P_SIZE
                s_j = s_ref[b, j]
                s_hi = s_j.astype(BF16)
                s_lo = (s_j - s_hi.astype(F32)).astype(BF16)
                inter = lax.dot_general(
                    s_hi, c_blk, dims, preferred_element_type=F32
                ) + lax.dot_general(s_lo, c_blk, dims, preferred_element_type=F32)
                inter = inter * jnp.exp(at_ref[0, j : j + 1, cols])
                o_ref[lo_row:hi_row, cols] = (
                    y_ref[lo_row:hi_row, cols]
                    + inter
                    + k_ref[lo_row:hi_row, :] * xt_ref[lo_row:hi_row, cols].astype(F32)
                )

    return pl.pallas_call(
        kernel,
        grid=(groups,),
        in_specs=[
            pl.BlockSpec((width_g, rows), lambda g: (g, 0)),
            pl.BlockSpec((rows, N), lambda g: (0, 2 * g + 1)),
            pl.BlockSpec((width_g, rows), lambda g: (g, 0)),
            pl.BlockSpec((1, per_group, rows), lambda g: (g, 0, 0)),
            pl.BlockSpec((blocks, per_group, P_SIZE, N), lambda g: (0, g, 0, 0)),
            pl.BlockSpec((width_g, 1), lambda g: (g, 0)),
        ],
        out_specs=pl.BlockSpec((width_g, rows), lambda g: (g, 0)),
        out_shape=jax.ShapeDtypeStruct((groups * width_g, rows), F32),
        interpret=interpret,
    )(intra_t, state_c, values_t, acc_t, start, skip_col)


def conv_silu(padded, kernel, offset, count, forward):
    taps = kernel.shape[0]
    total = jnp.zeros((count, padded.shape[1]), F32) + offset[None, :]
    for index in range(taps):
        start = index if forward else taps - 1 - index
        total = total + kernel[index][None, :] * padded[start : start + count].astype(F32)
    return jax.nn.silu(total).astype(BF16)


def on_device(
    hidden,
    bases,
    w_gate,
    w_values,
    w_state_io,
    w_step,
    conv_values,
    conv_values_bias,
    conv_state_io,
    conv_state_bias,
    step_bias,
    decay_rate,
    skip_gain,
    norm_gain,
    w_out,
):
    rows, width = hidden.shape
    heads = w_step.shape[1]
    groups = w_state_io.shape[1] // (2 * N)
    per_group = heads // groups
    blocks = rows // Q
    known = jnp.where(bases == 4, 0.0, 1.0).astype(F32)

    lane_idx = jnp.arange(LANE)
    anti = (lane_idx[:, None] + lane_idx[None, :] == LANE - 1).astype(BF16)

    def lane_reverse(block):
        count = block.shape[0]
        flipped = jnp.einsum(
            "rki,ij->rkj", block.reshape(count, width // LANE, LANE), anti, preferred_element_type=F32
        ).astype(BF16)
        return jnp.flip(flipped, 1).reshape(count, width)

    hidden_rev = lane_reverse(hidden)

    taps = K - 1
    known_cols = jnp.broadcast_to(known.astype(BF16)[:, None], (rows, LANE))
    edge_first = jnp.concatenate([hidden[:taps], known_cols[:taps]], axis=1)
    edge_last = jnp.concatenate([hidden[rows - taps :], known_cols[rows - taps :]], axis=1)
    from_prev = shifted(edge_last, "seq", 1)
    from_next = shifted(edge_first, "seq", -1)
    rim_rows = jnp.concatenate([from_prev[:, :width], lane_reverse(from_next[:, :width])], axis=0)
    rim_known = jnp.concatenate([from_prev[:, width], from_next[:, width]], axis=0).astype(F32)
    rim_values = (
        jnp.dot(rim_rows, w_values, preferred_element_type=F32) * rim_known[:, None]
    ).astype(BF16)
    rim_state = jnp.dot(rim_rows, w_state_io, preferred_element_type=F32).astype(BF16)

    def project(source):
        gate_in = jnp.dot(source, w_gate, preferred_element_type=F32).astype(BF16)
        values = (jnp.dot(source, w_values, preferred_element_type=F32) * known[:, None]).astype(BF16)
        state_io = jnp.dot(source, w_state_io, preferred_element_type=F32).astype(BF16)
        step_raw = jnp.dot(source, w_step, preferred_element_type=F32).astype(BF16)
        return gate_in, values, state_io, step_raw

    t_idx = jnp.arange(Q)

    def local_scan(pieces, forward):
        gate_in, values, state_io, step_raw = pieces
        sign = 1 if forward else -1
        if forward:
            pv = jnp.concatenate([rim_values[:taps], values], axis=0)
            ps = jnp.concatenate([rim_state[:taps], state_io], axis=0)
        else:
            pv = jnp.concatenate([values, rim_values[taps:]], axis=0)
            ps = jnp.concatenate([state_io, rim_state[taps:]], axis=0)
        values_c = conv_silu(pv, conv_values, conv_values_bias, rows, forward)
        state_c = conv_silu(ps, conv_state_io, conv_state_bias, rows, forward)
        delta = jax.nn.softplus(step_raw.astype(F32) + step_bias[None, :])
        logdec = -decay_rate[None, :] * delta

        sb = state_c.reshape(blocks, Q, groups, 2, N)
        c_vec = sb[:, :, :, 1, :]
        ld = logdec.reshape(blocks, Q, heads)
        if forward:
            mask = t_idx[:, None] >= t_idx[None, :]
        else:
            mask = t_idx[:, None] <= t_idx[None, :]
        acc = jnp.einsum("ts,bsh->bth", mask.astype(F32), ld, precision=HIGHEST)
        blk = jnp.sum(ld, axis=1)
        acc_g, delta_g, acc_t, delta_t = group_layout(acc.reshape(rows, heads), delta, groups, per_group)
        values_t = values_c.T
        states = block_states(state_c, values_t, acc_t, delta_t, forward)

        order = list(range(blocks)) if forward else list(range(blocks - 1, -1, -1))
        block_decay = jnp.exp(blk)
        running = jnp.zeros((heads, P_SIZE, N), F32)
        local_start = [None] * blocks
        entering = [None] * blocks
        log_before = jnp.zeros((heads,), F32)
        for index in order:
            local_start[index] = running
            entering[index] = jnp.exp(log_before)
            running = block_decay[index][:, None, None] * running + states[index]
            log_before = log_before + blk[index]
        total = log_before
        carried = exclusive_carry(total, running, sign)
        intra_t = block_intra(state_c, values_t, acc_g, acc_t, delta_t, forward)
        start = jnp.stack(
            [local_start[index] + entering[index][:, None, None] * carried for index in range(blocks)]
        )
        skip_col = jnp.repeat(skip_gain, P_SIZE)[:, None]
        outputs = block_finish(intra_t, state_c, values_t, acc_t, start, skip_col).T
        gated = outputs.reshape(rows, heads * P_SIZE) * jax.nn.silu(gate_in.astype(F32))
        grouped = gated.reshape(rows, groups, per_group * P_SIZE)
        scale = lax.rsqrt(jnp.mean(grouped * grouped, axis=-1, keepdims=True) + EPSILON)
        return ((grouped * scale).reshape(rows, heads * P_SIZE) * norm_gain[None, :]).astype(BF16)

    forward_out = local_scan(project(hidden), True)
    backward_out = local_scan(project(hidden_rev), False)
    combined = (forward_out.astype(F32) + backward_out.astype(F32)).astype(BF16)
    chan = lax.axis_size("chan")
    partial = jnp.dot(combined, w_out, preferred_element_type=F32).astype(BF16)
    partial = jnp.transpose(partial.reshape(rows, chan, width // chan), (1, 0, 2))
    summed = lax.psum_scatter(partial, "chan", scatter_dimension=0, tiled=True)
    return summed.reshape(rows, width // chan)


def solution(mesh):
    return jax.shard_map(
        on_device,
        mesh=mesh,
        in_specs=(
            P(("groups", "seq"), None),
            P(("groups", "seq")),
            P(None, "chan"),
            P(None, "chan"),
            P(None, "chan"),
            P(None, "chan"),
            P(None, "chan"),
            P("chan"),
            P(None, "chan"),
            P("chan"),
            P("chan"),
            P("chan"),
            P("chan"),
            P("chan"),
            P("chan", None),
        ),
        out_specs=P(("groups", "seq"), "chan"),
        check_vma=False,
    )
```

```python
import jax
import jax.numpy as jnp
from jax import lax
from jax.sharding import PartitionSpec as P
from jax.experimental import pallas as pl

P_SIZE = 64
N = 128
K = 4
Q = 128
LANE = 128


EPSILON = 1e-05
HIGHEST = lax.Precision.HIGHEST
F32 = jnp.float32
BF16 = jnp.bfloat16


def shifted(value, axis, steps):
    count = lax.axis_size(axis)
    pairs = [(source, source + steps) for source in range(count) if 0 <= source + steps < count]
    if not pairs:
        return jax.tree.map(jnp.zeros_like, value)
    return lax.ppermute(value, axis, pairs)


def exclusive_carry(total_log, state, sign):
    count = lax.axis_size("seq")
    heads = state.shape[0]
    flat = state.reshape(heads, -1)
    size = flat.shape[1]

    def send(log, st, distance):
        log_hi = log.astype(BF16)
        log_lo = (log - log_hi.astype(F32)).astype(BF16)
        packed = jnp.concatenate(
            [
                st.astype(BF16),
                jnp.broadcast_to(log_hi[:, None], (heads, LANE)),
                jnp.broadcast_to(log_lo[:, None], (heads, LANE)),
            ],
            axis=1,
        )
        got = shifted(packed, "seq", sign * distance)
        got_log = got[:, size].astype(F32) + got[:, size + LANE].astype(F32)
        return got_log, got[:, :size].astype(F32)

    got_log, got_state = send(total_log, flat, 1)
    x_log, x_state = got_log, got_state
    i_log = got_log + total_log
    i_state = jnp.exp(total_log)[:, None] * got_state + flat
    covered, window = 1, 2
    while covered < count - 1:
        r_log, r_state = send(i_log, i_state, window)
        x_state = jnp.exp(x_log)[:, None] * r_state + x_state
        x_log = x_log + r_log
        covered += window
        if covered < count - 1:
            i_state = jnp.exp(i_log)[:, None] * r_state + i_state
            i_log = i_log + r_log
            window *= 2
    return x_state.reshape(state.shape)


def group_layout(acc, delta, groups, per_group):
    rows = acc.shape[0]
    acc_g = jnp.transpose(acc.reshape(rows, groups, per_group), (1, 0, 2))
    delta_g = jnp.transpose(delta.reshape(rows, groups, per_group), (1, 0, 2))
    return acc_g, delta_g, jnp.transpose(acc_g, (0, 2, 1)), jnp.transpose(delta_g, (0, 2, 1))


def block_states(state_c, values_t, acc_t, delta_t, forward, interpret=False):
    rows = values_t.shape[1]
    groups, per_group, _ = acc_t.shape
    blocks = rows // Q
    width_g = per_group * P_SIZE

    def kernel(b_ref, xt_ref, at_ref, dt_ref, s_ref):
      for blk in range(blocks):
        cols = slice(blk * Q, (blk + 1) * Q)
        b_blk = b_ref[cols, :]
        for j in range(per_group):
            a_row = at_ref[0, j : j + 1, cols]
            d_row = dt_ref[0, j : j + 1, cols]
            a_end = a_row[:, Q - 1 : Q] if forward else a_row[:, 0:1]
            xt_j = xt_ref[j * P_SIZE : (j + 1) * P_SIZE, cols]
            tx = (jnp.exp(a_end - a_row) * d_row) * xt_j.astype(F32)
            t_hi = tx.astype(BF16)
            t_lo = (tx - t_hi.astype(F32)).astype(BF16)
            s_ref[blk, j] = jnp.dot(t_hi, b_blk, preferred_element_type=F32) + jnp.dot(
                t_lo, b_blk, preferred_element_type=F32
            )

    return pl.pallas_call(
        kernel,
        grid=(groups,),
        in_specs=[
            pl.BlockSpec((rows, N), lambda g: (0, 2 * g)),
            pl.BlockSpec((width_g, rows), lambda g: (g, 0)),
            pl.BlockSpec((1, per_group, rows), lambda g: (g, 0, 0)),
            pl.BlockSpec((1, per_group, rows), lambda g: (g, 0, 0)),
        ],
        out_specs=pl.BlockSpec((blocks, per_group, P_SIZE, N), lambda g: (0, g, 0, 0)),
        out_shape=jax.ShapeDtypeStruct((blocks, groups * per_group, P_SIZE, N), F32),
        interpret=interpret,
    )(state_c, values_t, acc_t, delta_t)


def block_intra(state_c, values_t, acc_g, acc_t, delta_t, forward, interpret=False):
    rows = values_t.shape[1]
    groups, _, per_group = acc_g.shape
    blocks = rows // Q
    width_g = per_group * P_SIZE

    def kernel(c_ref, b_ref, xt_ref, a_ref, at_ref, dt_ref, y_ref):
        inner = lax.dot_general(
            c_ref[...], b_ref[...], (((1,), (1,)), ((), ())), preferred_element_type=F32
        )
        row = lax.broadcasted_iota(jnp.int32, (Q, Q), 0)
        col = lax.broadcasted_iota(jnp.int32, (Q, Q), 1)
        mask = row >= col if forward else row <= col
        for j in range(per_group):
            a_col = a_ref[0, :, j : j + 1]
            a_row = at_ref[0, j : j + 1, :]
            d_row = dt_ref[0, j : j + 1, :]
            differ = jnp.where(mask, a_col - a_row, 0.0)
            m = jnp.where(mask, jnp.exp(differ), 0.0) * d_row * inner
            xt_j = xt_ref[j * P_SIZE : (j + 1) * P_SIZE, :]
            y_ref[j * P_SIZE : (j + 1) * P_SIZE, :] = lax.dot_general(
                xt_j, m.astype(BF16), (((1,), (1,)), ((), ())), preferred_element_type=F32
            )

    return pl.pallas_call(
        kernel,
        grid=(blocks, groups),
        in_specs=[
            pl.BlockSpec((Q, N), lambda b, g: (b, 2 * g + 1)),
            pl.BlockSpec((Q, N), lambda b, g: (b, 2 * g)),
            pl.BlockSpec((width_g, Q), lambda b, g: (g, b)),
            pl.BlockSpec((1, Q, per_group), lambda b, g: (g, b, 0)),
            pl.BlockSpec((1, per_group, Q), lambda b, g: (g, 0, b)),
            pl.BlockSpec((1, per_group, Q), lambda b, g: (g, 0, b)),
        ],
        out_specs=pl.BlockSpec((width_g, Q), lambda b, g: (g, b)),
        out_shape=jax.ShapeDtypeStruct((groups * width_g, rows), F32),
        interpret=interpret,
    )(state_c, state_c, values_t, acc_g, acc_t, delta_t)


def block_finish(intra_t, state_c, values_t, acc_t, start, skip_col, interpret=False):
    rows = values_t.shape[1]
    groups, per_group, _ = acc_t.shape
    blocks = rows // Q
    width_g = per_group * P_SIZE

    def kernel(y_ref, c_ref, xt_ref, at_ref, s_ref, k_ref, o_ref):
        dims = (((1,), (1,)), ((), ()))
        for b in range(blocks):
            cols = slice(b * Q, (b + 1) * Q)
            c_blk = c_ref[cols, :]
            for j in range(per_group):
                lo_row, hi_row = j * P_SIZE, (j + 1) * P_SIZE
                s_j = s_ref[b, j]
                s_hi = s_j.astype(BF16)
                s_lo = (s_j - s_hi.astype(F32)).astype(BF16)
                inter = lax.dot_general(
                    s_hi, c_blk, dims, preferred_element_type=F32
                ) + lax.dot_general(s_lo, c_blk, dims, preferred_element_type=F32)
                inter = inter * jnp.exp(at_ref[0, j : j + 1, cols])
                o_ref[lo_row:hi_row, cols] = (
                    y_ref[lo_row:hi_row, cols]
                    + inter
                    + k_ref[lo_row:hi_row, :] * xt_ref[lo_row:hi_row, cols].astype(F32)
                )

    return pl.pallas_call(
        kernel,
        grid=(groups,),
        in_specs=[
            pl.BlockSpec((width_g, rows), lambda g: (g, 0)),
            pl.BlockSpec((rows, N), lambda g: (0, 2 * g + 1)),
            pl.BlockSpec((width_g, rows), lambda g: (g, 0)),
            pl.BlockSpec((1, per_group, rows), lambda g: (g, 0, 0)),
            pl.BlockSpec((blocks, per_group, P_SIZE, N), lambda g: (0, g, 0, 0)),
            pl.BlockSpec((width_g, 1), lambda g: (g, 0)),
        ],
        out_specs=pl.BlockSpec((width_g, rows), lambda g: (g, 0)),
        out_shape=jax.ShapeDtypeStruct((groups * width_g, rows), F32),
        interpret=interpret,
    )(intra_t, state_c, values_t, acc_t, start, skip_col)


def conv_silu(padded, kernel, offset, count, forward):
    taps = kernel.shape[0]
    total = jnp.zeros((count, padded.shape[1]), F32) + offset[None, :]
    for index in range(taps):
        start = index if forward else taps - 1 - index
        total = total + kernel[index][None, :] * padded[start : start + count].astype(F32)
    return jax.nn.silu(total).astype(BF16)


def on_device(
    hidden,
    bases,
    w_gate,
    w_values,
    w_state_io,
    w_step,
    conv_values,
    conv_values_bias,
    conv_state_io,
    conv_state_bias,
    step_bias,
    decay_rate,
    skip_gain,
    norm_gain,
    w_out,
):
    rows, width = hidden.shape
    heads = w_step.shape[1]
    groups = w_state_io.shape[1] // (2 * N)
    per_group = heads // groups
    blocks = rows // Q
    known = jnp.where(bases == 4, 0.0, 1.0).astype(F32)

    lane_idx = jnp.arange(LANE)
    anti = (lane_idx[:, None] + lane_idx[None, :] == LANE - 1).astype(BF16)

    def lane_reverse(block):
        count = block.shape[0]
        flipped = jnp.einsum(
            "rki,ij->rkj", block.reshape(count, width // LANE, LANE), anti, preferred_element_type=F32
        ).astype(BF16)
        return jnp.flip(flipped, 1).reshape(count, width)

    hidden_rev = lane_reverse(hidden)

    taps = K - 1
    known_cols = jnp.broadcast_to(known.astype(BF16)[:, None], (rows, LANE))
    edge_first = jnp.concatenate([hidden[:taps], known_cols[:taps]], axis=1)
    edge_last = jnp.concatenate([hidden[rows - taps :], known_cols[rows - taps :]], axis=1)
    from_prev = shifted(edge_last, "seq", 1)
    from_next = shifted(edge_first, "seq", -1)
    rim_rows = jnp.concatenate([from_prev[:, :width], lane_reverse(from_next[:, :width])], axis=0)
    rim_known = jnp.concatenate([from_prev[:, width], from_next[:, width]], axis=0).astype(F32)
    rim_values = (
        jnp.dot(rim_rows, w_values, preferred_element_type=F32) * rim_known[:, None]
    ).astype(BF16)
    rim_state = jnp.dot(rim_rows, w_state_io, preferred_element_type=F32).astype(BF16)

    def project(source):
        gate_in = jnp.dot(source, w_gate, preferred_element_type=F32).astype(BF16)
        values = (jnp.dot(source, w_values, preferred_element_type=F32) * known[:, None]).astype(BF16)
        state_io = jnp.dot(source, w_state_io, preferred_element_type=F32).astype(BF16)
        step_raw = jnp.dot(source, w_step, preferred_element_type=F32).astype(BF16)
        return gate_in, values, state_io, step_raw

    t_idx = jnp.arange(Q)

    def local_scan(pieces, forward):
        gate_in, values, state_io, step_raw = pieces
        sign = 1 if forward else -1
        if forward:
            pv = jnp.concatenate([rim_values[:taps], values], axis=0)
            ps = jnp.concatenate([rim_state[:taps], state_io], axis=0)
        else:
            pv = jnp.concatenate([values, rim_values[taps:]], axis=0)
            ps = jnp.concatenate([state_io, rim_state[taps:]], axis=0)
        values_c = conv_silu(pv, conv_values, conv_values_bias, rows, forward)
        state_c = conv_silu(ps, conv_state_io, conv_state_bias, rows, forward)
        delta = jax.nn.softplus(step_raw.astype(F32) + step_bias[None, :])
        logdec = -decay_rate[None, :] * delta

        sb = state_c.reshape(blocks, Q, groups, 2, N)
        c_vec = sb[:, :, :, 1, :]
        ld = logdec.reshape(blocks, Q, heads)
        if forward:
            mask = t_idx[:, None] >= t_idx[None, :]
        else:
            mask = t_idx[:, None] <= t_idx[None, :]
        acc = jnp.einsum("ts,bsh->bth", mask.astype(F32), ld, precision=HIGHEST)
        blk = jnp.sum(ld, axis=1)
        acc_g, delta_g, acc_t, delta_t = group_layout(acc.reshape(rows, heads), delta, groups, per_group)
        values_t = values_c.T
        states = block_states(state_c, values_t, acc_t, delta_t, forward)

        order = list(range(blocks)) if forward else list(range(blocks - 1, -1, -1))
        block_decay = jnp.exp(blk)
        running = jnp.zeros((heads, P_SIZE, N), F32)
        local_start = [None] * blocks
        entering = [None] * blocks
        log_before = jnp.zeros((heads,), F32)
        for index in order:
            local_start[index] = running
            entering[index] = jnp.exp(log_before)
            running = block_decay[index][:, None, None] * running + states[index]
            log_before = log_before + blk[index]
        total = log_before
        carried = exclusive_carry(total, running, sign)
        intra_t = block_intra(state_c, values_t, acc_g, acc_t, delta_t, forward)
        start = jnp.stack(
            [local_start[index] + entering[index][:, None, None] * carried for index in range(blocks)]
        )
        skip_col = jnp.repeat(skip_gain, P_SIZE)[:, None]
        outputs = block_finish(intra_t, state_c, values_t, acc_t, start, skip_col).T
        gated = outputs.reshape(rows, heads * P_SIZE) * jax.nn.silu(gate_in.astype(F32))
        grouped = gated.reshape(rows, groups, per_group * P_SIZE)
        scale = lax.rsqrt(jnp.mean(grouped * grouped, axis=-1, keepdims=True) + EPSILON)
        return ((grouped * scale).reshape(rows, heads * P_SIZE) * norm_gain[None, :]).astype(BF16)

    forward_out = local_scan(project(hidden), True)
    backward_out = local_scan(project(hidden_rev), False)
    combined = (forward_out.astype(F32) + backward_out.astype(F32)).astype(BF16)
    chan = lax.axis_size("chan")
    partial = jnp.dot(combined, w_out, preferred_element_type=F32).astype(BF16)
    partial = jnp.transpose(partial.reshape(rows, chan, width // chan), (1, 0, 2))
    summed = lax.psum_scatter(partial, "chan", scatter_dimension=0, tiled=True)
    return summed.reshape(rows, width // chan)


def solution(mesh):
    return jax.shard_map(
        on_device,
        mesh=mesh,
        in_specs=(
            P(("groups", "seq"), None),
            P(("groups", "seq")),
            P(None, "chan"),
            P(None, "chan"),
            P(None, "chan"),
            P(None, "chan"),
            P(None, "chan"),
            P("chan"),
            P(None, "chan"),
            P("chan"),
            P("chan"),
            P("chan"),
            P("chan"),
            P("chan"),
            P("chan", None),
        ),
        out_specs=P(("groups", "seq"), "chan"),
        check_vma=False,
    )
```

```python
import jax
import jax.numpy as jnp
from jax import lax
from jax.sharding import PartitionSpec as P
from jax.experimental import pallas as pl

P_SIZE = 64
N = 128
K = 4
Q = 128
LANE = 128


EPSILON = 1e-05
HIGHEST = lax.Precision.HIGHEST
F32 = jnp.float32
BF16 = jnp.bfloat16


def shifted(value, axis, steps):
    count = lax.axis_size(axis)
    pairs = [(source, source + steps) for source in range(count) if 0 <= source + steps < count]
    if not pairs:
        return jax.tree.map(jnp.zeros_like, value)
    return lax.ppermute(value, axis, pairs)


def exclusive_carry(total_log, state, sign):
    count = lax.axis_size("seq")
    heads = state.shape[0]
    flat = state.reshape(heads, -1)
    size = flat.shape[1]

    def send(log, st, distance):
        log_hi = log.astype(BF16)
        log_lo = (log - log_hi.astype(F32)).astype(BF16)
        packed = jnp.concatenate(
            [
                st.astype(BF16),
                jnp.broadcast_to(log_hi[:, None], (heads, LANE)),
                jnp.broadcast_to(log_lo[:, None], (heads, LANE)),
            ],
            axis=1,
        )
        got = shifted(packed, "seq", sign * distance)
        got_log = got[:, size].astype(F32) + got[:, size + LANE].astype(F32)
        return got_log, got[:, :size].astype(F32)

    got_log, got_state = send(total_log, flat, 1)
    x_log, x_state = got_log, got_state
    i_log = got_log + total_log
    i_state = jnp.exp(total_log)[:, None] * got_state + flat
    covered, window = 1, 2
    while covered < count - 1:
        r_log, r_state = send(i_log, i_state, window)
        x_state = jnp.exp(x_log)[:, None] * r_state + x_state
        x_log = x_log + r_log
        covered += window
        if covered < count - 1:
            i_state = jnp.exp(i_log)[:, None] * r_state + i_state
            i_log = i_log + r_log
            window *= 2
    return x_state.reshape(state.shape)


def group_layout(acc, delta, groups, per_group):
    rows = acc.shape[0]
    acc_g = jnp.transpose(acc.reshape(rows, groups, per_group), (1, 0, 2))
    delta_g = jnp.transpose(delta.reshape(rows, groups, per_group), (1, 0, 2))
    return acc_g, delta_g, jnp.transpose(acc_g, (0, 2, 1)), jnp.transpose(delta_g, (0, 2, 1))


def block_states(state_c, values_t, acc_t, delta_t, forward, interpret=False):
    rows = values_t.shape[1]
    groups, per_group, _ = acc_t.shape
    blocks = rows // Q
    width_g = per_group * P_SIZE

    def kernel(b_ref, xt_ref, at_ref, dt_ref, s_ref):
      for blk in range(blocks):
        cols = slice(blk * Q, (blk + 1) * Q)
        b_blk = b_ref[cols, :]
        for j in range(per_group):
            a_row = at_ref[0, j : j + 1, cols]
            d_row = dt_ref[0, j : j + 1, cols]
            a_end = a_row[:, Q - 1 : Q] if forward else a_row[:, 0:1]
            xt_j = xt_ref[j * P_SIZE : (j + 1) * P_SIZE, cols]
            tx = (jnp.exp(a_end - a_row) * d_row) * xt_j.astype(F32)
            t_hi = tx.astype(BF16)
            t_lo = (tx - t_hi.astype(F32)).astype(BF16)
            s_ref[blk, j] = jnp.dot(t_hi, b_blk, preferred_element_type=F32) + jnp.dot(
                t_lo, b_blk, preferred_element_type=F32
            )

    return pl.pallas_call(
        kernel,
        grid=(groups,),
        in_specs=[
            pl.BlockSpec((rows, N), lambda g: (0, 2 * g)),
            pl.BlockSpec((width_g, rows), lambda g: (g, 0)),
            pl.BlockSpec((1, per_group, rows), lambda g: (g, 0, 0)),
            pl.BlockSpec((1, per_group, rows), lambda g: (g, 0, 0)),
        ],
        out_specs=pl.BlockSpec((blocks, per_group, P_SIZE, N), lambda g: (0, g, 0, 0)),
        out_shape=jax.ShapeDtypeStruct((blocks, groups * per_group, P_SIZE, N), F32),
        interpret=interpret,
    )(state_c, values_t, acc_t, delta_t)


def block_intra(state_c, values_t, acc_g, acc_t, delta_t, forward, interpret=False):
    rows = values_t.shape[1]
    groups, _, per_group = acc_g.shape
    blocks = rows // Q
    width_g = per_group * P_SIZE

    def kernel(c_ref, b_ref, xt_ref, a_ref, at_ref, dt_ref, y_ref):
        row = lax.broadcasted_iota(jnp.int32, (Q, Q), 0)
        col = lax.broadcasted_iota(jnp.int32, (Q, Q), 1)
        mask = row >= col if forward else row <= col
        for blk in range(blocks):
            cols = slice(blk * Q, (blk + 1) * Q)
            inner = lax.dot_general(
                c_ref[cols, :], b_ref[cols, :], (((1,), (1,)), ((), ())), preferred_element_type=F32
            )
            for j in range(per_group):
                a_col = a_ref[0, cols, j : j + 1]
                a_row = at_ref[0, j : j + 1, cols]
                d_row = dt_ref[0, j : j + 1, cols]
                differ = jnp.where(mask, a_col - a_row, 0.0)
                m = jnp.where(mask, jnp.exp(differ), 0.0) * d_row * inner
                xt_j = xt_ref[j * P_SIZE : (j + 1) * P_SIZE, cols]
                y_ref[j * P_SIZE : (j + 1) * P_SIZE, cols] = lax.dot_general(
                    xt_j, m.astype(BF16), (((1,), (1,)), ((), ())), preferred_element_type=F32
                )

    return pl.pallas_call(
        kernel,
        grid=(groups,),
        in_specs=[
            pl.BlockSpec((rows, N), lambda g: (0, 2 * g + 1)),
            pl.BlockSpec((rows, N), lambda g: (0, 2 * g)),
            pl.BlockSpec((width_g, rows), lambda g: (g, 0)),
            pl.BlockSpec((1, rows, per_group), lambda g: (g, 0, 0)),
            pl.BlockSpec((1, per_group, rows), lambda g: (g, 0, 0)),
            pl.BlockSpec((1, per_group, rows), lambda g: (g, 0, 0)),
        ],
        out_specs=pl.BlockSpec((width_g, rows), lambda g: (g, 0)),
        out_shape=jax.ShapeDtypeStruct((groups * width_g, rows), F32),
        interpret=interpret,
    )(state_c, state_c, values_t, acc_g, acc_t, delta_t)


def block_finish(intra_t, state_c, values_t, acc_t, start, skip_col, interpret=False):
    rows = values_t.shape[1]
    groups, per_group, _ = acc_t.shape
    blocks = rows // Q
    width_g = per_group * P_SIZE

    def kernel(y_ref, c_ref, xt_ref, at_ref, s_ref, k_ref, o_ref):
        dims = (((1,), (1,)), ((), ()))
        for b in range(blocks):
            cols = slice(b * Q, (b + 1) * Q)
            c_blk = c_ref[cols, :]
            for j in range(per_group):
                lo_row, hi_row = j * P_SIZE, (j + 1) * P_SIZE
                s_j = s_ref[b, j]
                s_hi = s_j.astype(BF16)
                s_lo = (s_j - s_hi.astype(F32)).astype(BF16)
                inter = lax.dot_general(
                    s_hi, c_blk, dims, preferred_element_type=F32
                ) + lax.dot_general(s_lo, c_blk, dims, preferred_element_type=F32)
                inter = inter * jnp.exp(at_ref[0, j : j + 1, cols])
                o_ref[lo_row:hi_row, cols] = (
                    y_ref[lo_row:hi_row, cols]
                    + inter
                    + k_ref[lo_row:hi_row, :] * xt_ref[lo_row:hi_row, cols].astype(F32)
                )

    return pl.pallas_call(
        kernel,
        grid=(groups,),
        in_specs=[
            pl.BlockSpec((width_g, rows), lambda g: (g, 0)),
            pl.BlockSpec((rows, N), lambda g: (0, 2 * g + 1)),
            pl.BlockSpec((width_g, rows), lambda g: (g, 0)),
            pl.BlockSpec((1, per_group, rows), lambda g: (g, 0, 0)),
            pl.BlockSpec((blocks, per_group, P_SIZE, N), lambda g: (0, g, 0, 0)),
            pl.BlockSpec((width_g, 1), lambda g: (g, 0)),
        ],
        out_specs=pl.BlockSpec((width_g, rows), lambda g: (g, 0)),
        out_shape=jax.ShapeDtypeStruct((groups * width_g, rows), F32),
        interpret=interpret,
    )(intra_t, state_c, values_t, acc_t, start, skip_col)


def conv_silu(padded, kernel, offset, count, forward):
    taps = kernel.shape[0]
    total = jnp.zeros((count, padded.shape[1]), F32) + offset[None, :]
    for index in range(taps):
        start = index if forward else taps - 1 - index
        total = total + kernel[index][None, :] * padded[start : start + count].astype(F32)
    return jax.nn.silu(total).astype(BF16)


def on_device(
    hidden,
    bases,
    w_gate,
    w_values,
    w_state_io,
    w_step,
    conv_values,
    conv_values_bias,
    conv_state_io,
    conv_state_bias,
    step_bias,
    decay_rate,
    skip_gain,
    norm_gain,
    w_out,
):
    rows, width = hidden.shape
    heads = w_step.shape[1]
    groups = w_state_io.shape[1] // (2 * N)
    per_group = heads // groups
    blocks = rows // Q
    known = jnp.where(bases == 4, 0.0, 1.0).astype(F32)

    lane_idx = jnp.arange(LANE)
    anti = (lane_idx[:, None] + lane_idx[None, :] == LANE - 1).astype(BF16)

    def lane_reverse(block):
        count = block.shape[0]
        flipped = jnp.einsum(
            "rki,ij->rkj", block.reshape(count, width // LANE, LANE), anti, preferred_element_type=F32
        ).astype(BF16)
        return jnp.flip(flipped, 1).reshape(count, width)

    hidden_rev = lane_reverse(hidden)

    taps = K - 1
    known_cols = jnp.broadcast_to(known.astype(BF16)[:, None], (rows, LANE))
    edge_first = jnp.concatenate([hidden[:taps], known_cols[:taps]], axis=1)
    edge_last = jnp.concatenate([hidden[rows - taps :], known_cols[rows - taps :]], axis=1)
    from_prev = shifted(edge_last, "seq", 1)
    from_next = shifted(edge_first, "seq", -1)
    rim_rows = jnp.concatenate([from_prev[:, :width], lane_reverse(from_next[:, :width])], axis=0)
    rim_known = jnp.concatenate([from_prev[:, width], from_next[:, width]], axis=0).astype(F32)
    rim_values = (
        jnp.dot(rim_rows, w_values, preferred_element_type=F32) * rim_known[:, None]
    ).astype(BF16)
    rim_state = jnp.dot(rim_rows, w_state_io, preferred_element_type=F32).astype(BF16)

    def project(source):
        gate_in = jnp.dot(source, w_gate, preferred_element_type=F32).astype(BF16)
        values = (jnp.dot(source, w_values, preferred_element_type=F32) * known[:, None]).astype(BF16)
        state_io = jnp.dot(source, w_state_io, preferred_element_type=F32).astype(BF16)
        step_raw = jnp.dot(source, w_step, preferred_element_type=F32).astype(BF16)
        return gate_in, values, state_io, step_raw

    t_idx = jnp.arange(Q)

    def local_scan(pieces, forward):
        gate_in, values, state_io, step_raw = pieces
        sign = 1 if forward else -1
        if forward:
            pv = jnp.concatenate([rim_values[:taps], values], axis=0)
            ps = jnp.concatenate([rim_state[:taps], state_io], axis=0)
        else:
            pv = jnp.concatenate([values, rim_values[taps:]], axis=0)
            ps = jnp.concatenate([state_io, rim_state[taps:]], axis=0)
        values_c = conv_silu(pv, conv_values, conv_values_bias, rows, forward)
        state_c = conv_silu(ps, conv_state_io, conv_state_bias, rows, forward)
        delta = jax.nn.softplus(step_raw.astype(F32) + step_bias[None, :])
        logdec = -decay_rate[None, :] * delta

        sb = state_c.reshape(blocks, Q, groups, 2, N)
        c_vec = sb[:, :, :, 1, :]
        ld = logdec.reshape(blocks, Q, heads)
        if forward:
            mask = t_idx[:, None] >= t_idx[None, :]
        else:
            mask = t_idx[:, None] <= t_idx[None, :]
        acc = jnp.einsum("ts,bsh->bth", mask.astype(F32), ld, precision=HIGHEST)
        blk = jnp.sum(ld, axis=1)
        acc_g, delta_g, acc_t, delta_t = group_layout(acc.reshape(rows, heads), delta, groups, per_group)
        values_t = values_c.T
        states = block_states(state_c, values_t, acc_t, delta_t, forward)

        order = list(range(blocks)) if forward else list(range(blocks - 1, -1, -1))
        block_decay = jnp.exp(blk)
        running = jnp.zeros((heads, P_SIZE, N), F32)
        local_start = [None] * blocks
        entering = [None] * blocks
        log_before = jnp.zeros((heads,), F32)
        for index in order:
            local_start[index] = running
            entering[index] = jnp.exp(log_before)
            running = block_decay[index][:, None, None] * running + states[index]
            log_before = log_before + blk[index]
        total = log_before
        carried = exclusive_carry(total, running, sign)
        intra_t = block_intra(state_c, values_t, acc_g, acc_t, delta_t, forward)
        start = jnp.stack(
            [local_start[index] + entering[index][:, None, None] * carried for index in range(blocks)]
        )
        skip_col = jnp.repeat(skip_gain, P_SIZE)[:, None]
        outputs = block_finish(intra_t, state_c, values_t, acc_t, start, skip_col).T
        gated = outputs.reshape(rows, heads * P_SIZE) * jax.nn.silu(gate_in.astype(F32))
        grouped = gated.reshape(rows, groups, per_group * P_SIZE)
        scale = lax.rsqrt(jnp.mean(grouped * grouped, axis=-1, keepdims=True) + EPSILON)
        return ((grouped * scale).reshape(rows, heads * P_SIZE) * norm_gain[None, :]).astype(BF16)

    forward_out = local_scan(project(hidden), True)
    backward_out = local_scan(project(hidden_rev), False)
    combined = (forward_out.astype(F32) + backward_out.astype(F32)).astype(BF16)
    chan = lax.axis_size("chan")
    partial = jnp.dot(combined, w_out, preferred_element_type=F32).astype(BF16)
    partial = jnp.transpose(partial.reshape(rows, chan, width // chan), (1, 0, 2))
    summed = lax.psum_scatter(partial, "chan", scatter_dimension=0, tiled=True)
    return summed.reshape(rows, width // chan)


def solution(mesh):
    return jax.shard_map(
        on_device,
        mesh=mesh,
        in_specs=(
            P(("groups", "seq"), None),
            P(("groups", "seq")),
            P(None, "chan"),
            P(None, "chan"),
            P(None, "chan"),
            P(None, "chan"),
            P(None, "chan"),
            P("chan"),
            P(None, "chan"),
            P("chan"),
            P("chan"),
            P("chan"),
            P("chan"),
            P("chan"),
            P("chan", None),
        ),
        out_specs=P(("groups", "seq"), "chan"),
        check_vma=False,
    )
```

```python
import jax
import jax.numpy as jnp
from jax import lax
from jax.sharding import PartitionSpec as P
from jax.experimental import pallas as pl

P_SIZE = 64
N = 128
K = 4
Q = 128
LANE = 128


EPSILON = 1e-05
HIGHEST = lax.Precision.HIGHEST
F32 = jnp.float32
BF16 = jnp.bfloat16


def shifted(value, axis, steps):
    count = lax.axis_size(axis)
    pairs = [(source, source + steps) for source in range(count) if 0 <= source + steps < count]
    if not pairs:
        return jax.tree.map(jnp.zeros_like, value)
    return lax.ppermute(value, axis, pairs)


def exclusive_carry(total_log, state, sign):
    count = lax.axis_size("seq")
    heads = state.shape[0]
    flat = state.reshape(heads, -1)
    size = flat.shape[1]

    def send(log, st, distance):
        log_hi = log.astype(BF16)
        log_lo = (log - log_hi.astype(F32)).astype(BF16)
        packed = jnp.concatenate(
            [
                st.astype(BF16),
                jnp.broadcast_to(log_hi[:, None], (heads, LANE)),
                jnp.broadcast_to(log_lo[:, None], (heads, LANE)),
            ],
            axis=1,
        )
        got = shifted(packed, "seq", sign * distance)
        got_log = got[:, size].astype(F32) + got[:, size + LANE].astype(F32)
        return got_log, got[:, :size].astype(F32)

    got_log, got_state = send(total_log, flat, 1)
    x_log, x_state = got_log, got_state
    i_log = got_log + total_log
    i_state = jnp.exp(total_log)[:, None] * got_state + flat
    covered, window = 1, 2
    while covered < count - 1:
        r_log, r_state = send(i_log, i_state, window)
        x_state = jnp.exp(x_log)[:, None] * r_state + x_state
        x_log = x_log + r_log
        covered += window
        if covered < count - 1:
            i_state = jnp.exp(i_log)[:, None] * r_state + i_state
            i_log = i_log + r_log
            window *= 2
    return x_state.reshape(state.shape)


def group_layout(acc, delta, groups, per_group):
    rows = acc.shape[0]
    acc_g = jnp.transpose(acc.reshape(rows, groups, per_group), (1, 0, 2))
    delta_g = jnp.transpose(delta.reshape(rows, groups, per_group), (1, 0, 2))
    return acc_g, delta_g, jnp.transpose(acc_g, (0, 2, 1)), jnp.transpose(delta_g, (0, 2, 1))


def block_states(state_c, values_t, acc_t, delta_t, forward, interpret=False):
    rows = values_t.shape[1]
    groups, per_group, _ = acc_t.shape
    blocks = rows // Q
    width_g = per_group * P_SIZE

    def kernel(b_ref, xt_ref, at_ref, dt_ref, s_ref):
      for blk in range(blocks):
        cols = slice(blk * Q, (blk + 1) * Q)
        b_blk = b_ref[cols, :]
        for j in range(per_group):
            a_row = at_ref[0, j : j + 1, cols]
            d_row = dt_ref[0, j : j + 1, cols]
            a_end = a_row[:, Q - 1 : Q] if forward else a_row[:, 0:1]
            xt_j = xt_ref[j * P_SIZE : (j + 1) * P_SIZE, cols]
            tx = (jnp.exp(a_end - a_row) * d_row) * xt_j.astype(F32)
            t_hi = tx.astype(BF16)
            t_lo = (tx - t_hi.astype(F32)).astype(BF16)
            s_ref[blk, j] = jnp.dot(t_hi, b_blk, preferred_element_type=F32) + jnp.dot(
                t_lo, b_blk, preferred_element_type=F32
            )

    return pl.pallas_call(
        kernel,
        grid=(groups,),
        in_specs=[
            pl.BlockSpec((rows, N), lambda g: (0, 2 * g)),
            pl.BlockSpec((width_g, rows), lambda g: (g, 0)),
            pl.BlockSpec((1, per_group, rows), lambda g: (g, 0, 0)),
            pl.BlockSpec((1, per_group, rows), lambda g: (g, 0, 0)),
        ],
        out_specs=pl.BlockSpec((blocks, per_group, P_SIZE, N), lambda g: (0, g, 0, 0)),
        out_shape=jax.ShapeDtypeStruct((blocks, groups * per_group, P_SIZE, N), F32),
        interpret=interpret,
    )(state_c, values_t, acc_t, delta_t)


def block_intra(state_c, values_t, acc_g, acc_t, delta_t, forward, interpret=False):
    rows = values_t.shape[1]
    groups, _, per_group = acc_g.shape
    blocks = rows // Q
    width_g = per_group * P_SIZE

    def kernel(c_ref, b_ref, xt_ref, a_ref, at_ref, dt_ref, y_ref):
        row = lax.broadcasted_iota(jnp.int32, (Q, Q), 0)
        col = lax.broadcasted_iota(jnp.int32, (Q, Q), 1)
        mask = row >= col if forward else row <= col
        for blk in range(blocks):
            cols = slice(blk * Q, (blk + 1) * Q)
            inner = lax.dot_general(
                c_ref[cols, :], b_ref[cols, :], (((1,), (1,)), ((), ())), preferred_element_type=F32
            )
            for j in range(per_group):
                a_col = a_ref[0, cols, j : j + 1]
                a_row = at_ref[0, j : j + 1, cols]
                d_row = dt_ref[0, j : j + 1, cols]
                differ = jnp.where(mask, a_col - a_row, 0.0)
                m = jnp.where(mask, jnp.exp(differ), 0.0) * d_row * inner
                xt_j = xt_ref[j * P_SIZE : (j + 1) * P_SIZE, cols]
                y_ref[j * P_SIZE : (j + 1) * P_SIZE, cols] = lax.dot_general(
                    xt_j, m.astype(BF16), (((1,), (1,)), ((), ())), preferred_element_type=F32
                )

    return pl.pallas_call(
        kernel,
        grid=(groups,),
        in_specs=[
            pl.BlockSpec((rows, N), lambda g: (0, 2 * g + 1)),
            pl.BlockSpec((rows, N), lambda g: (0, 2 * g)),
            pl.BlockSpec((width_g, rows), lambda g: (g, 0)),
            pl.BlockSpec((1, rows, per_group), lambda g: (g, 0, 0)),
            pl.BlockSpec((1, per_group, rows), lambda g: (g, 0, 0)),
            pl.BlockSpec((1, per_group, rows), lambda g: (g, 0, 0)),
        ],
        out_specs=pl.BlockSpec((width_g, rows), lambda g: (g, 0)),
        out_shape=jax.ShapeDtypeStruct((groups * width_g, rows), F32),
        interpret=interpret,
    )(state_c, state_c, values_t, acc_g, acc_t, delta_t)


def block_finish(intra_t, state_c, values_t, acc_t, start, skip_col, interpret=False):
    rows = values_t.shape[1]
    groups, per_group, _ = acc_t.shape
    blocks = rows // Q
    width_g = per_group * P_SIZE

    def kernel(y_ref, c_ref, xt_ref, at_ref, s_ref, k_ref, o_ref):
        dims = (((1,), (1,)), ((), ()))
        for b in range(blocks):
            cols = slice(b * Q, (b + 1) * Q)
            c_blk = c_ref[cols, :]
            for j in range(per_group):
                lo_row, hi_row = j * P_SIZE, (j + 1) * P_SIZE
                inter = lax.dot_general(
                    s_ref[b, j].astype(BF16), c_blk, dims, preferred_element_type=F32
                )
                inter = inter * jnp.exp(at_ref[0, j : j + 1, cols])
                o_ref[lo_row:hi_row, cols] = (
                    y_ref[lo_row:hi_row, cols]
                    + inter
                    + k_ref[lo_row:hi_row, :] * xt_ref[lo_row:hi_row, cols].astype(F32)
                )

    return pl.pallas_call(
        kernel,
        grid=(groups,),
        in_specs=[
            pl.BlockSpec((width_g, rows), lambda g: (g, 0)),
            pl.BlockSpec((rows, N), lambda g: (0, 2 * g + 1)),
            pl.BlockSpec((width_g, rows), lambda g: (g, 0)),
            pl.BlockSpec((1, per_group, rows), lambda g: (g, 0, 0)),
            pl.BlockSpec((blocks, per_group, P_SIZE, N), lambda g: (0, g, 0, 0)),
            pl.BlockSpec((width_g, 1), lambda g: (g, 0)),
        ],
        out_specs=pl.BlockSpec((width_g, rows), lambda g: (g, 0)),
        out_shape=jax.ShapeDtypeStruct((groups * width_g, rows), F32),
        interpret=interpret,
    )(intra_t, state_c, values_t, acc_t, start, skip_col)


def conv_silu(padded, kernel, offset, count, forward):
    taps = kernel.shape[0]
    total = jnp.zeros((count, padded.shape[1]), F32) + offset[None, :]
    for index in range(taps):
        start = index if forward else taps - 1 - index
        total = total + kernel[index][None, :] * padded[start : start + count].astype(F32)
    return jax.nn.silu(total).astype(BF16)


def on_device(
    hidden,
    bases,
    w_gate,
    w_values,
    w_state_io,
    w_step,
    conv_values,
    conv_values_bias,
    conv_state_io,
    conv_state_bias,
    step_bias,
    decay_rate,
    skip_gain,
    norm_gain,
    w_out,
):
    rows, width = hidden.shape
    heads = w_step.shape[1]
    groups = w_state_io.shape[1] // (2 * N)
    per_group = heads // groups
    blocks = rows // Q
    known = jnp.where(bases == 4, 0.0, 1.0).astype(F32)

    lane_idx = jnp.arange(LANE)
    anti = (lane_idx[:, None] + lane_idx[None, :] == LANE - 1).astype(BF16)

    def lane_reverse(block):
        count = block.shape[0]
        flipped = jnp.einsum(
            "rki,ij->rkj", block.reshape(count, width // LANE, LANE), anti, preferred_element_type=F32
        ).astype(BF16)
        return jnp.flip(flipped, 1).reshape(count, width)

    hidden_rev = lane_reverse(hidden)

    taps = K - 1
    known_cols = jnp.broadcast_to(known.astype(BF16)[:, None], (rows, LANE))
    edge_first = jnp.concatenate([hidden[:taps], known_cols[:taps]], axis=1)
    edge_last = jnp.concatenate([hidden[rows - taps :], known_cols[rows - taps :]], axis=1)
    from_prev = shifted(edge_last, "seq", 1)
    from_next = shifted(edge_first, "seq", -1)
    rim_rows = jnp.concatenate([from_prev[:, :width], lane_reverse(from_next[:, :width])], axis=0)
    rim_known = jnp.concatenate([from_prev[:, width], from_next[:, width]], axis=0).astype(F32)
    rim_values = (
        jnp.dot(rim_rows, w_values, preferred_element_type=F32) * rim_known[:, None]
    ).astype(BF16)
    rim_state = jnp.dot(rim_rows, w_state_io, preferred_element_type=F32).astype(BF16)

    def project(source):
        gate_in = jnp.dot(source, w_gate, preferred_element_type=F32).astype(BF16)
        values = (jnp.dot(source, w_values, preferred_element_type=F32) * known[:, None]).astype(BF16)
        state_io = jnp.dot(source, w_state_io, preferred_element_type=F32).astype(BF16)
        step_raw = jnp.dot(source, w_step, preferred_element_type=F32).astype(BF16)
        return gate_in, values, state_io, step_raw

    t_idx = jnp.arange(Q)

    def local_scan(pieces, forward):
        gate_in, values, state_io, step_raw = pieces
        sign = 1 if forward else -1
        if forward:
            pv = jnp.concatenate([rim_values[:taps], values], axis=0)
            ps = jnp.concatenate([rim_state[:taps], state_io], axis=0)
        else:
            pv = jnp.concatenate([values, rim_values[taps:]], axis=0)
            ps = jnp.concatenate([state_io, rim_state[taps:]], axis=0)
        values_c = conv_silu(pv, conv_values, conv_values_bias, rows, forward)
        state_c = conv_silu(ps, conv_state_io, conv_state_bias, rows, forward)
        delta = jax.nn.softplus(step_raw.astype(F32) + step_bias[None, :])
        logdec = -decay_rate[None, :] * delta

        sb = state_c.reshape(blocks, Q, groups, 2, N)
        c_vec = sb[:, :, :, 1, :]
        ld = logdec.reshape(blocks, Q, heads)
        if forward:
            mask = t_idx[:, None] >= t_idx[None, :]
        else:
            mask = t_idx[:, None] <= t_idx[None, :]
        acc = jnp.einsum("ts,bsh->bth", mask.astype(F32), ld, precision=HIGHEST)
        blk = jnp.sum(ld, axis=1)
        acc_g, delta_g, acc_t, delta_t = group_layout(acc.reshape(rows, heads), delta, groups, per_group)
        values_t = values_c.T
        states = block_states(state_c, values_t, acc_t, delta_t, forward)

        order = list(range(blocks)) if forward else list(range(blocks - 1, -1, -1))
        block_decay = jnp.exp(blk)
        running = jnp.zeros((heads, P_SIZE, N), F32)
        local_start = [None] * blocks
        entering = [None] * blocks
        log_before = jnp.zeros((heads,), F32)
        for index in order:
            local_start[index] = running
            entering[index] = jnp.exp(log_before)
            running = block_decay[index][:, None, None] * running + states[index]
            log_before = log_before + blk[index]
        total = log_before
        carried = exclusive_carry(total, running, sign)
        intra_t = block_intra(state_c, values_t, acc_g, acc_t, delta_t, forward)
        start = jnp.stack(
            [local_start[index] + entering[index][:, None, None] * carried for index in range(blocks)]
        )
        skip_col = jnp.repeat(skip_gain, P_SIZE)[:, None]
        outputs = block_finish(intra_t, state_c, values_t, acc_t, start, skip_col).T
        gated = outputs.reshape(rows, heads * P_SIZE) * jax.nn.silu(gate_in.astype(F32))
        grouped = gated.reshape(rows, groups, per_group * P_SIZE)
        scale = lax.rsqrt(jnp.mean(grouped * grouped, axis=-1, keepdims=True) + EPSILON)
        return ((grouped * scale).reshape(rows, heads * P_SIZE) * norm_gain[None, :]).astype(BF16)

    forward_out = local_scan(project(hidden), True)
    backward_out = local_scan(project(hidden_rev), False)
    combined = (forward_out.astype(F32) + backward_out.astype(F32)).astype(BF16)
    chan = lax.axis_size("chan")
    partial = jnp.dot(combined, w_out, preferred_element_type=F32).astype(BF16)
    partial = jnp.transpose(partial.reshape(rows, chan, width // chan), (1, 0, 2))
    summed = lax.psum_scatter(partial, "chan", scatter_dimension=0, tiled=True)
    return summed.reshape(rows, width // chan)


def solution(mesh):
    return jax.shard_map(
        on_device,
        mesh=mesh,
        in_specs=(
            P(("groups", "seq"), None),
            P(("groups", "seq")),
            P(None, "chan"),
            P(None, "chan"),
            P(None, "chan"),
            P(None, "chan"),
            P(None, "chan"),
            P("chan"),
            P(None, "chan"),
            P("chan"),
            P("chan"),
            P("chan"),
            P("chan"),
            P("chan"),
            P("chan", None),
        ),
        out_specs=P(("groups", "seq"), "chan"),
        check_vma=False,
    )
```

```python
import jax
import jax.numpy as jnp
from jax import lax
from jax.sharding import PartitionSpec as P
from jax.experimental import pallas as pl

P_SIZE = 64
N = 128
K = 4
Q = 128
LANE = 128


EPSILON = 1e-05
HIGHEST = lax.Precision.HIGHEST
F32 = jnp.float32
BF16 = jnp.bfloat16


def shifted(value, axis, steps):
    count = lax.axis_size(axis)
    pairs = [(source, source + steps) for source in range(count) if 0 <= source + steps < count]
    if not pairs:
        return jax.tree.map(jnp.zeros_like, value)
    return lax.ppermute(value, axis, pairs)


def exclusive_carry(total_log, state, sign):
    count = lax.axis_size("seq")
    heads = state.shape[0]
    flat = state.reshape(heads, -1)
    size = flat.shape[1]

    def send(log, st, distance):
        log_hi = log.astype(BF16)
        log_lo = (log - log_hi.astype(F32)).astype(BF16)
        packed = jnp.concatenate(
            [
                st.astype(BF16),
                jnp.broadcast_to(log_hi[:, None], (heads, LANE)),
                jnp.broadcast_to(log_lo[:, None], (heads, LANE)),
            ],
            axis=1,
        )
        got = shifted(packed, "seq", sign * distance)
        got_log = got[:, size].astype(F32) + got[:, size + LANE].astype(F32)
        return got_log, got[:, :size].astype(F32)

    got_log, got_state = send(total_log, flat, 1)
    x_log, x_state = got_log, got_state
    i_log = got_log + total_log
    i_state = jnp.exp(total_log)[:, None] * got_state + flat
    covered, window = 1, 2
    while covered < count - 1:
        r_log, r_state = send(i_log, i_state, window)
        x_state = jnp.exp(x_log)[:, None] * r_state + x_state
        x_log = x_log + r_log
        covered += window
        if covered < count - 1:
            i_state = jnp.exp(i_log)[:, None] * r_state + i_state
            i_log = i_log + r_log
            window *= 2
    return x_state.reshape(state.shape)


def group_layout(acc, delta, groups, per_group):
    rows = acc.shape[0]
    acc_g = jnp.transpose(acc.reshape(rows, groups, per_group), (1, 0, 2))
    delta_g = jnp.transpose(delta.reshape(rows, groups, per_group), (1, 0, 2))
    return acc_g, delta_g, jnp.transpose(acc_g, (0, 2, 1)), jnp.transpose(delta_g, (0, 2, 1))


def block_states(state_c, values_t, acc_t, delta_t, forward, interpret=False):
    rows = values_t.shape[1]
    groups, per_group, _ = acc_t.shape
    blocks = rows // Q
    width_g = per_group * P_SIZE

    def kernel(b_ref, xt_ref, at_ref, dt_ref, s_ref):
      for blk in range(blocks):
        cols = slice(blk * Q, (blk + 1) * Q)
        b_blk = b_ref[cols, :]
        for j in range(per_group):
            a_row = at_ref[0, j : j + 1, cols]
            d_row = dt_ref[0, j : j + 1, cols]
            a_end = a_row[:, Q - 1 : Q] if forward else a_row[:, 0:1]
            xt_j = xt_ref[j * P_SIZE : (j + 1) * P_SIZE, cols]
            tx = (jnp.exp(a_end - a_row) * d_row) * xt_j.astype(F32)
            s_ref[blk, j] = jnp.dot(tx.astype(BF16), b_blk, preferred_element_type=F32)

    return pl.pallas_call(
        kernel,
        grid=(groups,),
        in_specs=[
            pl.BlockSpec((rows, N), lambda g: (0, 2 * g)),
            pl.BlockSpec((width_g, rows), lambda g: (g, 0)),
            pl.BlockSpec((1, per_group, rows), lambda g: (g, 0, 0)),
            pl.BlockSpec((1, per_group, rows), lambda g: (g, 0, 0)),
        ],
        out_specs=pl.BlockSpec((blocks, per_group, P_SIZE, N), lambda g: (0, g, 0, 0)),
        out_shape=jax.ShapeDtypeStruct((blocks, groups * per_group, P_SIZE, N), F32),
        interpret=interpret,
    )(state_c, values_t, acc_t, delta_t)


def block_intra(state_c, values_t, acc_g, acc_t, delta_t, forward, interpret=False):
    rows = values_t.shape[1]
    groups, _, per_group = acc_g.shape
    blocks = rows // Q
    width_g = per_group * P_SIZE

    def kernel(c_ref, b_ref, xt_ref, a_ref, at_ref, dt_ref, y_ref):
        row = lax.broadcasted_iota(jnp.int32, (Q, Q), 0)
        col = lax.broadcasted_iota(jnp.int32, (Q, Q), 1)
        mask = row >= col if forward else row <= col
        for blk in range(blocks):
            cols = slice(blk * Q, (blk + 1) * Q)
            inner = lax.dot_general(
                c_ref[cols, :], b_ref[cols, :], (((1,), (1,)), ((), ())), preferred_element_type=F32
            )
            for j in range(per_group):
                a_col = a_ref[0, cols, j : j + 1]
                a_row = at_ref[0, j : j + 1, cols]
                d_row = dt_ref[0, j : j + 1, cols]
                differ = jnp.where(mask, a_col - a_row, 0.0)
                m = jnp.where(mask, jnp.exp(differ), 0.0) * d_row * inner
                xt_j = xt_ref[j * P_SIZE : (j + 1) * P_SIZE, cols]
                y_ref[j * P_SIZE : (j + 1) * P_SIZE, cols] = lax.dot_general(
                    xt_j, m.astype(BF16), (((1,), (1,)), ((), ())), preferred_element_type=F32
                )

    return pl.pallas_call(
        kernel,
        grid=(groups,),
        in_specs=[
            pl.BlockSpec((rows, N), lambda g: (0, 2 * g + 1)),
            pl.BlockSpec((rows, N), lambda g: (0, 2 * g)),
            pl.BlockSpec((width_g, rows), lambda g: (g, 0)),
            pl.BlockSpec((1, rows, per_group), lambda g: (g, 0, 0)),
            pl.BlockSpec((1, per_group, rows), lambda g: (g, 0, 0)),
            pl.BlockSpec((1, per_group, rows), lambda g: (g, 0, 0)),
        ],
        out_specs=pl.BlockSpec((width_g, rows), lambda g: (g, 0)),
        out_shape=jax.ShapeDtypeStruct((groups * width_g, rows), F32),
        interpret=interpret,
    )(state_c, state_c, values_t, acc_g, acc_t, delta_t)


def block_finish(intra_t, state_c, values_t, acc_t, start, skip_col, interpret=False):
    rows = values_t.shape[1]
    groups, per_group, _ = acc_t.shape
    blocks = rows // Q
    width_g = per_group * P_SIZE

    def kernel(y_ref, c_ref, xt_ref, at_ref, s_ref, k_ref, o_ref):
        dims = (((1,), (1,)), ((), ()))
        for b in range(blocks):
            cols = slice(b * Q, (b + 1) * Q)
            c_blk = c_ref[cols, :]
            for j in range(per_group):
                lo_row, hi_row = j * P_SIZE, (j + 1) * P_SIZE
                inter = lax.dot_general(
                    s_ref[b, j].astype(BF16), c_blk, dims, preferred_element_type=F32
                )
                inter = inter * jnp.exp(at_ref[0, j : j + 1, cols])
                o_ref[lo_row:hi_row, cols] = (
                    y_ref[lo_row:hi_row, cols]
                    + inter
                    + k_ref[lo_row:hi_row, :] * xt_ref[lo_row:hi_row, cols].astype(F32)
                )

    return pl.pallas_call(
        kernel,
        grid=(groups,),
        in_specs=[
            pl.BlockSpec((width_g, rows), lambda g: (g, 0)),
            pl.BlockSpec((rows, N), lambda g: (0, 2 * g + 1)),
            pl.BlockSpec((width_g, rows), lambda g: (g, 0)),
            pl.BlockSpec((1, per_group, rows), lambda g: (g, 0, 0)),
            pl.BlockSpec((blocks, per_group, P_SIZE, N), lambda g: (0, g, 0, 0)),
            pl.BlockSpec((width_g, 1), lambda g: (g, 0)),
        ],
        out_specs=pl.BlockSpec((width_g, rows), lambda g: (g, 0)),
        out_shape=jax.ShapeDtypeStruct((groups * width_g, rows), F32),
        interpret=interpret,
    )(intra_t, state_c, values_t, acc_t, start, skip_col)


def conv_silu(padded, kernel, offset, count, forward):
    taps = kernel.shape[0]
    total = jnp.zeros((count, padded.shape[1]), F32) + offset[None, :]
    for index in range(taps):
        start = index if forward else taps - 1 - index
        total = total + kernel[index][None, :] * padded[start : start + count].astype(F32)
    return jax.nn.silu(total).astype(BF16)


def on_device(
    hidden,
    bases,
    w_gate,
    w_values,
    w_state_io,
    w_step,
    conv_values,
    conv_values_bias,
    conv_state_io,
    conv_state_bias,
    step_bias,
    decay_rate,
    skip_gain,
    norm_gain,
    w_out,
):
    rows, width = hidden.shape
    heads = w_step.shape[1]
    groups = w_state_io.shape[1] // (2 * N)
    per_group = heads // groups
    blocks = rows // Q
    known = jnp.where(bases == 4, 0.0, 1.0).astype(F32)

    lane_idx = jnp.arange(LANE)
    anti = (lane_idx[:, None] + lane_idx[None, :] == LANE - 1).astype(BF16)

    def lane_reverse(block):
        count = block.shape[0]
        flipped = jnp.einsum(
            "rki,ij->rkj", block.reshape(count, width // LANE, LANE), anti, preferred_element_type=F32
        ).astype(BF16)
        return jnp.flip(flipped, 1).reshape(count, width)

    hidden_rev = lane_reverse(hidden)

    taps = K - 1
    known_cols = jnp.broadcast_to(known.astype(BF16)[:, None], (rows, LANE))
    edge_first = jnp.concatenate([hidden[:taps], known_cols[:taps]], axis=1)
    edge_last = jnp.concatenate([hidden[rows - taps :], known_cols[rows - taps :]], axis=1)
    from_prev = shifted(edge_last, "seq", 1)
    from_next = shifted(edge_first, "seq", -1)
    rim_rows = jnp.concatenate([from_prev[:, :width], lane_reverse(from_next[:, :width])], axis=0)
    rim_known = jnp.concatenate([from_prev[:, width], from_next[:, width]], axis=0).astype(F32)
    rim_values = (
        jnp.dot(rim_rows, w_values, preferred_element_type=F32) * rim_known[:, None]
    ).astype(BF16)
    rim_state = jnp.dot(rim_rows, w_state_io, preferred_element_type=F32).astype(BF16)

    def project(source):
        gate_in = jnp.dot(source, w_gate, preferred_element_type=F32).astype(BF16)
        values = (jnp.dot(source, w_values, preferred_element_type=F32) * known[:, None]).astype(BF16)
        state_io = jnp.dot(source, w_state_io, preferred_element_type=F32).astype(BF16)
        step_raw = jnp.dot(source, w_step, preferred_element_type=F32).astype(BF16)
        return gate_in, values, state_io, step_raw

    t_idx = jnp.arange(Q)

    def local_scan(pieces, forward):
        gate_in, values, state_io, step_raw = pieces
        sign = 1 if forward else -1
        if forward:
            pv = jnp.concatenate([rim_values[:taps], values], axis=0)
            ps = jnp.concatenate([rim_state[:taps], state_io], axis=0)
        else:
            pv = jnp.concatenate([values, rim_values[taps:]], axis=0)
            ps = jnp.concatenate([state_io, rim_state[taps:]], axis=0)
        values_c = conv_silu(pv, conv_values, conv_values_bias, rows, forward)
        state_c = conv_silu(ps, conv_state_io, conv_state_bias, rows, forward)
        delta = jax.nn.softplus(step_raw.astype(F32) + step_bias[None, :])
        logdec = -decay_rate[None, :] * delta

        sb = state_c.reshape(blocks, Q, groups, 2, N)
        c_vec = sb[:, :, :, 1, :]
        ld = logdec.reshape(blocks, Q, heads)
        if forward:
            mask = t_idx[:, None] >= t_idx[None, :]
        else:
            mask = t_idx[:, None] <= t_idx[None, :]
        acc = jnp.einsum("ts,bsh->bth", mask.astype(F32), ld, precision=HIGHEST)
        blk = jnp.sum(ld, axis=1)
        acc_g, delta_g, acc_t, delta_t = group_layout(acc.reshape(rows, heads), delta, groups, per_group)
        values_t = values_c.T
        states = block_states(state_c, values_t, acc_t, delta_t, forward)

        order = list(range(blocks)) if forward else list(range(blocks - 1, -1, -1))
        block_decay = jnp.exp(blk)
        running = jnp.zeros((heads, P_SIZE, N), F32)
        local_start = [None] * blocks
        entering = [None] * blocks
        log_before = jnp.zeros((heads,), F32)
        for index in order:
            local_start[index] = running
            entering[index] = jnp.exp(log_before)
            running = block_decay[index][:, None, None] * running + states[index]
            log_before = log_before + blk[index]
        total = log_before
        carried = exclusive_carry(total, running, sign)
        intra_t = block_intra(state_c, values_t, acc_g, acc_t, delta_t, forward)
        start = jnp.stack(
            [local_start[index] + entering[index][:, None, None] * carried for index in range(blocks)]
        )
        skip_col = jnp.repeat(skip_gain, P_SIZE)[:, None]
        outputs = block_finish(intra_t, state_c, values_t, acc_t, start, skip_col).T
        gated = outputs.reshape(rows, heads * P_SIZE) * jax.nn.silu(gate_in.astype(F32))
        grouped = gated.reshape(rows, groups, per_group * P_SIZE)
        scale = lax.rsqrt(jnp.mean(grouped * grouped, axis=-1, keepdims=True) + EPSILON)
        return ((grouped * scale).reshape(rows, heads * P_SIZE) * norm_gain[None, :]).astype(BF16)

    forward_out = local_scan(project(hidden), True)
    backward_out = local_scan(project(hidden_rev), False)
    combined = (forward_out.astype(F32) + backward_out.astype(F32)).astype(BF16)
    chan = lax.axis_size("chan")
    partial = jnp.dot(combined, w_out, preferred_element_type=F32).astype(BF16)
    partial = jnp.transpose(partial.reshape(rows, chan, width // chan), (1, 0, 2))
    summed = lax.psum_scatter(partial, "chan", scatter_dimension=0, tiled=True)
    return summed.reshape(rows, width // chan)


def solution(mesh):
    return jax.shard_map(
        on_device,
        mesh=mesh,
        in_specs=(
            P(("groups", "seq"), None),
            P(("groups", "seq")),
            P(None, "chan"),
            P(None, "chan"),
            P(None, "chan"),
            P(None, "chan"),
            P(None, "chan"),
            P("chan"),
            P(None, "chan"),
            P("chan"),
            P("chan"),
            P("chan"),
            P("chan"),
            P("chan"),
            P("chan", None),
        ),
        out_specs=P(("groups", "seq"), "chan"),
        check_vma=False,
    )
```
